256 devices in a mesh: seq: 64 (over z, x, core), tp: 4 (over y).
Axes of the slice: x: 4, y: 4, z: 8, core: 2. Of those that a mesh axis runs over, the one named last changes fastest.
Arguments:
- queries: bfloat16 [320, 1536], P(None, 'tp'), may hold values from -6 to 6
- new_keys: bfloat16 [320, 512], P('seq', 'tp'), may hold values from -12 to 12
- new_values: bfloat16 [320, 512], P('seq', 'tp'), may hold values from -6 to 6
- key_cache: bfloat16 [524288, 512], P('seq', 'tp'), may hold values from -64 to 64
- value_cache: bfloat16 [524288, 512], P('seq', 'tp'), may hold values from -6 to 6
- out_weight: bfloat16 [1536, 1536], P('tp'), may hold values from -0.75 to 0.75
- group_ids: int32 [64], replicated, may hold values from 0 to 5, as said below
- prefix_len: int32 [6], replicated, may hold values from 2560 to 10240, as said below
- suffix_len: int32 [64], replicated, may hold values from 1536 to 6144, as said below
Outputs:
- attended: bfloat16 [320, 1536], P('seq', 'tp')
The draws below stay inside these ranges and needn't reach their ends.
Inputs may be any that keep to these rules, and one draw needn't show every extreme that they name: `group_ids`: non-decreasing; every prompt is used by 8 to 16 requests. `prefix_len`: some prompt has exactly 10240 positions. `suffix_len`: some request has exactly 6144 own positions.
All inputs are finite; a program needn't handle non-finite values.
Results may differ from the reference program's by a relative error of at most 0.011.
Values sent between devices are 32-bit elements; how exact they have to be, the bound alone decides.
No kernel may reach another device: no remote copies, remote signals or barrier semaphores. Data moves between devices by JAX's collectives and lax.ppermute only.
A program may use at most 64 MiB of HBM per device.

```python
import jax
import jax.numpy as jnp
from jax import lax

H = 24
KVH = 8
HD = 64
D = 1536
NEW = 5
REQ = 64
GROUPS = 6
GMIN = 8
ROWS = 320
CACHE = 524288
PRE_MAX = 10240
SUF_MAX = 6144


def layout(key):
    inner = jax.random.fold_in(key, 101)
    key_a, key_b, key_c, key_d, key_e = jax.random.split(inner, 5)
    groups = jnp.arange(GROUPS, dtype=jnp.int32)
    slots = jax.random.permutation(key_a, GROUPS * GMIN).astype(jnp.int32)
    chosen = (slots[:REQ - GMIN * GROUPS] // GMIN).astype(jnp.int32)
    sizes = (GMIN + jnp.sum((chosen[:, None] == groups[None, :]).astype(jnp.int32), axis=0)).astype(jnp.int32)
    ends = jnp.cumsum(sizes).astype(jnp.int32)
    index = jnp.arange(REQ, dtype=jnp.int32)
    group_ids = jnp.sum((index[:, None] >= ends[None, :]).astype(jnp.int32), axis=1).astype(jnp.int32)
    prefix = jax.random.randint(key_b, (GROUPS,), PRE_MAX // 4, PRE_MAX + 1, dtype=jnp.int32)
    widest = jax.random.randint(key_c, (), 0, GROUPS, dtype=jnp.int32)
    prefix = jnp.where(groups == widest, PRE_MAX, prefix).astype(jnp.int32)
    suffix = jax.random.randint(key_d, (REQ,), SUF_MAX // 4, SUF_MAX + 1, dtype=jnp.int32)
    longest = jax.random.randint(key_e, (), 0, REQ, dtype=jnp.int32)
    suffix = jnp.where(index == longest, SUF_MAX, suffix).astype(jnp.int32)
    return (group_ids, prefix, suffix)


def draw_group_ids(key, part):
    return layout(key)[0]


def draw_prefix_len(key, part):
    return layout(key)[1]


def draw_suffix_len(key, part):
    return layout(key)[2]


def float_base(key, salt, shape):
    inner = jax.random.fold_in(key, salt)
    values = jnp.clip(jax.random.normal(inner, shape, jnp.float32), -6.0, 6.0)
    return values


def draw_queries(key, part):
    return float_base(key, 202, (ROWS, H * HD)).astype(jnp.bfloat16)


def draw_new_keys(key, part):
    query = float_base(key, 202, (ROWS, H * HD)).reshape(ROWS, KVH, H // KVH, HD)
    noise = float_base(key, 303, (ROWS, KVH, HD))
    keys = 0.5 * jnp.sum(query, axis=2) + 0.5 * noise
    return keys.reshape(ROWS, KVH * HD).astype(jnp.bfloat16)


def draw_key_cache(key, part):
    cache = float_base(key, 404, (CACHE, KVH * HD))
    return cache.astype(jnp.bfloat16)


def block_levels(stream_key, dims, cuts, low, high):
    gain = 1.0
    for axis_at, parts in cuts:
        steps = jax.random.uniform(jax.random.fold_in(jax.random.fold_in(stream_key, 6), axis_at), (parts,), jnp.float32, low / len(cuts), high / len(cuts))
        gain = gain * jnp.repeat(jnp.exp(steps), dims[axis_at] // parts).reshape((-1,) + (1,) * (len(dims) - 1 - axis_at))
    return gain


def centred(key, extent, deviation, limit, pieces=(), held_as=jnp.bfloat16):
    gain = block_levels(key, extent, pieces, -0.22, 0.18) if pieces else 1.0
    entries = jax.random.normal(key, extent, jnp.float32) * deviation * gain
    return jnp.minimum(jnp.maximum(entries, -limit), limit).astype(held_as)


def setup_inputs(seed: int = 0) -> dict:
    arg_keys = jax.random.split(jax.random.key(seed), 10)
    return {
        "queries": draw_queries(jax.random.fold_in(arg_keys[9], 71), 0),
        "new_keys": draw_new_keys(jax.random.fold_in(arg_keys[9], 71), 0),
        "new_values": centred(arg_keys[2], (ROWS, KVH * HD), 1.0, 6.0, ((0, 64), (1, 4))),
        "key_cache": draw_key_cache(jax.random.fold_in(arg_keys[9], 71), 0),
        "value_cache": centred(arg_keys[4], (CACHE, KVH * HD), 1.0, 6.0, ((0, 64), (1, 4))),
        "out_weight": centred(arg_keys[5], (H * HD, D), HD ** -0.5, 0.75, ((0, 4),)),
        "group_ids": draw_group_ids(jax.random.fold_in(arg_keys[9], 71), 0),
        "prefix_len": draw_prefix_len(jax.random.fold_in(arg_keys[9], 71), 0),
        "suffix_len": draw_suffix_len(jax.random.fold_in(arg_keys[9], 71), 0),
    }


fill_score = -1e30


def segment_starts(group_ids, prefix_len, suffix_len):
    groups = jnp.arange(prefix_len.shape[0], dtype=jnp.int32)
    prefix_excl = (jnp.cumsum(prefix_len) - prefix_len).astype(jnp.int32)
    suffix_excl = (jnp.cumsum(suffix_len) - suffix_len).astype(jnp.int32)
    earlier = group_ids[None, :] < groups[:, None]
    prompt_start = prefix_excl + jnp.sum(jnp.where(earlier, suffix_len[None, :], 0), axis=1).astype(jnp.int32)
    member = group_ids[:, None] == groups[None, :]
    req_prompt_start = jnp.sum(jnp.where(member, prompt_start[None, :], 0), axis=1).astype(jnp.int32)
    req_prompt_len = jnp.sum(jnp.where(member, prefix_len[None, :], 0), axis=1).astype(jnp.int32)
    prefix_incl = jnp.sum(jnp.where(member, (prefix_excl + prefix_len)[None, :], 0), axis=1).astype(jnp.int32)
    own_start = (prefix_incl + suffix_excl).astype(jnp.int32)
    return req_prompt_start, req_prompt_len, own_start


def reference(queries, new_keys, new_values, key_cache, value_cache, out_weight, group_ids, prefix_len, suffix_len):
    prompt_start, prompt_len, own_start = segment_starts(group_ids, prefix_len, suffix_len)
    rep = H // KVH
    query_all = queries.reshape(REQ, NEW, KVH, rep, HD)
    keys_new = new_keys.reshape(REQ, NEW, KVH, HD)
    values_new = new_values.reshape(REQ, NEW, KVH, HD)
    causal = jnp.arange(NEW)[:, None] >= jnp.arange(NEW)[None, :]

    def one_request(index):
        pstart = jnp.minimum(prompt_start[index], CACHE - PRE_MAX).astype(jnp.int32)
        sstart = jnp.minimum(own_start[index], CACHE - SUF_MAX).astype(jnp.int32)
        keys_p = lax.dynamic_slice_in_dim(key_cache, pstart, PRE_MAX, 0)
        vals_p = lax.dynamic_slice_in_dim(value_cache, pstart, PRE_MAX, 0)
        keys_s = lax.dynamic_slice_in_dim(key_cache, sstart, SUF_MAX, 0)
        vals_s = lax.dynamic_slice_in_dim(value_cache, sstart, SUF_MAX, 0)
        pos_p = pstart + jnp.arange(PRE_MAX, dtype=jnp.int32)
        pos_s = sstart + jnp.arange(SUF_MAX, dtype=jnp.int32)
        live_p = (pos_p >= prompt_start[index]) & (pos_p < prompt_start[index] + prompt_len[index])
        live_s = (pos_s >= own_start[index]) & (pos_s < own_start[index] + suffix_len[index])
        cached = jnp.concatenate([live_p, live_s])
        live = jnp.concatenate([jnp.broadcast_to(cached[None, :], (NEW, cached.shape[0])), causal], axis=1)
        keys = jnp.concatenate([keys_p.reshape(PRE_MAX, KVH, HD), keys_s.reshape(SUF_MAX, KVH, HD), keys_new[index]], axis=0)
        vals = jnp.concatenate([vals_p.reshape(PRE_MAX, KVH, HD), vals_s.reshape(SUF_MAX, KVH, HD), values_new[index]], axis=0)
        score = jnp.einsum("tgjd,lgd->tgjl", query_all[index].astype(jnp.float32), keys.astype(jnp.float32)) * 0.125
        mask = live[:, None, None, :]
        score = jnp.where(mask, score, fill_score)
        top = jnp.max(score, axis=-1, keepdims=True)
        expo = jnp.where(mask, jnp.exp(score - top), 0.0)
        total = jnp.sum(expo, axis=-1)
        weight = lax.optimization_barrier(expo.astype(jnp.bfloat16)).astype(jnp.float32)
        summed = jnp.einsum("tgjl,lgd->tgjd", weight, vals.astype(jnp.float32))
        return (summed / total[..., None]).astype(jnp.bfloat16).reshape(NEW, H * HD)

    mixed = lax.map(one_request, jnp.arange(REQ, dtype=jnp.int32)).reshape(ROWS, H * HD)
    return jnp.dot(mixed, out_weight, preferred_element_type=jnp.float32).astype(jnp.bfloat16)
```

```python
import jax
import jax.numpy as jnp
from jax import lax
from jax.sharding import PartitionSpec as P

HD = 64
NEW = 5


fill_score = -1e30


def segment_starts(group_ids, prefix_len, suffix_len):
    groups = jnp.arange(prefix_len.shape[0], dtype=jnp.int32)
    prefix_excl = jnp.cumsum(prefix_len) - prefix_len
    suffix_excl = jnp.cumsum(suffix_len) - suffix_len
    earlier = group_ids[None, :] < groups[:, None]
    prompt_start = prefix_excl + jnp.sum(jnp.where(earlier, suffix_len[None, :], 0), axis=1)
    member = group_ids[:, None] == groups[None, :]
    req_prompt_start = jnp.sum(jnp.where(member, prompt_start[None, :], 0), axis=1)
    req_prompt_len = jnp.sum(jnp.where(member, prefix_len[None, :], 0), axis=1)
    prefix_incl = jnp.sum(jnp.where(member, (prefix_excl + prefix_len)[None, :], 0), axis=1)
    own_start = prefix_incl + suffix_excl
    group_suffix = jnp.sum(jnp.where(member, suffix_len[:, None], 0), axis=0)
    group_end = prompt_start + prefix_len + group_suffix
    req_group_end = jnp.sum(jnp.where(member, group_end[None, :], 0), axis=1)
    return (req_prompt_start, req_prompt_len, own_start, req_group_end)


def per_device(
    queries,
    new_keys,
    new_values,
    key_cache,
    value_cache,
    out_weight,
    group_ids,
    prefix_len,
    suffix_len,
):
    rows = queries.shape[0]
    heads_local = queries.shape[1] // HD
    kv_local = key_cache.shape[1] // HD
    repeat = heads_local // kv_local
    requests = rows // NEW
    window = min(requests, 32)
    block = key_cache.shape[0]
    step_len = 1024
    prompt_start, prompt_len, own_start, group_end = segment_starts(
        group_ids, prefix_len, suffix_len
    )
    offset = lax.axis_index("seq") * block
    query_all = queries.reshape(requests, NEW, kv_local, repeat, HD)
    first_req = jnp.sum((group_end <= offset).astype(jnp.int32))
    low = jnp.minimum(first_req, requests - window)
    query_win = lax.dynamic_slice_in_dim(query_all, low, window, 0)
    pstart_win = lax.dynamic_slice_in_dim(prompt_start, low, window, 0)
    pend_win = pstart_win + lax.dynamic_slice_in_dim(prompt_len, low, window, 0)
    ostart_win = lax.dynamic_slice_in_dim(own_start, low, window, 0)
    oend_win = ostart_win + lax.dynamic_slice_in_dim(suffix_len, low, window, 0)

    def key_step(turn, carry):
        row_max, total, summed = carry
        start = turn * step_len
        keys = lax.dynamic_slice_in_dim(key_cache, start, step_len, 0).reshape(
            step_len, kv_local, HD
        )
        vals = lax.dynamic_slice_in_dim(value_cache, start, step_len, 0).reshape(
            step_len, kv_local, HD
        )
        places = offset + start + jnp.arange(step_len, dtype=jnp.int32)
        in_prompt = (places[None, :] >= pstart_win[:, None]) & (places[None, :] < pend_win[:, None])
        in_own = (places[None, :] >= ostart_win[:, None]) & (places[None, :] < oend_win[:, None])
        mask = (in_prompt | in_own)[:, None, None, None, :]
        score = (
            jnp.einsum("rtgjd,kgd->rtgjk", query_win, keys, preferred_element_type=jnp.float32)
            * 0.125
        )
        block_max = jnp.max(jnp.where(mask, score, fill_score), axis=-1)
        new_max = jnp.maximum(row_max, block_max)
        expo = jnp.where(mask, jnp.exp(score - new_max[..., None]), 0.0)
        factor = jnp.exp(row_max - new_max)
        total = total * factor + jnp.sum(expo, axis=-1)
        summed = summed * factor[..., None] + jnp.einsum(
            "rtgjk,kgd->rtgjd", expo.astype(jnp.bfloat16), vals, preferred_element_type=jnp.float32
        )
        return (new_max, total, summed)

    shape_win = (window, NEW, kv_local, repeat)
    start_state = (
        jnp.full(shape_win, fill_score, jnp.float32),
        jnp.zeros(shape_win, jnp.float32),
        jnp.zeros(shape_win + (HD,), jnp.float32),
    )
    win_max, win_total, win_summed = lax.fori_loop(0, block // step_len, key_step, start_state)
    shape_stat = (requests, NEW, kv_local, repeat)
    row_max = lax.dynamic_update_slice_in_dim(
        jnp.full(shape_stat, fill_score, jnp.float32), win_max, low, 0
    )
    total = lax.dynamic_update_slice_in_dim(jnp.zeros(shape_stat, jnp.float32), win_total, low, 0)
    summed = lax.dynamic_update_slice_in_dim(
        jnp.zeros(shape_stat + (HD,), jnp.float32), win_summed, low, 0
    )
    mine = lax.axis_index("seq")
    packed = jnp.concatenate([summed, row_max[..., None], total[..., None]], axis=-1)
    packed = lax.all_to_all(packed, "seq", split_axis=0, concat_axis=0, tiled=True)
    sums = packed[..., :HD]
    maxes = packed[..., HD]
    totals = packed[..., HD + 1]
    own_max = jnp.max(maxes, axis=0)
    rescale = jnp.exp(maxes - own_max[None])
    own_total = jnp.sum(totals * rescale, axis=0)
    own_summed = jnp.sum(sums * rescale[..., None], axis=0)
    own_query = lax.dynamic_slice_in_dim(query_all, mine, 1, 0)[0]
    keys_new = new_keys.reshape(NEW, kv_local, HD)
    values_new = new_values.reshape(NEW, kv_local, HD)
    causal = (jnp.arange(NEW)[:, None] >= jnp.arange(NEW)[None, :])[:, None, None, :]
    score_new = (
        jnp.einsum("tgjd,ugd->tgju", own_query, keys_new, preferred_element_type=jnp.float32)
        * 0.125
    )
    joined = jnp.maximum(own_max, jnp.max(jnp.where(causal, score_new, fill_score), axis=-1))
    expo_new = jnp.where(causal, jnp.exp(score_new - joined[..., None]), 0.0)
    factor_own = jnp.exp(own_max - joined)
    denominator = own_total * factor_own + jnp.sum(expo_new, axis=-1)
    numerator = own_summed * factor_own[..., None] + jnp.einsum(
        "tgju,ugd->tgjd",
        expo_new.astype(jnp.bfloat16),
        values_new,
        preferred_element_type=jnp.float32,
    )
    mixed = (numerator / denominator[..., None]).astype(jnp.bfloat16).reshape(NEW, heads_local * HD)
    partial_out = jnp.dot(mixed, out_weight, preferred_element_type=jnp.float32)
    parts = lax.axis_size("tp")
    width = partial_out.shape[1] // parts
    pieces = partial_out.reshape(NEW, parts, width)
    me = lax.axis_index("tp")
    result = lax.dynamic_index_in_dim(pieces, me, 1, keepdims=False)
    for shift in range(1, parts):
        sent = lax.dynamic_index_in_dim(pieces, (me + shift) % parts, 1, keepdims=False)
        pairs = [(i, (i + shift) % parts) for i in range(parts)]
        result = result + lax.ppermute(sent, "tp", pairs)
    return result.astype(jnp.bfloat16)


def solution(mesh):
    placed = (
        P(None, "tp"),
        P("seq", "tp"),
        P("seq", "tp"),
        P("seq", "tp"),
        P("seq", "tp"),
        P("tp", None),
        P(),
        P(),
        P(),
    )
    return jax.shard_map(
        per_device, mesh=mesh, in_specs=placed, out_specs=P("seq", "tp"), check_vma=False
    )
```

```python
import jax
import jax.numpy as jnp
from jax import lax
from jax.sharding import PartitionSpec as P

HD = 64
NEW = 5
STEP = 1024
SPAN = 17


fill_score = -1e30


def segment_starts(group_ids, prefix_len, suffix_len):
    groups = jnp.arange(prefix_len.shape[0], dtype=jnp.int32)
    prefix_excl = jnp.cumsum(prefix_len) - prefix_len
    suffix_excl = jnp.cumsum(suffix_len) - suffix_len
    earlier = group_ids[None, :] < groups[:, None]
    prompt_start = prefix_excl + jnp.sum(jnp.where(earlier, suffix_len[None, :], 0), axis=1)
    member = group_ids[:, None] == groups[None, :]
    req_prompt_start = jnp.sum(jnp.where(member, prompt_start[None, :], 0), axis=1)
    req_prompt_len = jnp.sum(jnp.where(member, prefix_len[None, :], 0), axis=1)
    prefix_incl = jnp.sum(jnp.where(member, (prefix_excl + prefix_len)[None, :], 0), axis=1)
    own_start = prefix_incl + suffix_excl
    return (req_prompt_start, req_prompt_len, own_start)


def per_device(
    queries,
    new_keys,
    new_values,
    key_cache,
    value_cache,
    out_weight,
    group_ids,
    prefix_len,
    suffix_len,
):
    rows = queries.shape[0]
    heads_local = queries.shape[1] // HD
    kv_local = key_cache.shape[1] // HD
    repeat = heads_local // kv_local
    requests = rows // NEW
    block = key_cache.shape[0]
    span = min(SPAN, requests)
    tj = NEW * repeat
    prompt_start, prompt_len, own_start = segment_starts(group_ids, prefix_len, suffix_len)
    prompt_end = prompt_start + prompt_len
    own_end = own_start + suffix_len
    offset = lax.axis_index("seq") * block
    query_all = (
        queries.reshape(requests, NEW, kv_local, repeat, HD)
        .transpose(0, 2, 1, 3, 4)
        .reshape(requests, kv_local, tj, HD)
    )
    steps = block // STEP
    chunk_starts = offset + STEP * jnp.arange(steps, dtype=jnp.int32)
    firsts = jnp.sum((own_end[None, :] <= chunk_starts[:, None]).astype(jnp.int32), axis=1)
    firsts = jnp.minimum(firsts, requests - span)

    def key_step(turn, carry):
        row_max, total, summed = carry
        start = turn * STEP
        low = firsts[turn]
        keys = lax.dynamic_slice_in_dim(key_cache, start, STEP, 0).reshape(STEP, kv_local, HD)
        vals = lax.dynamic_slice_in_dim(value_cache, start, STEP, 0).reshape(STEP, kv_local, HD)
        query_win = lax.dynamic_slice_in_dim(query_all, low, span, 0)
        ps = lax.dynamic_slice_in_dim(prompt_start, low, span, 0)
        pe = lax.dynamic_slice_in_dim(prompt_end, low, span, 0)
        os_ = lax.dynamic_slice_in_dim(own_start, low, span, 0)
        oe = lax.dynamic_slice_in_dim(own_end, low, span, 0)
        places = offset + start + jnp.arange(STEP, dtype=jnp.int32)
        in_prompt = (places[None, :] >= ps[:, None]) & (places[None, :] < pe[:, None])
        in_own = (places[None, :] >= os_[:, None]) & (places[None, :] < oe[:, None])
        mask = (in_prompt | in_own)[:, None, None, :]
        old_max = lax.dynamic_slice_in_dim(row_max, low, span, 0)
        old_total = lax.dynamic_slice_in_dim(total, low, span, 0)
        old_summed = lax.dynamic_slice_in_dim(summed, low, span, 0)
        score = (
            jnp.einsum("rgqd,kgd->rgqk", query_win, keys, preferred_element_type=jnp.float32)
            * 0.125
        )
        block_max = jnp.max(jnp.where(mask, score, fill_score), axis=-1)
        new_max = jnp.maximum(old_max, block_max)
        expo = jnp.where(mask, jnp.exp(score - new_max[..., None]), 0.0)
        factor = jnp.exp(old_max - new_max)
        new_total = old_total * factor + jnp.sum(expo, axis=-1)
        new_summed = old_summed * factor[..., None] + jnp.einsum(
            "rgqk,kgd->rgqd", expo.astype(jnp.bfloat16), vals, preferred_element_type=jnp.float32
        )
        row_max = lax.dynamic_update_slice_in_dim(row_max, new_max, low, 0)
        total = lax.dynamic_update_slice_in_dim(total, new_total, low, 0)
        summed = lax.dynamic_update_slice_in_dim(summed, new_summed, low, 0)
        return (row_max, total, summed)

    shape_stat = (requests, kv_local, tj)
    start_state = (
        jnp.full(shape_stat, fill_score, jnp.float32),
        jnp.zeros(shape_stat, jnp.float32),
        jnp.zeros(shape_stat + (HD,), jnp.float32),
    )
    row_max, total, summed = lax.fori_loop(0, steps, key_step, start_state)
    width = kv_local * tj
    packed = jnp.concatenate(
        [
            summed.reshape(requests, width * HD),
            row_max.reshape(requests, width),
            total.reshape(requests, width),
        ],
        axis=1,
    )
    packed = lax.all_to_all(packed, "seq", split_axis=0, concat_axis=0, tiled=True)
    sums = packed[:, : width * HD].reshape(requests, kv_local, tj, HD)
    maxes = packed[:, width * HD : width * (HD + 1)].reshape(requests, kv_local, tj)
    totals = packed[:, width * (HD + 1) :].reshape(requests, kv_local, tj)
    own_max = jnp.max(maxes, axis=0)
    rescale = jnp.exp(maxes - own_max[None])
    own_total = jnp.sum(totals * rescale, axis=0)
    own_summed = jnp.sum(sums * rescale[..., None], axis=0)
    mine = lax.axis_index("seq")
    own_query = lax.dynamic_index_in_dim(query_all, mine, 0, keepdims=False)
    keys_new = new_keys.reshape(NEW, kv_local, HD)
    values_new = new_values.reshape(NEW, kv_local, HD)
    token_of = jnp.arange(tj) // repeat
    causal = (token_of[:, None] >= jnp.arange(NEW)[None, :])[None]
    score_new = (
        jnp.einsum("gqd,ugd->gqu", own_query, keys_new, preferred_element_type=jnp.float32)
        * 0.125
    )
    joined = jnp.maximum(own_max, jnp.max(jnp.where(causal, score_new, fill_score), axis=-1))
    expo_new = jnp.where(causal, jnp.exp(score_new - joined[..., None]), 0.0)
    factor_own = jnp.exp(own_max - joined)
    denominator = own_total * factor_own + jnp.sum(expo_new, axis=-1)
    numerator = own_summed * factor_own[..., None] + jnp.einsum(
        "gqu,ugd->gqd",
        expo_new.astype(jnp.bfloat16),
        values_new,
        preferred_element_type=jnp.float32,
    )
    mixed = (numerator / denominator[..., None]).astype(jnp.bfloat16)
    mixed = mixed.reshape(kv_local, NEW, repeat, HD).transpose(1, 0, 2, 3)
    mixed = mixed.reshape(NEW, heads_local * HD)
    partial_out = jnp.dot(mixed, out_weight, preferred_element_type=jnp.float32)
    parts = lax.axis_size("tp")
    piece = partial_out.shape[1] // parts
    pieces = partial_out.reshape(NEW, parts, piece)
    me = lax.axis_index("tp")
    result = lax.dynamic_index_in_dim(pieces, me, 1, keepdims=False)
    for shift in range(1, parts):
        sent = lax.dynamic_index_in_dim(pieces, (me + shift) % parts, 1, keepdims=False)
        pairs = [(i, (i + shift) % parts) for i in range(parts)]
        result = result + lax.ppermute(sent, "tp", pairs)
    return result.astype(jnp.bfloat16)


def solution(mesh):
    placed = (
        P(None, "tp"),
        P("seq", "tp"),
        P("seq", "tp"),
        P("seq", "tp"),
        P("seq", "tp"),
        P("tp", None),
        P(),
        P(),
        P(),
    )
    return jax.shard_map(
        per_device, mesh=mesh, in_specs=placed, out_specs=P("seq", "tp"), check_vma=False
    )
```

```python
import jax
import jax.numpy as jnp
from jax import lax
from jax.experimental import pallas as pl
from jax.experimental.pallas import tpu as pltpu
from jax.sharding import PartitionSpec as P

HD = 64
NEW = 5
STEP = 1024
SPAN = 17
PAD = 16
LANES = 128


fill_score = -1e30


def segment_starts(group_ids, prefix_len, suffix_len):
    groups = jnp.arange(prefix_len.shape[0], dtype=jnp.int32)
    prefix_excl = jnp.cumsum(prefix_len) - prefix_len
    suffix_excl = jnp.cumsum(suffix_len) - suffix_len
    earlier = group_ids[None, :] < groups[:, None]
    prompt_start = prefix_excl + jnp.sum(jnp.where(earlier, suffix_len[None, :], 0), axis=1)
    member = group_ids[:, None] == groups[None, :]
    req_prompt_start = jnp.sum(jnp.where(member, prompt_start[None, :], 0), axis=1)
    req_prompt_len = jnp.sum(jnp.where(member, prefix_len[None, :], 0), axis=1)
    prefix_incl = jnp.sum(jnp.where(member, (prefix_excl + prefix_len)[None, :], 0), axis=1)
    own_start = prefix_incl + suffix_excl
    return (req_prompt_start, req_prompt_len, own_start)


def attend_kernel(firsts_ref, q_ref, bound_ref, k_ref, v_ref, o_ref, stat_ref):
    turn = pl.program_id(0)
    span = q_ref.shape[1] if q_ref.shape[1] < SPAN else SPAN
    rows = span * PAD

    @pl.when(turn == 0)
    def _():
        o_ref[...] = jnp.zeros(o_ref.shape, jnp.float32)
        lane = lax.broadcasted_iota(jnp.int32, stat_ref.shape, 2)
        stat_ref[...] = jnp.where(lane % 2 == 0, fill_score, 0.0).astype(jnp.float32)

    low = firsts_ref[turn]
    keys = k_ref[...]
    vals = v_ref[...]
    bound = bound_ref[pl.ds(low, span)].reshape(rows, LANES)
    places = turn * STEP + lax.broadcasted_iota(jnp.int32, (1, STEP), 1)
    mask = ((places >= bound[:, 0:1]) & (places < bound[:, 1:2])) | (
        (places >= bound[:, 2:3]) & (places < bound[:, 3:4])
    )
    stat = stat_ref[pl.ds(low, span)].reshape(rows, LANES)
    o_old = o_ref[pl.ds(low, span)].reshape(rows, LANES)
    lane = lax.broadcasted_iota(jnp.int32, (rows, LANES), 1)
    first_half = lane < HD
    o_new = None
    stat_new = jnp.zeros((rows, LANES), jnp.float32)
    for g in range(2):
        query = q_ref[g, pl.ds(low, span)].reshape(rows, LANES)
        score = lax.dot_general(
            query, keys, (((1,), (1,)), ((), ())), preferred_element_type=jnp.float32
        )
        score = jnp.where(mask, score, fill_score)
        m_old = stat[:, 2 * g : 2 * g + 1]
        l_old = stat[:, 2 * g + 1 : 2 * g + 2]
        m_new = jnp.maximum(m_old, jnp.max(score, axis=1, keepdims=True))
        expo = jnp.exp(score - m_new)
        alpha = jnp.exp(m_old - m_new)
        l_new = alpha * l_old + jnp.sum(expo, axis=1, keepdims=True)
        mixed = jnp.dot(expo.astype(jnp.bfloat16), vals, preferred_element_type=jnp.float32)
        if g == 0:
            o_new = jnp.where(first_half, o_old * alpha + mixed, 0.0)
        else:
            o_new = jnp.where(first_half, o_new, o_old * alpha + mixed)
        stat_new = jnp.where(lane == 2 * g, m_new, stat_new)
        stat_new = jnp.where(lane == 2 * g + 1, l_new, stat_new)
    o_ref[pl.ds(low, span)] = o_new.reshape(span, PAD, LANES)
    stat_ref[pl.ds(low, span)] = stat_new.reshape(span, PAD, LANES)


def per_device(
    queries,
    new_keys,
    new_values,
    key_cache,
    value_cache,
    out_weight,
    group_ids,
    prefix_len,
    suffix_len,
):
    rows = queries.shape[0]
    heads_local = queries.shape[1] // HD
    kv_local = key_cache.shape[1] // HD
    repeat = heads_local // kv_local
    requests = rows // NEW
    block = key_cache.shape[0]
    span = min(SPAN, requests)
    tj = NEW * repeat
    prompt_start, prompt_len, own_start = segment_starts(group_ids, prefix_len, suffix_len)
    prompt_end = prompt_start + prompt_len
    own_end = own_start + suffix_len
    offset = lax.axis_index("seq") * block
    steps = block // STEP
    chunk_starts = offset + STEP * jnp.arange(steps, dtype=jnp.int32)
    firsts = jnp.sum((own_end[None, :] <= chunk_starts[:, None]).astype(jnp.int32), axis=1)
    firsts = jnp.minimum(firsts, requests - span).astype(jnp.int32)
    scaled = (queries * jnp.asarray(0.125, queries.dtype)).reshape(requests, NEW, kv_local, repeat, HD)
    scaled = scaled.transpose(2, 0, 1, 3, 4).reshape(kv_local, requests, tj, HD)
    query_pad = jnp.stack(
        [
            jnp.pad(scaled[g], ((0, 0), (0, PAD - tj), (g * HD, LANES - (g + 1) * HD)))
            for g in range(kv_local)
        ]
    )
    edges = jnp.stack([prompt_start, prompt_end, own_start, own_end], axis=1) - offset
    bound = jnp.pad(edges, ((0, 0), (0, LANES - 4)))
    bound = jnp.broadcast_to(bound[:, None, :], (requests, PAD, LANES))
    full = lambda shape: pl.BlockSpec(shape, lambda t, f: (0,) * len(shape))
    o_out, stat_out = pl.pallas_call(
        attend_kernel,
        grid_spec=pltpu.PrefetchScalarGridSpec(
            num_scalar_prefetch=1,
            grid=(steps,),
            in_specs=[
                full((kv_local, requests, PAD, LANES)),
                full((requests, PAD, LANES)),
                pl.BlockSpec((STEP, LANES), lambda t, f: (t, 0)),
                pl.BlockSpec((STEP, LANES), lambda t, f: (t, 0)),
            ],
            out_specs=[full((requests, PAD, LANES)), full((requests, PAD, LANES))],
        ),
        out_shape=[
            jax.ShapeDtypeStruct((requests, PAD, LANES), jnp.float32),
            jax.ShapeDtypeStruct((requests, PAD, LANES), jnp.float32),
        ],
        compiler_params=pltpu.CompilerParams(dimension_semantics=("arbitrary",)),
    )(firsts, query_pad, bound, key_cache, value_cache)
    width = tj * LANES
    packed = jnp.concatenate(
        [
            o_out[:, :tj, :].reshape(requests, width),
            stat_out[:, :tj, : 2 * kv_local].reshape(requests, tj * 2 * kv_local),
        ],
        axis=1,
    )
    packed = lax.all_to_all(packed, "seq", split_axis=0, concat_axis=0, tiled=True)
    sums = packed[:, :width].reshape(requests, tj, kv_local, HD)
    stats = packed[:, width:].reshape(requests, tj, kv_local, 2)
    maxes = stats[..., 0]
    totals = stats[..., 1]
    own_max = jnp.max(maxes, axis=0)
    rescale = jnp.exp(maxes - own_max[None])
    own_total = jnp.sum(totals * rescale, axis=0)
    own_summed = jnp.sum(sums * rescale[..., None], axis=0)
    mine = lax.axis_index("seq")
    own_query = lax.dynamic_slice_in_dim(queries, mine * NEW, NEW, 0)
    own_query = own_query.reshape(NEW, kv_local, repeat, HD).transpose(0, 2, 1, 3)
    own_query = own_query.reshape(tj, kv_local, HD)
    keys_new = new_keys.reshape(NEW, kv_local, HD)
    values_new = new_values.reshape(NEW, kv_local, HD)
    token_of = jnp.arange(tj) // repeat
    causal = (token_of[:, None] >= jnp.arange(NEW)[None, :])[:, None, :]
    score_new = (
        jnp.einsum("qgd,ugd->qgu", own_query, keys_new, preferred_element_type=jnp.float32)
        * 0.125
    )
    joined = jnp.maximum(own_max, jnp.max(jnp.where(causal, score_new, fill_score), axis=-1))
    expo_new = jnp.where(causal, jnp.exp(score_new - joined[..., None]), 0.0)
    factor_own = jnp.exp(own_max - joined)
    denominator = own_total * factor_own + jnp.sum(expo_new, axis=-1)
    numerator = own_summed * factor_own[..., None] + jnp.einsum(
        "qgu,ugd->qgd",
        expo_new.astype(jnp.bfloat16),
        values_new,
        preferred_element_type=jnp.float32,
    )
    mixed = (numerator / denominator[..., None]).astype(jnp.bfloat16)
    mixed = mixed.reshape(NEW, repeat, kv_local, HD).transpose(0, 2, 1, 3)
    mixed = mixed.reshape(NEW, heads_local * HD)
    partial_out = jnp.dot(mixed, out_weight, preferred_element_type=jnp.float32)
    parts = lax.axis_size("tp")
    piece = partial_out.shape[1] // parts
    pieces = partial_out.reshape(NEW, parts, piece)
    me = lax.axis_index("tp")
    result = lax.dynamic_index_in_dim(pieces, me, 1, keepdims=False)
    for shift in range(1, parts):
        sent = lax.dynamic_index_in_dim(pieces, (me + shift) % parts, 1, keepdims=False)
        pairs = [(i, (i + shift) % parts) for i in range(parts)]
        result = result + lax.ppermute(sent, "tp", pairs)
    return result.astype(jnp.bfloat16)


def solution(mesh):
    placed = (
        P(None, "tp"),
        P("seq", "tp"),
        P("seq", "tp"),
        P("seq", "tp"),
        P("seq", "tp"),
        P("tp", None),
        P(),
        P(),
        P(),
    )
    return jax.shard_map(
        per_device, mesh=mesh, in_specs=placed, out_specs=P("seq", "tp"), check_vma=False
    )
```

```python
import jax
import jax.numpy as jnp
from jax import lax
from jax.experimental import pallas as pl
from jax.experimental.pallas import tpu as pltpu
from jax.sharding import PartitionSpec as P

HD = 64
NEW = 5
STEP = 1024
SPAN = 17
GROUP_MAX = 16
OWNERS = 2
PAD = 16
LANES = 128


fill_score = -1e30


def segment_starts(group_ids, prefix_len, suffix_len):
    groups = jnp.arange(prefix_len.shape[0], dtype=jnp.int32)
    prefix_excl = jnp.cumsum(prefix_len) - prefix_len
    suffix_excl = jnp.cumsum(suffix_len) - suffix_len
    earlier = group_ids[None, :] < groups[:, None]
    prompt_start = prefix_excl + jnp.sum(jnp.where(earlier, suffix_len[None, :], 0), axis=1)
    member = group_ids[:, None] == groups[None, :]
    req_prompt_start = jnp.sum(jnp.where(member, prompt_start[None, :], 0), axis=1)
    req_prompt_len = jnp.sum(jnp.where(member, prefix_len[None, :], 0), axis=1)
    prefix_incl = jnp.sum(jnp.where(member, (prefix_excl + prefix_len)[None, :], 0), axis=1)
    own_start = prefix_incl + suffix_excl
    return (req_prompt_start, req_prompt_len, own_start)


def attend_window(turn, low, span, masked, q_ref, bound_ref, k_ref, v_ref, o_ref, stat_ref):
    rows = span * PAD
    keys = k_ref[...]
    vals = v_ref[...]
    bound = bound_ref[pl.ds(low, span)].reshape(rows, LANES)
    if masked:
        places = turn * STEP + lax.broadcasted_iota(jnp.int32, (1, STEP), 1)
        mask = ((places >= bound[:, 0:1]) & (places < bound[:, 1:2])) | (
            (places >= bound[:, 2:3]) & (places < bound[:, 3:4])
        )
    else:
        first = turn * STEP
        keep = (bound[:, 0:1] <= first) & (bound[:, 1:2] >= first + STEP)
    stat = stat_ref[pl.ds(low, span)].reshape(rows, LANES)
    o_old = o_ref[pl.ds(low, span)].reshape(rows, LANES)
    lane = lax.broadcasted_iota(jnp.int32, (rows, LANES), 1)
    first_half = lane < HD
    o_new = None
    stat_new = jnp.zeros((rows, LANES), jnp.float32)
    for g in range(2):
        query = q_ref[g, pl.ds(low, span)].reshape(rows, LANES)
        score = lax.dot_general(
            query, keys, (((1,), (1,)), ((), ())), preferred_element_type=jnp.float32
        )
        if masked:
            score = jnp.where(mask, score, fill_score)
        m_old = stat[:, 2 * g : 2 * g + 1]
        l_old = stat[:, 2 * g + 1 : 2 * g + 2]
        m_new = jnp.maximum(m_old, jnp.max(score, axis=1, keepdims=True))
        expo = jnp.exp(score - m_new)
        alpha = jnp.exp(m_old - m_new)
        l_new = alpha * l_old + jnp.sum(expo, axis=1, keepdims=True)
        mixed = jnp.dot(expo.astype(jnp.bfloat16), vals, preferred_element_type=jnp.float32)
        if g == 0:
            o_new = jnp.where(first_half, o_old * alpha + mixed, 0.0)
        else:
            o_new = jnp.where(first_half, o_new, o_old * alpha + mixed)
        stat_new = jnp.where(lane == 2 * g, m_new, stat_new)
        stat_new = jnp.where(lane == 2 * g + 1, l_new, stat_new)
    if not masked:
        o_new = jnp.where(keep, o_new, o_old)
        stat_new = jnp.where(keep, stat_new, stat)
    o_ref[pl.ds(low, span)] = o_new.reshape(span, PAD, LANES)
    stat_ref[pl.ds(low, span)] = stat_new.reshape(span, PAD, LANES)


def attend_kernel(firsts_ref, kinds_ref, q_ref, bound_ref, k_ref, v_ref, o_ref, stat_ref):
    turn = pl.program_id(0)
    requests = q_ref.shape[1]
    refs = (q_ref, bound_ref, k_ref, v_ref, o_ref, stat_ref)

    @pl.when(turn == 0)
    def _():
        o_ref[...] = jnp.zeros(o_ref.shape, jnp.float32)
        lane = lax.broadcasted_iota(jnp.int32, stat_ref.shape, 2)
        stat_ref[...] = jnp.where(lane % 2 == 0, fill_score, 0.0).astype(jnp.float32)

    kind = kinds_ref[turn]
    first = firsts_ref[turn]

    @pl.when(kind == 0)
    def _():
        span = min(SPAN, requests)
        attend_window(turn, jnp.minimum(first, requests - span), span, True, *refs)

    @pl.when(kind == 1)
    def _():
        span = min(GROUP_MAX, requests)
        attend_window(turn, jnp.minimum(first, requests - span), span, False, *refs)

    @pl.when(kind == 2)
    def _():
        span = min(OWNERS, requests)
        attend_window(turn, jnp.minimum(first, requests - span), span, True, *refs)


def per_device(
    queries,
    new_keys,
    new_values,
    key_cache,
    value_cache,
    out_weight,
    group_ids,
    prefix_len,
    suffix_len,
):
    rows = queries.shape[0]
    heads_local = queries.shape[1] // HD
    kv_local = key_cache.shape[1] // HD
    repeat = heads_local // kv_local
    requests = rows // NEW
    block = key_cache.shape[0]
    span = min(SPAN, requests)
    tj = NEW * repeat
    prompt_start, prompt_len, own_start = segment_starts(group_ids, prefix_len, suffix_len)
    prompt_end = prompt_start + prompt_len
    own_end = own_start + suffix_len
    offset = lax.axis_index("seq") * block
    steps = block // STEP
    chunk_starts = offset + STEP * jnp.arange(steps, dtype=jnp.int32)
    firsts = jnp.sum((own_end[None, :] <= chunk_starts[:, None]).astype(jnp.int32), axis=1)
    firsts = firsts.astype(jnp.int32)
    chunk_ends = chunk_starts + STEP
    inside = (prompt_start[None, :] <= chunk_starts[:, None]) & (prompt_end[None, :] >= chunk_ends[:, None])
    touches = (prompt_start[None, :] < chunk_ends[:, None]) & (prompt_end[None, :] > chunk_starts[:, None])
    kinds = jnp.where(jnp.any(inside, axis=1), 1, jnp.where(jnp.any(touches, axis=1), 0, 2))
    kinds = kinds.astype(jnp.int32)
    scaled = (queries * jnp.asarray(0.125, queries.dtype)).reshape(requests, NEW, kv_local, repeat, HD)
    scaled = scaled.transpose(2, 0, 1, 3, 4).reshape(kv_local, requests, tj, HD)
    query_pad = jnp.stack(
        [
            jnp.pad(scaled[g], ((0, 0), (0, PAD - tj), (g * HD, LANES - (g + 1) * HD)))
            for g in range(kv_local)
        ]
    )
    edges = jnp.stack([prompt_start, prompt_end, own_start, own_end], axis=1) - offset
    bound = jnp.pad(edges, ((0, 0), (0, LANES - 4)))
    bound = jnp.broadcast_to(bound[:, None, :], (requests, PAD, LANES))
    full = lambda shape: pl.BlockSpec(shape, lambda t, f, k: (0,) * len(shape))
    o_out, stat_out = pl.pallas_call(
        attend_kernel,
        grid_spec=pltpu.PrefetchScalarGridSpec(
            num_scalar_prefetch=2,
            grid=(steps,),
            in_specs=[
                full((kv_local, requests, PAD, LANES)),
                full((requests, PAD, LANES)),
                pl.BlockSpec((STEP, LANES), lambda t, f, k: (t, 0)),
                pl.BlockSpec((STEP, LANES), lambda t, f, k: (t, 0)),
            ],
            out_specs=[full((requests, PAD, LANES)), full((requests, PAD, LANES))],
        ),
        out_shape=[
            jax.ShapeDtypeStruct((requests, PAD, LANES), jnp.float32),
            jax.ShapeDtypeStruct((requests, PAD, LANES), jnp.float32),
        ],
        compiler_params=pltpu.CompilerParams(dimension_semantics=("arbitrary",)),
    )(firsts, kinds, query_pad, bound, key_cache, value_cache)
    width = tj * LANES
    packed = jnp.concatenate(
        [
            o_out[:, :tj, :].reshape(requests, width),
            stat_out[:, :tj, : 2 * kv_local].reshape(requests, tj * 2 * kv_local),
        ],
        axis=1,
    )
    packed = lax.all_to_all(packed, "seq", split_axis=0, concat_axis=0, tiled=True)
    sums = packed[:, :width].reshape(requests, tj, kv_local, HD)
    stats = packed[:, width:].reshape(requests, tj, kv_local, 2)
    maxes = stats[..., 0]
    totals = stats[..., 1]
    own_max = jnp.max(maxes, axis=0)
    rescale = jnp.exp(maxes - own_max[None])
    own_total = jnp.sum(totals * rescale, axis=0)
    own_summed = jnp.sum(sums * rescale[..., None], axis=0)
    mine = lax.axis_index("seq")
    own_query = lax.dynamic_slice_in_dim(queries, mine * NEW, NEW, 0)
    own_query = own_query.reshape(NEW, kv_local, repeat, HD).transpose(0, 2, 1, 3)
    own_query = own_query.reshape(tj, kv_local, HD)
    keys_new = new_keys.reshape(NEW, kv_local, HD)
    values_new = new_values.reshape(NEW, kv_local, HD)
    token_of = jnp.arange(tj) // repeat
    causal = (token_of[:, None] >= jnp.arange(NEW)[None, :])[:, None, :]
    score_new = (
        jnp.einsum("qgd,ugd->qgu", own_query, keys_new, preferred_element_type=jnp.float32)
        * 0.125
    )
    joined = jnp.maximum(own_max, jnp.max(jnp.where(causal, score_new, fill_score), axis=-1))
    expo_new = jnp.where(causal, jnp.exp(score_new - joined[..., None]), 0.0)
    factor_own = jnp.exp(own_max - joined)
    denominator = own_total * factor_own + jnp.sum(expo_new, axis=-1)
    numerator = own_summed * factor_own[..., None] + jnp.einsum(
        "qgu,ugd->qgd",
        expo_new.astype(jnp.bfloat16),
        values_new,
        preferred_element_type=jnp.float32,
    )
    mixed = (numerator / denominator[..., None]).astype(jnp.bfloat16)
    mixed = mixed.reshape(NEW, repeat, kv_local, HD).transpose(0, 2, 1, 3)
    mixed = mixed.reshape(NEW, heads_local * HD)
    partial_out = jnp.dot(mixed, out_weight, preferred_element_type=jnp.float32)
    parts = lax.axis_size("tp")
    piece = partial_out.shape[1] // parts
    pieces = partial_out.reshape(NEW, parts, piece)
    me = lax.axis_index("tp")
    result = lax.dynamic_index_in_dim(pieces, me, 1, keepdims=False)
    for shift in range(1, parts):
        sent = lax.dynamic_index_in_dim(pieces, (me + shift) % parts, 1, keepdims=False)
        pairs = [(i, (i + shift) % parts) for i in range(parts)]
        result = result + lax.ppermute(sent, "tp", pairs)
    return result.astype(jnp.bfloat16)


def solution(mesh):
    placed = (
        P(None, "tp"),
        P("seq", "tp"),
        P("seq", "tp"),
        P("seq", "tp"),
        P("seq", "tp"),
        P("tp", None),
        P(),
        P(),
        P(),
    )
    return jax.shard_map(
        per_device, mesh=mesh, in_specs=placed, out_specs=P("seq", "tp"), check_vma=False
    )
```

```python
import jax
import jax.numpy as jnp
from jax import lax
from jax.experimental import pallas as pl
from jax.experimental.pallas import tpu as pltpu
from jax.sharding import PartitionSpec as P

HD = 64
NEW = 5
STEP = 1024
SPAN = 17
GROUP_MAX = 16
OWNERS = 2
PAD = 16
LANES = 128


fill_score = -1e30


def segment_starts(group_ids, prefix_len, suffix_len):
    groups = jnp.arange(prefix_len.shape[0], dtype=jnp.int32)
    prefix_excl = jnp.cumsum(prefix_len) - prefix_len
    suffix_excl = jnp.cumsum(suffix_len) - suffix_len
    earlier = group_ids[None, :] < groups[:, None]
    prompt_start = prefix_excl + jnp.sum(jnp.where(earlier, suffix_len[None, :], 0), axis=1)
    member = group_ids[:, None] == groups[None, :]
    req_prompt_start = jnp.sum(jnp.where(member, prompt_start[None, :], 0), axis=1)
    req_prompt_len = jnp.sum(jnp.where(member, prefix_len[None, :], 0), axis=1)
    prefix_incl = jnp.sum(jnp.where(member, (prefix_excl + prefix_len)[None, :], 0), axis=1)
    own_start = prefix_incl + suffix_excl
    return (req_prompt_start, req_prompt_len, own_start)


def attend_window(turn, low, span, masked, q_ref, bound_ref, k_ref, v_ref, o_ref, stat_ref):
    rows = span * PAD
    keys = k_ref[...]
    vals = v_ref[...]
    bound = bound_ref[pl.ds(low, span)].reshape(rows, LANES)
    if masked:
        places = turn * STEP + lax.broadcasted_iota(jnp.int32, (1, STEP), 1)
        mask = ((places >= bound[:, 0:1]) & (places < bound[:, 1:2])) | (
            (places >= bound[:, 2:3]) & (places < bound[:, 3:4])
        )
    else:
        first = turn * STEP
        keep = (bound[:, 0:1] <= first) & (bound[:, 1:2] >= first + STEP)
    stat = stat_ref[pl.ds(low, span)].reshape(rows, LANES)
    o_old = o_ref[pl.ds(low, span)].reshape(rows, LANES)
    lane = lax.broadcasted_iota(jnp.int32, (rows, LANES), 1)
    first_half = lane < HD
    query = jnp.concatenate(
        [q_ref[g, pl.ds(low, span)].reshape(rows, LANES) for g in range(2)], axis=0
    )
    score = lax.dot_general(
        query, keys, (((1,), (1,)), ((), ())), preferred_element_type=jnp.float32
    )
    if masked:
        score = jnp.where(jnp.concatenate([mask, mask], axis=0), score, fill_score)
    m_old = jnp.concatenate([stat[:, 0:1], stat[:, 2:3]], axis=0)
    l_old = jnp.concatenate([stat[:, 1:2], stat[:, 3:4]], axis=0)
    m_new = jnp.maximum(m_old, jnp.max(score, axis=1, keepdims=True))
    expo = jnp.exp(score - m_new)
    alpha = jnp.exp(m_old - m_new)
    l_new = alpha * l_old + jnp.sum(expo, axis=1, keepdims=True)
    mixed = jnp.dot(expo.astype(jnp.bfloat16), vals, preferred_element_type=jnp.float32)
    o_new = jnp.where(
        first_half,
        o_old * alpha[:rows] + mixed[:rows],
        o_old * alpha[rows:] + mixed[rows:],
    )
    stat_new = jnp.where(lane == 0, m_new[:rows], 0.0)
    stat_new = jnp.where(lane == 1, l_new[:rows], stat_new)
    stat_new = jnp.where(lane == 2, m_new[rows:], stat_new)
    stat_new = jnp.where(lane == 3, l_new[rows:], stat_new)
    if not masked:
        o_new = jnp.where(keep, o_new, o_old)
        stat_new = jnp.where(keep, stat_new, stat)
    o_ref[pl.ds(low, span)] = o_new.reshape(span, PAD, LANES)
    stat_ref[pl.ds(low, span)] = stat_new.reshape(span, PAD, LANES)


def attend_kernel(firsts_ref, kinds_ref, q_ref, bound_ref, k_ref, v_ref, o_ref, stat_ref):
    turn = pl.program_id(0)
    requests = q_ref.shape[1]
    refs = (q_ref, bound_ref, k_ref, v_ref, o_ref, stat_ref)

    @pl.when(turn == 0)
    def _():
        o_ref[...] = jnp.zeros(o_ref.shape, jnp.float32)
        lane = lax.broadcasted_iota(jnp.int32, stat_ref.shape, 2)
        stat_ref[...] = jnp.where(lane % 2 == 0, fill_score, 0.0).astype(jnp.float32)

    kind = kinds_ref[turn]
    first = firsts_ref[turn]

    @pl.when(kind == 0)
    def _():
        span = min(SPAN, requests)
        attend_window(turn, jnp.minimum(first, requests - span), span, True, *refs)

    @pl.when(kind == 1)
    def _():
        span = min(GROUP_MAX, requests)
        attend_window(turn, jnp.minimum(first, requests - span), span, False, *refs)

    @pl.when(kind == 2)
    def _():
        span = min(OWNERS, requests)
        attend_window(turn, jnp.minimum(first, requests - span), span, True, *refs)


def per_device(
    queries,
    new_keys,
    new_values,
    key_cache,
    value_cache,
    out_weight,
    group_ids,
    prefix_len,
    suffix_len,
):
    rows = queries.shape[0]
    heads_local = queries.shape[1] // HD
    kv_local = key_cache.shape[1] // HD
    repeat = heads_local // kv_local
    requests = rows // NEW
    block = key_cache.shape[0]
    span = min(SPAN, requests)
    tj = NEW * repeat
    prompt_start, prompt_len, own_start = segment_starts(group_ids, prefix_len, suffix_len)
    prompt_end = prompt_start + prompt_len
    own_end = own_start + suffix_len
    offset = lax.axis_index("seq") * block
    steps = block // STEP
    chunk_starts = offset + STEP * jnp.arange(steps, dtype=jnp.int32)
    firsts = jnp.sum((own_end[None, :] <= chunk_starts[:, None]).astype(jnp.int32), axis=1)
    firsts = firsts.astype(jnp.int32)
    chunk_ends = chunk_starts + STEP
    inside = (prompt_start[None, :] <= chunk_starts[:, None]) & (prompt_end[None, :] >= chunk_ends[:, None])
    touches = (prompt_start[None, :] < chunk_ends[:, None]) & (prompt_end[None, :] > chunk_starts[:, None])
    kinds = jnp.where(jnp.any(inside, axis=1), 1, jnp.where(jnp.any(touches, axis=1), 0, 2))
    kinds = kinds.astype(jnp.int32)
    scaled = (queries * jnp.asarray(0.125, queries.dtype)).reshape(requests, NEW, kv_local, repeat, HD)
    scaled = scaled.transpose(2, 0, 1, 3, 4).reshape(kv_local, requests, tj, HD)
    query_pad = jnp.stack(
        [
            jnp.pad(scaled[g], ((0, 0), (0, PAD - tj), (g * HD, LANES - (g + 1) * HD)))
            for g in range(kv_local)
        ]
    )
    edges = jnp.stack([prompt_start, prompt_end, own_start, own_end], axis=1) - offset
    bound = jnp.pad(edges, ((0, 0), (0, LANES - 4)))
    bound = jnp.broadcast_to(bound[:, None, :], (requests, PAD, LANES))
    full = lambda shape: pl.BlockSpec(shape, lambda t, f, k: (0,) * len(shape))
    o_out, stat_out = pl.pallas_call(
        attend_kernel,
        grid_spec=pltpu.PrefetchScalarGridSpec(
            num_scalar_prefetch=2,
            grid=(steps,),
            in_specs=[
                full((kv_local, requests, PAD, LANES)),
                full((requests, PAD, LANES)),
                pl.BlockSpec((STEP, LANES), lambda t, f, k: (t, 0)),
                pl.BlockSpec((STEP, LANES), lambda t, f, k: (t, 0)),
            ],
            out_specs=[full((requests, PAD, LANES)), full((requests, PAD, LANES))],
        ),
        out_shape=[
            jax.ShapeDtypeStruct((requests, PAD, LANES), jnp.float32),
            jax.ShapeDtypeStruct((requests, PAD, LANES), jnp.float32),
        ],
        compiler_params=pltpu.CompilerParams(dimension_semantics=("arbitrary",)),
    )(firsts, kinds, query_pad, bound, key_cache, value_cache)
    width = tj * LANES
    packed = jnp.concatenate(
        [
            o_out[:, :tj, :].reshape(requests, width),
            stat_out[:, :tj, : 2 * kv_local].reshape(requests, tj * 2 * kv_local),
        ],
        axis=1,
    )
    packed = lax.all_to_all(packed, "seq", split_axis=0, concat_axis=0, tiled=True)
    sums = packed[:, :width].reshape(requests, tj, kv_local, HD)
    stats = packed[:, width:].reshape(requests, tj, kv_local, 2)
    maxes = stats[..., 0]
    totals = stats[..., 1]
    own_max = jnp.max(maxes, axis=0)
    rescale = jnp.exp(maxes - own_max[None])
    own_total = jnp.sum(totals * rescale, axis=0)
    own_summed = jnp.sum(sums * rescale[..., None], axis=0)
    mine = lax.axis_index("seq")
    own_query = lax.dynamic_slice_in_dim(queries, mine * NEW, NEW, 0)
    own_query = own_query.reshape(NEW, kv_local, repeat, HD).transpose(0, 2, 1, 3)
    own_query = own_query.reshape(tj, kv_local, HD)
    keys_new = new_keys.reshape(NEW, kv_local, HD)
    values_new = new_values.reshape(NEW, kv_local, HD)
    token_of = jnp.arange(tj) // repeat
    causal = (token_of[:, None] >= jnp.arange(NEW)[None, :])[:, None, :]
    score_new = (
        jnp.einsum("qgd,ugd->qgu", own_query, keys_new, preferred_element_type=jnp.float32)
        * 0.125
    )
    joined = jnp.maximum(own_max, jnp.max(jnp.where(causal, score_new, fill_score), axis=-1))
    expo_new = jnp.where(causal, jnp.exp(score_new - joined[..., None]), 0.0)
    factor_own = jnp.exp(own_max - joined)
    denominator = own_total * factor_own + jnp.sum(expo_new, axis=-1)
    numerator = own_summed * factor_own[..., None] + jnp.einsum(
        "qgu,ugd->qgd",
        expo_new.astype(jnp.bfloat16),
        values_new,
        preferred_element_type=jnp.float32,
    )
    mixed = (numerator / denominator[..., None]).astype(jnp.bfloat16)
    mixed = mixed.reshape(NEW, repeat, kv_local, HD).transpose(0, 2, 1, 3)
    mixed = mixed.reshape(NEW, heads_local * HD)
    partial_out = jnp.dot(mixed, out_weight, preferred_element_type=jnp.float32)
    parts = lax.axis_size("tp")
    piece = partial_out.shape[1] // parts
    pieces = partial_out.reshape(NEW, parts, piece)
    me = lax.axis_index("tp")
    result = lax.dynamic_index_in_dim(pieces, me, 1, keepdims=False)
    for shift in range(1, parts):
        sent = lax.dynamic_index_in_dim(pieces, (me + shift) % parts, 1, keepdims=False)
        pairs = [(i, (i + shift) % parts) for i in range(parts)]
        result = result + lax.ppermute(sent, "tp", pairs)
    return result.astype(jnp.bfloat16)


def solution(mesh):
    placed = (
        P(None, "tp"),
        P("seq", "tp"),
        P("seq", "tp"),
        P("seq", "tp"),
        P("seq", "tp"),
        P("tp", None),
        P(),
        P(),
        P(),
    )
    return jax.shard_map(
        per_device, mesh=mesh, in_specs=placed, out_specs=P("seq", "tp"), check_vma=False
    )
```

```python
import jax
import jax.numpy as jnp
from jax import lax
from jax.experimental import pallas as pl
from jax.experimental.pallas import tpu as pltpu
from jax.sharding import PartitionSpec as P

HD = 64
NEW = 5
STEP = 1024
SPAN = 17
GROUP_MAX = 16
OWNERS = 2
PAD = 16
LANES = 128


fill_score = -1e30


def segment_starts(group_ids, prefix_len, suffix_len):
    groups = jnp.arange(prefix_len.shape[0], dtype=jnp.int32)
    prefix_excl = jnp.cumsum(prefix_len) - prefix_len
    suffix_excl = jnp.cumsum(suffix_len) - suffix_len
    earlier = group_ids[None, :] < groups[:, None]
    prompt_start = prefix_excl + jnp.sum(jnp.where(earlier, suffix_len[None, :], 0), axis=1)
    member = group_ids[:, None] == groups[None, :]
    req_prompt_start = jnp.sum(jnp.where(member, prompt_start[None, :], 0), axis=1)
    req_prompt_len = jnp.sum(jnp.where(member, prefix_len[None, :], 0), axis=1)
    prefix_incl = jnp.sum(jnp.where(member, (prefix_excl + prefix_len)[None, :], 0), axis=1)
    own_start = prefix_incl + suffix_excl
    return (req_prompt_start, req_prompt_len, own_start)


def attend_window(turn, low, span, masked, q_ref, bound_ref, k_ref, v_ref, o_ref, stat_ref):
    rows = span * PAD
    keys = k_ref[...]
    vals = v_ref[...]
    bound = bound_ref[pl.ds(low, span)].reshape(rows, LANES)
    if masked:
        places = turn * STEP + lax.broadcasted_iota(jnp.int32, (1, STEP), 1)
        mask = ((places >= bound[:, 0:1]) & (places < bound[:, 1:2])) | (
            (places >= bound[:, 2:3]) & (places < bound[:, 3:4])
        )
    else:
        first = turn * STEP
        keep = (bound[:, 0:1] <= first) & (bound[:, 1:2] >= first + STEP)
    stat = stat_ref[pl.ds(low, span)].reshape(rows, LANES)
    o_old = o_ref[pl.ds(low, span)].reshape(rows, LANES)
    lane = lax.broadcasted_iota(jnp.int32, (rows, LANES), 1)
    first_half = lane < HD
    o_new = None
    stat_new = jnp.zeros((rows, LANES), jnp.float32)
    for g in range(2):
        query = q_ref[g, pl.ds(low, span)].reshape(rows, LANES)
        score = lax.dot_general(
            query, keys, (((1,), (1,)), ((), ())), preferred_element_type=jnp.float32
        )
        if masked:
            score = jnp.where(mask, score, fill_score)
        m_old = stat[:, 2 * g : 2 * g + 1]
        l_old = stat[:, 2 * g + 1 : 2 * g + 2]
        m_new = jnp.maximum(m_old, jnp.max(score, axis=1, keepdims=True))
        expo = jnp.exp(score - m_new)
        alpha = jnp.exp(m_old - m_new)
        l_new = alpha * l_old + jnp.sum(expo, axis=1, keepdims=True)
        mixed = jnp.dot(expo.astype(jnp.bfloat16), vals, preferred_element_type=jnp.float32)
        if g == 0:
            o_new = jnp.where(first_half, o_old * alpha + mixed, 0.0)
        else:
            o_new = jnp.where(first_half, o_new, o_old * alpha + mixed)
        stat_new = jnp.where(lane == 2 * g, m_new, stat_new)
        stat_new = jnp.where(lane == 2 * g + 1, l_new, stat_new)
    if not masked:
        o_new = jnp.where(keep, o_new, o_old)
        stat_new = jnp.where(keep, stat_new, stat)
    o_ref[pl.ds(low, span)] = o_new.reshape(span, PAD, LANES)
    stat_ref[pl.ds(low, span)] = stat_new.reshape(span, PAD, LANES)


def attend_kernel(
    gid_ref, pre_ref, suf_ref, off_ref, q_ref, k_ref, v_ref, o_ref, stat_ref, edge_ref, bound_ref
):
    turn = pl.program_id(0)
    requests = q_ref.shape[1]
    groups = pre_ref.shape[0]
    refs = (q_ref, bound_ref, k_ref, v_ref, o_ref, stat_ref)

    @pl.when(turn == 0)
    def _():
        o_ref[...] = jnp.zeros(o_ref.shape, jnp.float32)
        lane3 = lax.broadcasted_iota(jnp.int32, stat_ref.shape, 2)
        stat_ref[...] = jnp.where(lane3 % 2 == 0, fill_score, 0.0).astype(jnp.float32)
        offset = off_ref[0]

        def sums(r, carry):
            run = carry[0]
            g = gid_ref[r]
            s = suf_ref[r]
            edge_ref[2 * requests + r] = run
            acc = tuple(a + jnp.where(g < gg, s, 0) for gg, a in enumerate(carry[1:]))
            return (run + s,) + acc

        carry = lax.fori_loop(0, requests, sums, (jnp.int32(0),) * (1 + groups))
        earlier = carry[1:]
        prefix_excl = []
        running = jnp.int32(0)
        for gg in range(groups):
            prefix_excl.append(running)
            running = running + pre_ref[gg]
        lane = lax.broadcasted_iota(jnp.int32, (PAD, LANES), 1)

        def edges(r, c):
            g = gid_ref[r]
            ps = jnp.int32(0)
            plen = jnp.int32(0)
            pin = jnp.int32(0)
            for gg in range(groups):
                hit = g == gg
                ps = ps + jnp.where(hit, prefix_excl[gg] + earlier[gg], 0)
                plen = plen + jnp.where(hit, pre_ref[gg], 0)
                pin = pin + jnp.where(hit, prefix_excl[gg] + pre_ref[gg], 0)
            os_ = pin + edge_ref[2 * requests + r]
            oe = os_ + suf_ref[r]
            ps = ps - offset
            pe = ps + plen
            os_ = os_ - offset
            oe = oe - offset
            edge_ref[r] = ps
            edge_ref[requests + r] = pe
            edge_ref[2 * requests + r] = os_
            edge_ref[3 * requests + r] = oe
            bound_ref[r] = jnp.where(
                lane == 0, ps, jnp.where(lane == 1, pe, jnp.where(lane == 2, os_, oe))
            )
            return c

        lax.fori_loop(0, requests, edges, 0)

    begin = turn * STEP

    def scan(r, carry):
        first, inside, touch = carry
        ps = edge_ref[r]
        pe = edge_ref[requests + r]
        oe = edge_ref[3 * requests + r]
        first = first + jnp.where(oe <= begin, 1, 0)
        inside = jnp.maximum(inside, jnp.where((ps <= begin) & (pe >= begin + STEP), 1, 0))
        touch = jnp.maximum(touch, jnp.where((ps < begin + STEP) & (pe > begin), 1, 0))
        return (first, inside, touch)

    zero = jnp.int32(0)
    first, inside, touch = lax.fori_loop(0, requests, scan, (zero, zero, zero))

    @pl.when((inside == 0) & (touch == 1))
    def _():
        span = min(SPAN, requests)
        attend_window(turn, jnp.minimum(first, requests - span), span, True, *refs)

    @pl.when(inside == 1)
    def _():
        span = min(GROUP_MAX, requests)
        attend_window(turn, jnp.minimum(first, requests - span), span, False, *refs)

    @pl.when((inside == 0) & (touch == 0))
    def _():
        span = min(OWNERS, requests)
        attend_window(turn, jnp.minimum(first, requests - span), span, True, *refs)


def per_device(
    queries,
    new_keys,
    new_values,
    key_cache,
    value_cache,
    out_weight,
    group_ids,
    prefix_len,
    suffix_len,
):
    rows = queries.shape[0]
    heads_local = queries.shape[1] // HD
    kv_local = key_cache.shape[1] // HD
    repeat = heads_local // kv_local
    requests = rows // NEW
    block = key_cache.shape[0]
    span = min(SPAN, requests)
    tj = NEW * repeat
    steps = block // STEP
    offset = jnp.full((1,), lax.axis_index("seq") * block, jnp.int32)
    scaled = (queries * jnp.asarray(0.125, queries.dtype)).reshape(requests, NEW, kv_local, repeat, HD)
    scaled = scaled.transpose(2, 0, 1, 3, 4).reshape(kv_local, requests, tj, HD)
    query_pad = jnp.stack(
        [
            jnp.pad(scaled[g], ((0, 0), (0, PAD - tj), (g * HD, LANES - (g + 1) * HD)))
            for g in range(kv_local)
        ]
    )
    full = lambda shape: pl.BlockSpec(shape, lambda t, *_: (0,) * len(shape))
    o_out, stat_out = pl.pallas_call(
        attend_kernel,
        grid_spec=pltpu.PrefetchScalarGridSpec(
            num_scalar_prefetch=4,
            grid=(steps,),
            in_specs=[
                full((kv_local, requests, PAD, LANES)),
                pl.BlockSpec((STEP, LANES), lambda t, *_: (t, 0)),
                pl.BlockSpec((STEP, LANES), lambda t, *_: (t, 0)),
            ],
            out_specs=[full((requests, PAD, LANES)), full((requests, PAD, LANES))],
            scratch_shapes=[
                pltpu.SMEM((4 * requests,), jnp.int32),
                pltpu.VMEM((requests, PAD, LANES), jnp.int32),
            ],
        ),
        out_shape=[
            jax.ShapeDtypeStruct((requests, PAD, LANES), jnp.float32),
            jax.ShapeDtypeStruct((requests, PAD, LANES), jnp.float32),
        ],
        compiler_params=pltpu.CompilerParams(dimension_semantics=("arbitrary",)),
    )(group_ids, prefix_len, suffix_len, offset, query_pad, key_cache, value_cache)
    width = tj * LANES
    packed = jnp.concatenate(
        [
            o_out[:, :tj, :].reshape(requests, width),
            stat_out[:, :tj, : 2 * kv_local].reshape(requests, tj * 2 * kv_local),
        ],
        axis=1,
    )
    packed = lax.all_to_all(packed, "seq", split_axis=0, concat_axis=0, tiled=True)
    sums = packed[:, :width].reshape(requests, tj, kv_local, HD)
    stats = packed[:, width:].reshape(requests, tj, kv_local, 2)
    maxes = stats[..., 0]
    totals = stats[..., 1]
    own_max = jnp.max(maxes, axis=0)
    rescale = jnp.exp(maxes - own_max[None])
    own_total = jnp.sum(totals * rescale, axis=0)
    own_summed = jnp.sum(sums * rescale[..., None], axis=0)
    mine = lax.axis_index("seq")
    own_query = lax.dynamic_slice_in_dim(queries, mine * NEW, NEW, 0)
    own_query = own_query.reshape(NEW, kv_local, repeat, HD).transpose(0, 2, 1, 3)
    own_query = own_query.reshape(tj, kv_local, HD)
    keys_new = new_keys.reshape(NEW, kv_local, HD)
    values_new = new_values.reshape(NEW, kv_local, HD)
    token_of = jnp.arange(tj) // repeat
    causal = (token_of[:, None] >= jnp.arange(NEW)[None, :])[:, None, :]
    score_new = (
        jnp.einsum("qgd,ugd->qgu", own_query, keys_new, preferred_element_type=jnp.float32)
        * 0.125
    )
    joined = jnp.maximum(own_max, jnp.max(jnp.where(causal, score_new, fill_score), axis=-1))
    expo_new = jnp.where(causal, jnp.exp(score_new - joined[..., None]), 0.0)
    factor_own = jnp.exp(own_max - joined)
    denominator = own_total * factor_own + jnp.sum(expo_new, axis=-1)
    numerator = own_summed * factor_own[..., None] + jnp.einsum(
        "qgu,ugd->qgd",
        expo_new.astype(jnp.bfloat16),
        values_new,
        preferred_element_type=jnp.float32,
    )
    mixed = (numerator / denominator[..., None]).astype(jnp.bfloat16)
    mixed = mixed.reshape(NEW, repeat, kv_local, HD).transpose(0, 2, 1, 3)
    mixed = mixed.reshape(NEW, heads_local * HD)
    partial_out = jnp.dot(mixed, out_weight, preferred_element_type=jnp.float32)
    parts = lax.axis_size("tp")
    piece = partial_out.shape[1] // parts
    pieces = partial_out.reshape(NEW, parts, piece)
    me = lax.axis_index("tp")
    result = lax.dynamic_index_in_dim(pieces, me, 1, keepdims=False)
    for shift in range(1, parts):
        sent = lax.dynamic_index_in_dim(pieces, (me + shift) % parts, 1, keepdims=False)
        pairs = [(i, (i + shift) % parts) for i in range(parts)]
        result = result + lax.ppermute(sent, "tp", pairs)
    return result.astype(jnp.bfloat16)


def solution(mesh):
    placed = (
        P(None, "tp"),
        P("seq", "tp"),
        P("seq", "tp"),
        P("seq", "tp"),
        P("seq", "tp"),
        P("tp", None),
        P(),
        P(),
        P(),
    )
    return jax.shard_map(
        per_device, mesh=mesh, in_specs=placed, out_specs=P("seq", "tp"), check_vma=False
    )
```

```python
import jax
import jax.numpy as jnp
from jax import lax
from jax.experimental import pallas as pl
from jax.experimental.pallas import tpu as pltpu
from jax.sharding import PartitionSpec as P

HD = 64
NEW = 5
STEP = 1024
SPAN = 17
GROUP_MAX = 16
OWNERS = 2
CHUNKS = 8
PAD = 16
LANES = 128


fill_score = -1e30


def segment_starts(group_ids, prefix_len, suffix_len):
    groups = jnp.arange(prefix_len.shape[0], dtype=jnp.int32)
    prefix_excl = jnp.cumsum(prefix_len) - prefix_len
    suffix_excl = jnp.cumsum(suffix_len) - suffix_len
    earlier = group_ids[None, :] < groups[:, None]
    prompt_start = prefix_excl + jnp.sum(jnp.where(earlier, suffix_len[None, :], 0), axis=1)
    member = group_ids[:, None] == groups[None, :]
    req_prompt_start = jnp.sum(jnp.where(member, prompt_start[None, :], 0), axis=1)
    req_prompt_len = jnp.sum(jnp.where(member, prefix_len[None, :], 0), axis=1)
    prefix_incl = jnp.sum(jnp.where(member, (prefix_excl + prefix_len)[None, :], 0), axis=1)
    own_start = prefix_incl + suffix_excl
    return (req_prompt_start, req_prompt_len, own_start)


def attend_window(turn, low, span, masked, q_ref, bound_ref, k_ref, v_ref, o_ref, stat_ref):
    rows = span * PAD
    keys = k_ref[...]
    vals = v_ref[...]
    bound = bound_ref[pl.ds(low, span)].reshape(rows, LANES)
    if masked:
        places = turn * STEP + lax.broadcasted_iota(jnp.int32, (1, STEP), 1)
        mask = ((places >= bound[:, 0:1]) & (places < bound[:, 1:2])) | (
            (places >= bound[:, 2:3]) & (places < bound[:, 3:4])
        )
    else:
        first = turn * STEP
        keep = (bound[:, 0:1] <= first) & (bound[:, 1:2] >= first + STEP)
    stat = stat_ref[pl.ds(low, span)].reshape(rows, LANES)
    o_old = o_ref[pl.ds(low, span)].reshape(rows, LANES)
    lane = lax.broadcasted_iota(jnp.int32, (rows, LANES), 1)
    first_half = lane < HD
    o_new = None
    stat_new = jnp.zeros((rows, LANES), jnp.float32)
    for g in range(2):
        query = q_ref[g, pl.ds(low, span)].reshape(rows, LANES)
        score = lax.dot_general(
            query, keys, (((1,), (1,)), ((), ())), preferred_element_type=jnp.float32
        )
        if masked:
            score = jnp.where(mask, score, fill_score)
        m_old = stat[:, 2 * g : 2 * g + 1]
        l_old = stat[:, 2 * g + 1 : 2 * g + 2]
        m_new = jnp.maximum(m_old, jnp.max(score, axis=1, keepdims=True))
        expo = jnp.exp(score - m_new)
        alpha = jnp.exp(m_old - m_new)
        l_new = alpha * l_old + jnp.sum(expo, axis=1, keepdims=True)
        mixed = jnp.dot(expo.astype(jnp.bfloat16), vals, preferred_element_type=jnp.float32)
        if g == 0:
            o_new = jnp.where(first_half, o_old * alpha + mixed, 0.0)
        else:
            o_new = jnp.where(first_half, o_new, o_old * alpha + mixed)
        stat_new = jnp.where(lane == 2 * g, m_new, stat_new)
        stat_new = jnp.where(lane == 2 * g + 1, l_new, stat_new)
    if not masked:
        o_new = jnp.where(keep, o_new, o_old)
        stat_new = jnp.where(keep, stat_new, stat)
    o_ref[pl.ds(low, span)] = o_new.reshape(span, PAD, LANES)
    stat_ref[pl.ds(low, span)] = stat_new.reshape(span, PAD, LANES)


def attend_kernel(
    gid_ref, pre_ref, suf_ref, off_ref, q_ref, k_ref, v_ref, o_ref, stat_ref, edge_ref, bound_ref,
    chunk_ref,
):
    turn = pl.program_id(0)
    requests = q_ref.shape[1]
    groups = pre_ref.shape[0]
    refs = (q_ref, bound_ref, k_ref, v_ref, o_ref, stat_ref)

    @pl.when(turn == 0)
    def _():
        o_ref[...] = jnp.zeros(o_ref.shape, jnp.float32)
        lane3 = lax.broadcasted_iota(jnp.int32, stat_ref.shape, 2)
        stat_ref[...] = jnp.where(lane3 % 2 == 0, fill_score, 0.0).astype(jnp.float32)
        offset = off_ref[0]

        def sums(r, carry):
            run = carry[0]
            g = gid_ref[r]
            s = suf_ref[r]
            edge_ref[2 * requests + r] = run
            acc = tuple(a + jnp.where(g < gg, s, 0) for gg, a in enumerate(carry[1:]))
            return (run + s,) + acc

        carry = lax.fori_loop(0, requests, sums, (jnp.int32(0),) * (1 + groups), unroll=8)
        earlier = carry[1:]
        prefix_excl = []
        running = jnp.int32(0)
        for gg in range(groups):
            prefix_excl.append(running)
            running = running + pre_ref[gg]
        lane = lax.broadcasted_iota(jnp.int32, (PAD, LANES), 1)

        def edges(r, c):
            g = gid_ref[r]
            ps = jnp.int32(0)
            plen = jnp.int32(0)
            pin = jnp.int32(0)
            for gg in range(groups):
                hit = g == gg
                ps = ps + jnp.where(hit, prefix_excl[gg] + earlier[gg], 0)
                plen = plen + jnp.where(hit, pre_ref[gg], 0)
                pin = pin + jnp.where(hit, prefix_excl[gg] + pre_ref[gg], 0)
            os_ = pin + edge_ref[2 * requests + r]
            oe = os_ + suf_ref[r]
            ps = ps - offset
            pe = ps + plen
            os_ = os_ - offset
            oe = oe - offset
            edge_ref[r] = ps
            edge_ref[requests + r] = pe
            edge_ref[2 * requests + r] = os_
            edge_ref[3 * requests + r] = oe
            bound_ref[r] = jnp.where(
                lane == 0, ps, jnp.where(lane == 1, pe, jnp.where(lane == 2, os_, oe))
            )
            firsts = []
            insides = []
            touches = []
            for t in range(CHUNKS):
                begin = t * STEP
                firsts.append(c[t] + jnp.where(oe <= begin, 1, 0))
                hold = (ps <= begin) & (pe >= begin + STEP)
                insides.append(jnp.maximum(c[CHUNKS + t], jnp.where(hold, 1, 0)))
                meet = (ps < begin + STEP) & (pe > begin)
                touches.append(jnp.maximum(c[2 * CHUNKS + t], jnp.where(meet, 1, 0)))
            return tuple(firsts + insides + touches)

        steps = pl.num_programs(0)
        zero = jnp.int32(0)
        tables = lax.fori_loop(0, requests, edges, (zero,) * (3 * CHUNKS), unroll=8)
        for t in range(CHUNKS):
            chunk_ref[t] = tables[t]
            chunk_ref[CHUNKS + t] = tables[CHUNKS + t]
            chunk_ref[2 * CHUNKS + t] = tables[2 * CHUNKS + t]

    first = chunk_ref[turn]
    inside = chunk_ref[CHUNKS + turn]
    touch = chunk_ref[2 * CHUNKS + turn]

    @pl.when((inside == 0) & (touch == 1))
    def _():
        span = min(SPAN, requests)
        attend_window(turn, jnp.minimum(first, requests - span), span, True, *refs)

    @pl.when(inside == 1)
    def _():
        span = min(GROUP_MAX, requests)
        attend_window(turn, jnp.minimum(first, requests - span), span, False, *refs)

    @pl.when((inside == 0) & (touch == 0))
    def _():
        span = min(OWNERS, requests)
        attend_window(turn, jnp.minimum(first, requests - span), span, True, *refs)


def per_device(
    queries,
    new_keys,
    new_values,
    key_cache,
    value_cache,
    out_weight,
    group_ids,
    prefix_len,
    suffix_len,
):
    rows = queries.shape[0]
    heads_local = queries.shape[1] // HD
    kv_local = key_cache.shape[1] // HD
    repeat = heads_local // kv_local
    requests = rows // NEW
    block = key_cache.shape[0]
    span = min(SPAN, requests)
    tj = NEW * repeat
    steps = block // STEP
    assert steps == CHUNKS
    offset = jnp.full((1,), lax.axis_index("seq") * block, jnp.int32)
    scaled = (queries * jnp.asarray(0.125, queries.dtype)).reshape(requests, NEW, kv_local, repeat, HD)
    scaled = scaled.transpose(2, 0, 1, 3, 4).reshape(kv_local, requests, tj, HD)
    query_pad = jnp.stack(
        [
            jnp.pad(scaled[g], ((0, 0), (0, PAD - tj), (g * HD, LANES - (g + 1) * HD)))
            for g in range(kv_local)
        ]
    )
    full = lambda shape: pl.BlockSpec(shape, lambda t, *_: (0,) * len(shape))
    o_out, stat_out = pl.pallas_call(
        attend_kernel,
        grid_spec=pltpu.PrefetchScalarGridSpec(
            num_scalar_prefetch=4,
            grid=(steps,),
            in_specs=[
                full((kv_local, requests, PAD, LANES)),
                pl.BlockSpec((STEP, LANES), lambda t, *_: (t, 0)),
                pl.BlockSpec((STEP, LANES), lambda t, *_: (t, 0)),
            ],
            out_specs=[full((requests, PAD, LANES)), full((requests, PAD, LANES))],
            scratch_shapes=[
                pltpu.SMEM((4 * requests,), jnp.int32),
                pltpu.VMEM((requests, PAD, LANES), jnp.int32),
                pltpu.SMEM((3 * steps,), jnp.int32),
            ],
        ),
        out_shape=[
            jax.ShapeDtypeStruct((requests, PAD, LANES), jnp.float32),
            jax.ShapeDtypeStruct((requests, PAD, LANES), jnp.float32),
        ],
        compiler_params=pltpu.CompilerParams(dimension_semantics=("arbitrary",)),
    )(group_ids, prefix_len, suffix_len, offset, query_pad, key_cache, value_cache)
    width = tj * LANES
    packed = jnp.concatenate(
        [
            o_out[:, :tj, :].reshape(requests, width),
            stat_out[:, :tj, : 2 * kv_local].reshape(requests, tj * 2 * kv_local),
        ],
        axis=1,
    )
    packed = lax.all_to_all(packed, "seq", split_axis=0, concat_axis=0, tiled=True)
    sums = packed[:, :width].reshape(requests, tj, kv_local, HD)
    stats = packed[:, width:].reshape(requests, tj, kv_local, 2)
    maxes = stats[..., 0]
    totals = stats[..., 1]
    own_max = jnp.max(maxes, axis=0)
    rescale = jnp.exp(maxes - own_max[None])
    own_total = jnp.sum(totals * rescale, axis=0)
    own_summed = jnp.sum(sums * rescale[..., None], axis=0)
    mine = lax.axis_index("seq")
    own_query = lax.dynamic_slice_in_dim(queries, mine * NEW, NEW, 0)
    own_query = own_query.reshape(NEW, kv_local, repeat, HD).transpose(0, 2, 1, 3)
    own_query = own_query.reshape(tj, kv_local, HD)
    keys_new = new_keys.reshape(NEW, kv_local, HD)
    values_new = new_values.reshape(NEW, kv_local, HD)
    token_of = jnp.arange(tj) // repeat
    causal = (token_of[:, None] >= jnp.arange(NEW)[None, :])[:, None, :]
    score_new = (
        jnp.einsum("qgd,ugd->qgu", own_query, keys_new, preferred_element_type=jnp.float32)
        * 0.125
    )
    joined = jnp.maximum(own_max, jnp.max(jnp.where(causal, score_new, fill_score), axis=-1))
    expo_new = jnp.where(causal, jnp.exp(score_new - joined[..., None]), 0.0)
    factor_own = jnp.exp(own_max - joined)
    denominator = own_total * factor_own + jnp.sum(expo_new, axis=-1)
    numerator = own_summed * factor_own[..., None] + jnp.einsum(
        "qgu,ugd->qgd",
        expo_new.astype(jnp.bfloat16),
        values_new,
        preferred_element_type=jnp.float32,
    )
    mixed = (numerator / denominator[..., None]).astype(jnp.bfloat16)
    mixed = mixed.reshape(NEW, repeat, kv_local, HD).transpose(0, 2, 1, 3)
    mixed = mixed.reshape(NEW, heads_local * HD)
    partial_out = jnp.dot(mixed, out_weight, preferred_element_type=jnp.float32)
    parts = lax.axis_size("tp")
    piece = partial_out.shape[1] // parts
    pieces = partial_out.reshape(NEW, parts, piece)
    me = lax.axis_index("tp")
    result = lax.dynamic_index_in_dim(pieces, me, 1, keepdims=False)
    for shift in range(1, parts):
        sent = lax.dynamic_index_in_dim(pieces, (me + shift) % parts, 1, keepdims=False)
        pairs = [(i, (i + shift) % parts) for i in range(parts)]
        result = result + lax.ppermute(sent, "tp", pairs)
    return result.astype(jnp.bfloat16)


def solution(mesh):
    placed = (
        P(None, "tp"),
        P("seq", "tp"),
        P("seq", "tp"),
        P("seq", "tp"),
        P("seq", "tp"),
        P("tp", None),
        P(),
        P(),
        P(),
    )
    return jax.shard_map(
        per_device, mesh=mesh, in_specs=placed, out_specs=P("seq", "tp"), check_vma=False
    )
```

```python
import jax
import jax.numpy as jnp
from jax import lax
from jax.experimental import pallas as pl
from jax.experimental.pallas import tpu as pltpu
from jax.sharding import PartitionSpec as P

HD = 64
NEW = 5
STEP = 1024
SPAN = 17
GROUP_MAX = 16
OWNERS = 2
CHUNKS = 8
PAD = 16
LANES = 128


fill_score = -1e30


def segment_starts(group_ids, prefix_len, suffix_len):
    groups = jnp.arange(prefix_len.shape[0], dtype=jnp.int32)
    prefix_excl = jnp.cumsum(prefix_len) - prefix_len
    suffix_excl = jnp.cumsum(suffix_len) - suffix_len
    earlier = group_ids[None, :] < groups[:, None]
    prompt_start = prefix_excl + jnp.sum(jnp.where(earlier, suffix_len[None, :], 0), axis=1)
    member = group_ids[:, None] == groups[None, :]
    req_prompt_start = jnp.sum(jnp.where(member, prompt_start[None, :], 0), axis=1)
    req_prompt_len = jnp.sum(jnp.where(member, prefix_len[None, :], 0), axis=1)
    prefix_incl = jnp.sum(jnp.where(member, (prefix_excl + prefix_len)[None, :], 0), axis=1)
    own_start = prefix_incl + suffix_excl
    return (req_prompt_start, req_prompt_len, own_start)


def attend_window(turn, low, span, masked, q_ref, bound_ref, k_ref, v_ref, o_ref, stat_ref):
    rows = span * PAD
    keys = k_ref[...]
    vals = v_ref[...]
    bound = bound_ref[pl.ds(low, span)].reshape(rows, LANES)
    if masked:
        places = turn * STEP + lax.broadcasted_iota(jnp.int32, (1, STEP), 1)
        mask = ((places >= bound[:, 0:1]) & (places < bound[:, 1:2])) | (
            (places >= bound[:, 2:3]) & (places < bound[:, 3:4])
        )
    else:
        first = turn * STEP
        keep = (bound[:, 0:1] <= first) & (bound[:, 1:2] >= first + STEP)
    stat = stat_ref[pl.ds(low, span)].reshape(rows, LANES)
    o_old = o_ref[pl.ds(low, span)].reshape(rows, LANES)
    lane = lax.broadcasted_iota(jnp.int32, (rows, LANES), 1)
    first_half = lane < HD
    o_new = None
    stat_new = jnp.zeros((rows, LANES), jnp.float32)
    for g in range(2):
        query = q_ref[g, pl.ds(low, span)].reshape(rows, LANES)
        score = lax.dot_general(
            query, keys, (((1,), (1,)), ((), ())), preferred_element_type=jnp.float32
        )
        if masked:
            score = jnp.where(mask, score, fill_score)
        m_old = stat[:, 2 * g : 2 * g + 1]
        l_old = stat[:, 2 * g + 1 : 2 * g + 2]
        m_new = jnp.maximum(m_old, jnp.max(score, axis=1, keepdims=True))
        expo = jnp.exp(score - m_new)
        alpha = jnp.exp(m_old - m_new)
        l_new = alpha * l_old + jnp.sum(expo, axis=1, keepdims=True)
        mixed = jnp.dot(expo.astype(jnp.bfloat16), vals, preferred_element_type=jnp.float32)
        if g == 0:
            o_new = jnp.where(first_half, o_old * alpha + mixed, 0.0)
        else:
            o_new = jnp.where(first_half, o_new, o_old * alpha + mixed)
        stat_new = jnp.where(lane == 2 * g, m_new, stat_new)
        stat_new = jnp.where(lane == 2 * g + 1, l_new, stat_new)
    if not masked:
        o_new = jnp.where(keep, o_new, o_old)
        stat_new = jnp.where(keep, stat_new, stat)
    o_ref[pl.ds(low, span)] = o_new.reshape(span, PAD, LANES)
    stat_ref[pl.ds(low, span)] = stat_new.reshape(span, PAD, LANES)


def attend_kernel(
    gid_ref, pre_ref, suf_ref, off_ref, q_ref, k_ref, v_ref, o_ref, stat_ref, edge_ref, bound_ref,
    chunk_ref, table_ref,
):
    turn = pl.program_id(0)
    requests = q_ref.shape[1]
    groups = pre_ref.shape[0]
    refs = (q_ref, bound_ref, k_ref, v_ref, o_ref, stat_ref)

    @pl.when(turn == 0)
    def _():
        o_ref[...] = jnp.zeros(o_ref.shape, jnp.float32)
        lane3 = lax.broadcasted_iota(jnp.int32, stat_ref.shape, 2)
        stat_ref[...] = jnp.where(lane3 % 2 == 0, fill_score, 0.0).astype(jnp.float32)
        offset = off_ref[0]
        for gg in range(groups):
            table_ref[3 * groups + gg] = 0
        for t in range(CHUNKS + 2):
            chunk_ref[3 * CHUNKS + t] = 0

        def sums(r, run):
            g = gid_ref[r]
            s = suf_ref[r]
            edge_ref[r] = run
            table_ref[3 * groups + g] = table_ref[3 * groups + g] + s
            return run + s

        lax.fori_loop(0, requests, sums, jnp.int32(0), unroll=8)
        prefix_excl = jnp.int32(0)
        earlier = jnp.int32(0)
        starts = []
        ends = []
        for gg in range(groups):
            start = prefix_excl + earlier - offset
            starts.append(start)
            ends.append(start + pre_ref[gg])
            table_ref[gg] = start
            table_ref[groups + gg] = start + pre_ref[gg]
            table_ref[2 * groups + gg] = prefix_excl + pre_ref[gg] - offset
            earlier = earlier + table_ref[3 * groups + gg]
            prefix_excl = prefix_excl + pre_ref[gg]
        for t in range(CHUNKS):
            begin = t * STEP
            inside = jnp.int32(0)
            touch = jnp.int32(0)
            for gg in range(groups):
                hold = (starts[gg] <= begin) & (ends[gg] >= begin + STEP)
                meet = (starts[gg] < begin + STEP) & (ends[gg] > begin)
                inside = jnp.maximum(inside, jnp.where(hold, 1, 0))
                touch = jnp.maximum(touch, jnp.where(meet, 1, 0))
            chunk_ref[CHUNKS + t] = inside
            chunk_ref[2 * CHUNKS + t] = touch
        lane = lax.broadcasted_iota(jnp.int32, (PAD, LANES), 1)

        def edges(r, c):
            g = gid_ref[r]
            ps = table_ref[g]
            pe = table_ref[groups + g]
            os_ = table_ref[2 * groups + g] + edge_ref[r]
            oe = os_ + suf_ref[r]
            bound_ref[r] = jnp.where(
                lane == 0, ps, jnp.where(lane == 1, pe, jnp.where(lane == 2, os_, oe))
            )
            bucket = jnp.clip(jnp.right_shift(oe + (STEP - 1), STEP.bit_length() - 1), 0, CHUNKS + 1)
            chunk_ref[3 * CHUNKS + bucket] = chunk_ref[3 * CHUNKS + bucket] + 1
            return c

        lax.fori_loop(0, requests, edges, 0, unroll=8)
        count = jnp.int32(0)
        for t in range(CHUNKS):
            count = count + chunk_ref[3 * CHUNKS + t]
            chunk_ref[t] = count

    first = chunk_ref[turn]
    inside = chunk_ref[CHUNKS + turn]
    touch = chunk_ref[2 * CHUNKS + turn]

    @pl.when((inside == 0) & (touch == 1))
    def _():
        span = min(SPAN, requests)
        attend_window(turn, jnp.minimum(first, requests - span), span, True, *refs)

    @pl.when(inside == 1)
    def _():
        span = min(GROUP_MAX, requests)
        attend_window(turn, jnp.minimum(first, requests - span), span, False, *refs)

    @pl.when((inside == 0) & (touch == 0))
    def _():
        span = min(OWNERS, requests)
        attend_window(turn, jnp.minimum(first, requests - span), span, True, *refs)


def per_device(
    queries,
    new_keys,
    new_values,
    key_cache,
    value_cache,
    out_weight,
    group_ids,
    prefix_len,
    suffix_len,
):
    rows = queries.shape[0]
    heads_local = queries.shape[1] // HD
    kv_local = key_cache.shape[1] // HD
    repeat = heads_local // kv_local
    requests = rows // NEW
    block = key_cache.shape[0]
    span = min(SPAN, requests)
    tj = NEW * repeat
    steps = block // STEP
    assert steps == CHUNKS
    offset = jnp.full((1,), lax.axis_index("seq") * block, jnp.int32)
    scaled = (queries * jnp.asarray(0.125, queries.dtype)).reshape(requests, NEW, kv_local, repeat, HD)
    scaled = scaled.transpose(2, 0, 1, 3, 4).reshape(kv_local, requests, tj, HD)
    query_pad = jnp.stack(
        [
            jnp.pad(scaled[g], ((0, 0), (0, PAD - tj), (g * HD, LANES - (g + 1) * HD)))
            for g in range(kv_local)
        ]
    )
    full = lambda shape: pl.BlockSpec(shape, lambda t, *_: (0,) * len(shape))
    o_out, stat_out = pl.pallas_call(
        attend_kernel,
        grid_spec=pltpu.PrefetchScalarGridSpec(
            num_scalar_prefetch=4,
            grid=(steps,),
            in_specs=[
                full((kv_local, requests, PAD, LANES)),
                pl.BlockSpec((STEP, LANES), lambda t, *_: (t, 0)),
                pl.BlockSpec((STEP, LANES), lambda t, *_: (t, 0)),
            ],
            out_specs=[full((requests, PAD, LANES)), full((requests, PAD, LANES))],
            scratch_shapes=[
                pltpu.SMEM((requests,), jnp.int32),
                pltpu.VMEM((requests, PAD, LANES), jnp.int32),
                pltpu.SMEM((4 * steps + 2,), jnp.int32),
                pltpu.SMEM((4 * prefix_len.shape[0],), jnp.int32),
            ],
        ),
        out_shape=[
            jax.ShapeDtypeStruct((requests, PAD, LANES), jnp.float32),
            jax.ShapeDtypeStruct((requests, PAD, LANES), jnp.float32),
        ],
        compiler_params=pltpu.CompilerParams(dimension_semantics=("arbitrary",)),
    )(group_ids, prefix_len, suffix_len, offset, query_pad, key_cache, value_cache)
    width = tj * LANES
    packed = jnp.concatenate(
        [
            o_out[:, :tj, :].reshape(requests, width),
            stat_out[:, :tj, : 2 * kv_local].reshape(requests, tj * 2 * kv_local),
        ],
        axis=1,
    )
    packed = lax.all_to_all(packed, "seq", split_axis=0, concat_axis=0, tiled=True)
    sums = packed[:, :width].reshape(requests, tj, kv_local, HD)
    stats = packed[:, width:].reshape(requests, tj, kv_local, 2)
    maxes = stats[..., 0]
    totals = stats[..., 1]
    own_max = jnp.max(maxes, axis=0)
    rescale = jnp.exp(maxes - own_max[None])
    own_total = jnp.sum(totals * rescale, axis=0)
    own_summed = jnp.sum(sums * rescale[..., None], axis=0)
    mine = lax.axis_index("seq")
    own_query = lax.dynamic_slice_in_dim(queries, mine * NEW, NEW, 0)
    own_query = own_query.reshape(NEW, kv_local, repeat, HD).transpose(0, 2, 1, 3)
    own_query = own_query.reshape(tj, kv_local, HD)
    keys_new = new_keys.reshape(NEW, kv_local, HD)
    values_new = new_values.reshape(NEW, kv_local, HD)
    token_of = jnp.arange(tj) // repeat
    causal = (token_of[:, None] >= jnp.arange(NEW)[None, :])[:, None, :]
    score_new = (
        jnp.einsum("qgd,ugd->qgu", own_query, keys_new, preferred_element_type=jnp.float32)
        * 0.125
    )
    joined = jnp.maximum(own_max, jnp.max(jnp.where(causal, score_new, fill_score), axis=-1))
    expo_new = jnp.where(causal, jnp.exp(score_new - joined[..., None]), 0.0)
    factor_own = jnp.exp(own_max - joined)
    denominator = own_total * factor_own + jnp.sum(expo_new, axis=-1)
    numerator = own_summed * factor_own[..., None] + jnp.einsum(
        "qgu,ugd->qgd",
        expo_new.astype(jnp.bfloat16),
        values_new,
        preferred_element_type=jnp.float32,
    )
    mixed = (numerator / denominator[..., None]).astype(jnp.bfloat16)
    mixed = mixed.reshape(NEW, repeat, kv_local, HD).transpose(0, 2, 1, 3)
    mixed = mixed.reshape(NEW, heads_local * HD)
    partial_out = jnp.dot(mixed, out_weight, preferred_element_type=jnp.float32)
    parts = lax.axis_size("tp")
    piece = partial_out.shape[1] // parts
    pieces = partial_out.reshape(NEW, parts, piece)
    me = lax.axis_index("tp")
    result = lax.dynamic_index_in_dim(pieces, me, 1, keepdims=False)
    for shift in range(1, parts):
        sent = lax.dynamic_index_in_dim(pieces, (me + shift) % parts, 1, keepdims=False)
        pairs = [(i, (i + shift) % parts) for i in range(parts)]
        result = result + lax.ppermute(sent, "tp", pairs)
    return result.astype(jnp.bfloat16)


def solution(mesh):
    placed = (
        P(None, "tp"),
        P("seq", "tp"),
        P("seq", "tp"),
        P("seq", "tp"),
        P("seq", "tp"),
        P("tp", None),
        P(),
        P(),
        P(),
    )
    return jax.shard_map(
        per_device, mesh=mesh, in_specs=placed, out_specs=P("seq", "tp"), check_vma=False
    )
```

```python
import jax
import jax.numpy as jnp
from jax import lax
from jax.experimental import pallas as pl
from jax.experimental.pallas import tpu as pltpu
from jax.sharding import PartitionSpec as P

HD = 64
NEW = 5
STEP = 1024
SPAN = 17
GROUP_MAX = 16
OWNERS = 2
CHUNKS = 8
PAD = 16
LANES = 128


fill_score = -1e30


def segment_starts(group_ids, prefix_len, suffix_len):
    groups = jnp.arange(prefix_len.shape[0], dtype=jnp.int32)
    prefix_excl = jnp.cumsum(prefix_len) - prefix_len
    suffix_excl = jnp.cumsum(suffix_len) - suffix_len
    earlier = group_ids[None, :] < groups[:, None]
    prompt_start = prefix_excl + jnp.sum(jnp.where(earlier, suffix_len[None, :], 0), axis=1)
    member = group_ids[:, None] == groups[None, :]
    req_prompt_start = jnp.sum(jnp.where(member, prompt_start[None, :], 0), axis=1)
    req_prompt_len = jnp.sum(jnp.where(member, prefix_len[None, :], 0), axis=1)
    prefix_incl = jnp.sum(jnp.where(member, (prefix_excl + prefix_len)[None, :], 0), axis=1)
    own_start = prefix_incl + suffix_excl
    return (req_prompt_start, req_prompt_len, own_start)


def attend_window(turn, low, span, masked, q_ref, bound_ref, k_ref, v_ref, o_ref, stat_ref):
    rows = span * PAD
    keys = k_ref[...]
    vals = v_ref[...]
    bound = bound_ref[pl.ds(low, span)].reshape(rows, LANES)
    if masked:
        places = turn * STEP + lax.broadcasted_iota(jnp.int32, (1, STEP), 1)
        mask = ((places >= bound[:, 0:1]) & (places < bound[:, 1:2])) | (
            (places >= bound[:, 2:3]) & (places < bound[:, 3:4])
        )
    else:
        first = turn * STEP
        keep = (bound[:, 0:1] <= first) & (bound[:, 1:2] >= first + STEP)
    stat = stat_ref[pl.ds(low, span)].reshape(rows, LANES)
    o_old = o_ref[pl.ds(low, span)].reshape(rows, LANES)
    lane = lax.broadcasted_iota(jnp.int32, (rows, LANES), 1)
    first_half = lane < HD
    o_new = None
    stat_new = jnp.zeros((rows, LANES), jnp.float32)
    for g in range(2):
        query = q_ref[g, pl.ds(low, span)].reshape(rows, LANES) * jnp.asarray(0.125, q_ref.dtype)
        score = lax.dot_general(
            query, keys, (((1,), (1,)), ((), ())), preferred_element_type=jnp.float32
        )
        if masked:
            score = jnp.where(mask, score, fill_score)
        m_old = stat[:, 2 * g : 2 * g + 1]
        l_old = stat[:, 2 * g + 1 : 2 * g + 2]
        m_new = jnp.maximum(m_old, jnp.max(score, axis=1, keepdims=True))
        expo = jnp.exp(score - m_new)
        alpha = jnp.exp(m_old - m_new)
        l_new = alpha * l_old + jnp.sum(expo, axis=1, keepdims=True)
        mixed = jnp.dot(expo.astype(jnp.bfloat16), vals, preferred_element_type=jnp.float32)
        if g == 0:
            o_new = jnp.where(first_half, o_old * alpha + mixed, 0.0)
        else:
            o_new = jnp.where(first_half, o_new, o_old * alpha + mixed)
        stat_new = jnp.where(lane == 2 * g, m_new, stat_new)
        stat_new = jnp.where(lane == 2 * g + 1, l_new, stat_new)
    if not masked:
        o_new = jnp.where(keep, o_new, o_old)
        stat_new = jnp.where(keep, stat_new, stat)
    o_ref[pl.ds(low, span)] = o_new.reshape(span, PAD, LANES)
    stat_ref[pl.ds(low, span)] = stat_new.reshape(span, PAD, LANES)


def attend_kernel(
    gid_ref, pre_ref, suf_ref, off_ref, q_ref, k_ref, v_ref, o_ref, stat_ref, edge_ref, bound_ref,
    chunk_ref, table_ref,
):
    turn = pl.program_id(0)
    requests = q_ref.shape[1]
    groups = pre_ref.shape[0]
    refs = (q_ref, bound_ref, k_ref, v_ref, o_ref, stat_ref)

    @pl.when(turn == 0)
    def _():
        o_ref[...] = jnp.zeros(o_ref.shape, jnp.float32)
        lane3 = lax.broadcasted_iota(jnp.int32, stat_ref.shape, 2)
        stat_ref[...] = jnp.where(lane3 % 2 == 0, fill_score, 0.0).astype(jnp.float32)
        offset = off_ref[0]
        for gg in range(groups):
            table_ref[3 * groups + gg] = 0
        for t in range(CHUNKS + 2):
            chunk_ref[3 * CHUNKS + t] = 0

        def sums(r, run):
            g = gid_ref[r]
            s = suf_ref[r]
            edge_ref[r] = run
            table_ref[3 * groups + g] = table_ref[3 * groups + g] + s
            return run + s

        lax.fori_loop(0, requests, sums, jnp.int32(0), unroll=8)
        prefix_excl = jnp.int32(0)
        earlier = jnp.int32(0)
        starts = []
        ends = []
        for gg in range(groups):
            start = prefix_excl + earlier - offset
            starts.append(start)
            ends.append(start + pre_ref[gg])
            table_ref[gg] = start
            table_ref[groups + gg] = start + pre_ref[gg]
            table_ref[2 * groups + gg] = prefix_excl + pre_ref[gg] - offset
            earlier = earlier + table_ref[3 * groups + gg]
            prefix_excl = prefix_excl + pre_ref[gg]
        for t in range(CHUNKS):
            begin = t * STEP
            inside = jnp.int32(0)
            touch = jnp.int32(0)
            for gg in range(groups):
                hold = (starts[gg] <= begin) & (ends[gg] >= begin + STEP)
                meet = (starts[gg] < begin + STEP) & (ends[gg] > begin)
                inside = jnp.maximum(inside, jnp.where(hold, 1, 0))
                touch = jnp.maximum(touch, jnp.where(meet, 1, 0))
            chunk_ref[CHUNKS + t] = inside
            chunk_ref[2 * CHUNKS + t] = touch
        lane = lax.broadcasted_iota(jnp.int32, (PAD, LANES), 1)

        def edges(r, c):
            g = gid_ref[r]
            ps = table_ref[g]
            pe = table_ref[groups + g]
            os_ = table_ref[2 * groups + g] + edge_ref[r]
            oe = os_ + suf_ref[r]
            bound_ref[r] = jnp.where(
                lane == 0, ps, jnp.where(lane == 1, pe, jnp.where(lane == 2, os_, oe))
            )
            bucket = jnp.clip(jnp.right_shift(oe + (STEP - 1), STEP.bit_length() - 1), 0, CHUNKS + 1)
            chunk_ref[3 * CHUNKS + bucket] = chunk_ref[3 * CHUNKS + bucket] + 1
            return c

        lax.fori_loop(0, requests, edges, 0, unroll=8)
        count = jnp.int32(0)
        for t in range(CHUNKS):
            count = count + chunk_ref[3 * CHUNKS + t]
            chunk_ref[t] = count

    first = chunk_ref[turn]
    inside = chunk_ref[CHUNKS + turn]
    touch = chunk_ref[2 * CHUNKS + turn]

    @pl.when((inside == 0) & (touch == 1))
    def _():
        span = min(SPAN, requests)
        attend_window(turn, jnp.minimum(first, requests - span), span, True, *refs)

    @pl.when(inside == 1)
    def _():
        span = min(GROUP_MAX, requests)
        attend_window(turn, jnp.minimum(first, requests - span), span, False, *refs)

    @pl.when((inside == 0) & (touch == 0))
    def _():
        span = min(OWNERS, requests)
        attend_window(turn, jnp.minimum(first, requests - span), span, True, *refs)


def per_device(
    queries,
    new_keys,
    new_values,
    key_cache,
    value_cache,
    out_weight,
    group_ids,
    prefix_len,
    suffix_len,
):
    rows = queries.shape[0]
    heads_local = queries.shape[1] // HD
    kv_local = key_cache.shape[1] // HD
    repeat = heads_local // kv_local
    requests = rows // NEW
    block = key_cache.shape[0]
    span = min(SPAN, requests)
    tj = NEW * repeat
    steps = block // STEP
    assert steps == CHUNKS
    offset = jnp.full((1,), lax.axis_index("seq") * block, jnp.int32)
    scaled = queries.reshape(requests, NEW, kv_local, repeat, HD)
    scaled = scaled.transpose(2, 0, 1, 3, 4).reshape(kv_local, requests, tj, HD)
    query_pad = jnp.stack(
        [
            jnp.pad(scaled[g], ((0, 0), (0, PAD - tj), (g * HD, LANES - (g + 1) * HD)))
            for g in range(kv_local)
        ]
    )
    full = lambda shape: pl.BlockSpec(shape, lambda t, *_: (0,) * len(shape))
    o_out, stat_out = pl.pallas_call(
        attend_kernel,
        grid_spec=pltpu.PrefetchScalarGridSpec(
            num_scalar_prefetch=4,
            grid=(steps,),
            in_specs=[
                full((kv_local, requests, PAD, LANES)),
                pl.BlockSpec((STEP, LANES), lambda t, *_: (t, 0)),
                pl.BlockSpec((STEP, LANES), lambda t, *_: (t, 0)),
            ],
            out_specs=[full((requests, PAD, LANES)), full((requests, PAD, LANES))],
            scratch_shapes=[
                pltpu.SMEM((requests,), jnp.int32),
                pltpu.VMEM((requests, PAD, LANES), jnp.int32),
                pltpu.SMEM((4 * steps + 2,), jnp.int32),
                pltpu.SMEM((4 * prefix_len.shape[0],), jnp.int32),
            ],
        ),
        out_shape=[
            jax.ShapeDtypeStruct((requests, PAD, LANES), jnp.float32),
            jax.ShapeDtypeStruct((requests, PAD, LANES), jnp.float32),
        ],
        compiler_params=pltpu.CompilerParams(dimension_semantics=("arbitrary",)),
    )(group_ids, prefix_len, suffix_len, offset, query_pad, key_cache, value_cache)
    small = stat_out[:, :tj, : 2 * kv_local].reshape(requests, tj * 2 * kv_local)
    small = jnp.pad(small, ((0, 0), (0, LANES - tj * 2 * kv_local)))
    packed = o_out.at[:, PAD - 1, :].set(small)
    packed = lax.all_to_all(packed, "seq", split_axis=0, concat_axis=0, tiled=True)
    sums = packed[:, :tj, :].reshape(requests, tj, kv_local, HD)
    stats = packed[:, PAD - 1, : tj * 2 * kv_local].reshape(requests, tj, kv_local, 2)
    maxes = stats[..., 0]
    totals = stats[..., 1]
    own_max = jnp.max(maxes, axis=0)
    rescale = jnp.exp(maxes - own_max[None])
    own_total = jnp.sum(totals * rescale, axis=0)
    own_summed = jnp.sum(sums * rescale[..., None], axis=0)
    mine = lax.axis_index("seq")
    own_query = lax.dynamic_slice_in_dim(queries, mine * NEW, NEW, 0)
    own_query = own_query.reshape(NEW, kv_local, repeat, HD).transpose(0, 2, 1, 3)
    own_query = own_query.reshape(tj, kv_local, HD)
    keys_new = new_keys.reshape(NEW, kv_local, HD)
    values_new = new_values.reshape(NEW, kv_local, HD)
    token_of = jnp.arange(tj) // repeat
    causal = (token_of[:, None] >= jnp.arange(NEW)[None, :])[:, None, :]
    score_new = (
        jnp.einsum("qgd,ugd->qgu", own_query, keys_new, preferred_element_type=jnp.float32)
        * 0.125
    )
    joined = jnp.maximum(own_max, jnp.max(jnp.where(causal, score_new, fill_score), axis=-1))
    expo_new = jnp.where(causal, jnp.exp(score_new - joined[..., None]), 0.0)
    factor_own = jnp.exp(own_max - joined)
    denominator = own_total * factor_own + jnp.sum(expo_new, axis=-1)
    numerator = own_summed * factor_own[..., None] + jnp.einsum(
        "qgu,ugd->qgd",
        expo_new.astype(jnp.bfloat16),
        values_new,
        preferred_element_type=jnp.float32,
    )
    mixed = (numerator / denominator[..., None]).astype(jnp.bfloat16)
    mixed = mixed.reshape(NEW, repeat, kv_local, HD).transpose(0, 2, 1, 3)
    mixed = mixed.reshape(NEW, heads_local * HD)
    partial_out = jnp.dot(mixed, out_weight, preferred_element_type=jnp.float32)
    parts = lax.axis_size("tp")
    piece = partial_out.shape[1] // parts
    pieces = partial_out.reshape(NEW, parts, piece)
    me = lax.axis_index("tp")
    result = lax.dynamic_index_in_dim(pieces, me, 1, keepdims=False)
    for shift in range(1, parts):
        sent = lax.dynamic_index_in_dim(pieces, (me + shift) % parts, 1, keepdims=False)
        pairs = [(i, (i + shift) % parts) for i in range(parts)]
        result = result + lax.ppermute(sent, "tp", pairs)
    return result.astype(jnp.bfloat16)


def solution(mesh):
    placed = (
        P(None, "tp"),
        P("seq", "tp"),
        P("seq", "tp"),
        P("seq", "tp"),
        P("seq", "tp"),
        P("tp", None),
        P(),
        P(),
        P(),
    )
    return jax.shard_map(
        per_device, mesh=mesh, in_specs=placed, out_specs=P("seq", "tp"), check_vma=False
    )
```

```python
import jax
import jax.numpy as jnp
from jax import lax
from jax.experimental import pallas as pl
from jax.experimental.pallas import tpu as pltpu
from jax.sharding import PartitionSpec as P

HD = 64
NEW = 5
STEP = 1024
SPAN = 17
GROUP_MAX = 16
OWNERS = 2
CHUNKS = 8
PAD = 16
LANES = 128


fill_score = -1e30


def segment_starts(group_ids, prefix_len, suffix_len):
    groups = jnp.arange(prefix_len.shape[0], dtype=jnp.int32)
    prefix_excl = jnp.cumsum(prefix_len) - prefix_len
    suffix_excl = jnp.cumsum(suffix_len) - suffix_len
    earlier = group_ids[None, :] < groups[:, None]
    prompt_start = prefix_excl + jnp.sum(jnp.where(earlier, suffix_len[None, :], 0), axis=1)
    member = group_ids[:, None] == groups[None, :]
    req_prompt_start = jnp.sum(jnp.where(member, prompt_start[None, :], 0), axis=1)
    req_prompt_len = jnp.sum(jnp.where(member, prefix_len[None, :], 0), axis=1)
    prefix_incl = jnp.sum(jnp.where(member, (prefix_excl + prefix_len)[None, :], 0), axis=1)
    own_start = prefix_incl + suffix_excl
    return (req_prompt_start, req_prompt_len, own_start)


def attend_window(turn, low, span, masked, q_ref, bound_ref, k_ref, v_ref, o_ref, stat_ref):
    rows = span * PAD
    keys = k_ref[...]
    vals = v_ref[...]
    bound = bound_ref[pl.ds(low, span)].reshape(rows, LANES)
    if masked:
        places = turn * STEP + lax.broadcasted_iota(jnp.int32, (1, STEP), 1)
        mask = ((places >= bound[:, 0:1]) & (places < bound[:, 1:2])) | (
            (places >= bound[:, 2:3]) & (places < bound[:, 3:4])
        )
    else:
        first = turn * STEP
        keep = (bound[:, 0:1] <= first) & (bound[:, 1:2] >= first + STEP)
    stat = stat_ref[pl.ds(low, span)].reshape(rows, LANES)
    o_old = o_ref[pl.ds(low, span)].reshape(rows, LANES)
    lane = lax.broadcasted_iota(jnp.int32, (rows, LANES), 1)
    first_half = lane < HD
    o_new = None
    stat_new = jnp.zeros((rows, LANES), jnp.float32)
    for g in range(2):
        query = q_ref[g, pl.ds(low, span)].reshape(rows, LANES)
        score = lax.dot_general(
            query, keys, (((1,), (1,)), ((), ())), preferred_element_type=jnp.float32
        )
        if masked:
            score = jnp.where(mask, score, fill_score)
        m_old = stat[:, 2 * g : 2 * g + 1]
        l_old = stat[:, 2 * g + 1 : 2 * g + 2]
        m_new = jnp.maximum(m_old, jnp.max(score, axis=1, keepdims=True))
        expo = jnp.exp(score - m_new)
        alpha = jnp.exp(m_old - m_new)
        l_new = alpha * l_old + jnp.sum(expo, axis=1, keepdims=True)
        mixed = jnp.dot(expo.astype(jnp.bfloat16), vals, preferred_element_type=jnp.float32)
        if g == 0:
            o_new = jnp.where(first_half, o_old * alpha + mixed, 0.0)
        else:
            o_new = jnp.where(first_half, o_new, o_old * alpha + mixed)
        stat_new = jnp.where(lane == 2 * g, m_new, stat_new)
        stat_new = jnp.where(lane == 2 * g + 1, l_new, stat_new)
    if not masked:
        o_new = jnp.where(keep, o_new, o_old)
        stat_new = jnp.where(keep, stat_new, stat)
    o_ref[pl.ds(low, span)] = o_new.reshape(span, PAD, LANES)
    stat_ref[pl.ds(low, span)] = stat_new.reshape(span, PAD, LANES)


def attend_kernel(
    gid_ref, pre_ref, suf_ref, off_ref, q_ref, k_ref, v_ref, o_ref, stat_ref, edge_ref, bound_ref,
    chunk_ref, table_ref,
):
    turn = pl.program_id(0)
    requests = q_ref.shape[1]
    groups = pre_ref.shape[0]
    refs = (q_ref, bound_ref, k_ref, v_ref, o_ref, stat_ref)

    @pl.when(turn == 0)
    def _():
        o_ref[...] = jnp.zeros(o_ref.shape, jnp.float32)
        lane3 = lax.broadcasted_iota(jnp.int32, stat_ref.shape, 2)
        stat_ref[...] = jnp.where(lane3 % 2 == 0, fill_score, 0.0).astype(jnp.float32)
        offset = off_ref[0]
        for gg in range(groups):
            table_ref[3 * groups + gg] = 0
        for t in range(CHUNKS + 2):
            chunk_ref[3 * CHUNKS + t] = 0

        def sums(r, run):
            g = gid_ref[r]
            s = suf_ref[r]
            edge_ref[r] = run
            table_ref[3 * groups + g] = table_ref[3 * groups + g] + s
            return run + s

        lax.fori_loop(0, requests, sums, jnp.int32(0), unroll=8)
        prefix_excl = jnp.int32(0)
        earlier = jnp.int32(0)
        starts = []
        ends = []
        for gg in range(groups):
            start = prefix_excl + earlier - offset
            starts.append(start)
            ends.append(start + pre_ref[gg])
            table_ref[gg] = start
            table_ref[groups + gg] = start + pre_ref[gg]
            table_ref[2 * groups + gg] = prefix_excl + pre_ref[gg] - offset
            earlier = earlier + table_ref[3 * groups + gg]
            prefix_excl = prefix_excl + pre_ref[gg]
        for t in range(CHUNKS):
            begin = t * STEP
            inside = jnp.int32(0)
            touch = jnp.int32(0)
            for gg in range(groups):
                hold = (starts[gg] <= begin) & (ends[gg] >= begin + STEP)
                meet = (starts[gg] < begin + STEP) & (ends[gg] > begin)
                inside = jnp.maximum(inside, jnp.where(hold, 1, 0))
                touch = jnp.maximum(touch, jnp.where(meet, 1, 0))
            chunk_ref[CHUNKS + t] = inside
            chunk_ref[2 * CHUNKS + t] = touch
        lane = lax.broadcasted_iota(jnp.int32, (PAD, LANES), 1)

        def edges(r, c):
            g = gid_ref[r]
            ps = table_ref[g]
            pe = table_ref[groups + g]
            os_ = table_ref[2 * groups + g] + edge_ref[r]
            oe = os_ + suf_ref[r]
            bound_ref[r] = jnp.where(
                lane == 0, ps, jnp.where(lane == 1, pe, jnp.where(lane == 2, os_, oe))
            )
            bucket = jnp.clip(jnp.right_shift(oe + (STEP - 1), STEP.bit_length() - 1), 0, CHUNKS + 1)
            chunk_ref[3 * CHUNKS + bucket] = chunk_ref[3 * CHUNKS + bucket] + 1
            return c

        lax.fori_loop(0, requests, edges, 0, unroll=8)
        count = jnp.int32(0)
        for t in range(CHUNKS):
            count = count + chunk_ref[3 * CHUNKS + t]
            chunk_ref[t] = count

    first = chunk_ref[turn]
    inside = chunk_ref[CHUNKS + turn]
    touch = chunk_ref[2 * CHUNKS + turn]

    @pl.when((inside == 0) & (touch == 1))
    def _():
        span = min(SPAN, requests)
        attend_window(turn, jnp.minimum(first, requests - span), span, True, *refs)

    @pl.when(inside == 1)
    def _():
        span = min(GROUP_MAX, requests)
        attend_window(turn, jnp.minimum(first, requests - span), span, False, *refs)

    @pl.when((inside == 0) & (touch == 0))
    def _():
        span = min(OWNERS, requests)
        attend_window(turn, jnp.minimum(first, requests - span), span, True, *refs)


def per_device(
    queries,
    new_keys,
    new_values,
    key_cache,
    value_cache,
    out_weight,
    group_ids,
    prefix_len,
    suffix_len,
):
    rows = queries.shape[0]
    heads_local = queries.shape[1] // HD
    kv_local = key_cache.shape[1] // HD
    repeat = heads_local // kv_local
    requests = rows // NEW
    block = key_cache.shape[0]
    span = min(SPAN, requests)
    tj = NEW * repeat
    steps = block // STEP
    assert steps == CHUNKS
    offset = jnp.full((1,), lax.axis_index("seq") * block, jnp.int32)
    scaled = (queries * jnp.asarray(0.125, queries.dtype)).reshape(requests, NEW, kv_local, repeat, HD)
    scaled = scaled.transpose(2, 0, 1, 3, 4).reshape(kv_local, requests, tj, HD)
    query_pad = jnp.stack(
        [
            jnp.pad(scaled[g], ((0, 0), (0, PAD - tj), (g * HD, LANES - (g + 1) * HD)))
            for g in range(kv_local)
        ]
    )
    full = lambda shape: pl.BlockSpec(shape, lambda t, *_: (0,) * len(shape))
    o_out, stat_out = pl.pallas_call(
        attend_kernel,
        grid_spec=pltpu.PrefetchScalarGridSpec(
            num_scalar_prefetch=4,
            grid=(steps,),
            in_specs=[
                full((kv_local, requests, PAD, LANES)),
                pl.BlockSpec((STEP, LANES), lambda t, *_: (t, 0)),
                pl.BlockSpec((STEP, LANES), lambda t, *_: (t, 0)),
            ],
            out_specs=[full((requests, PAD, LANES)), full((requests, PAD, LANES))],
            scratch_shapes=[
                pltpu.SMEM((requests,), jnp.int32),
                pltpu.VMEM((requests, PAD, LANES), jnp.int32),
                pltpu.SMEM((4 * steps + 2,), jnp.int32),
                pltpu.SMEM((4 * prefix_len.shape[0],), jnp.int32),
            ],
        ),
        out_shape=[
            jax.ShapeDtypeStruct((requests, PAD, LANES), jnp.float32),
            jax.ShapeDtypeStruct((requests, PAD, LANES), jnp.float32),
        ],
        compiler_params=pltpu.CompilerParams(dimension_semantics=("arbitrary",)),
    )(group_ids, prefix_len, suffix_len, offset, query_pad, key_cache, value_cache)
    width = tj * LANES
    packed = jnp.concatenate(
        [
            o_out[:, :tj, :].reshape(requests, width),
            stat_out[:, :tj, : 2 * kv_local].reshape(requests, tj * 2 * kv_local),
        ],
        axis=1,
    )
    packed = lax.all_to_all(packed, "seq", split_axis=0, concat_axis=0, tiled=True)
    sums = packed[:, :width].reshape(requests, tj, kv_local, HD)
    stats = packed[:, width:].reshape(requests, tj, kv_local, 2)
    maxes = stats[..., 0]
    totals = stats[..., 1]
    own_max = jnp.max(maxes, axis=0)
    rescale = jnp.exp(maxes - own_max[None])
    own_total = jnp.sum(totals * rescale, axis=0)
    own_summed = jnp.sum(sums * rescale[..., None], axis=0)
    mine = lax.axis_index("seq")
    own_query = lax.dynamic_slice_in_dim(queries, mine * NEW, NEW, 0)
    own_query = own_query.reshape(NEW, kv_local, repeat, HD).transpose(0, 2, 1, 3)
    own_query = own_query.reshape(tj, kv_local, HD)
    keys_new = new_keys.reshape(NEW, kv_local, HD)
    values_new = new_values.reshape(NEW, kv_local, HD)
    token_of = jnp.arange(tj) // repeat
    causal = (token_of[:, None] >= jnp.arange(NEW)[None, :])[:, None, :]
    score_new = (
        jnp.einsum("qgd,ugd->qgu", own_query, keys_new, preferred_element_type=jnp.float32)
        * 0.125
    )
    joined = jnp.maximum(own_max, jnp.max(jnp.where(causal, score_new, fill_score), axis=-1))
    expo_new = jnp.where(causal, jnp.exp(score_new - joined[..., None]), 0.0)
    factor_own = jnp.exp(own_max - joined)
    denominator = own_total * factor_own + jnp.sum(expo_new, axis=-1)
    numerator = own_summed * factor_own[..., None] + jnp.einsum(
        "qgu,ugd->qgd",
        expo_new.astype(jnp.bfloat16),
        values_new,
        preferred_element_type=jnp.float32,
    )
    mixed = (numerator / denominator[..., None]).astype(jnp.bfloat16)
    mixed = mixed.reshape(NEW, repeat, kv_local, HD).transpose(0, 2, 1, 3)
    mixed = mixed.reshape(NEW, heads_local * HD)
    partial_out = jnp.dot(mixed, out_weight, preferred_element_type=jnp.float32)
    parts = lax.axis_size("tp")
    piece = partial_out.shape[1] // parts
    pieces = partial_out.reshape(NEW, parts, piece).transpose(1, 0, 2)
    pieces = lax.all_to_all(pieces, "tp", split_axis=0, concat_axis=0, tiled=True)
    result = jnp.sum(pieces, axis=0)
    return result.astype(jnp.bfloat16)


def solution(mesh):
    placed = (
        P(None, "tp"),
        P("seq", "tp"),
        P("seq", "tp"),
        P("seq", "tp"),
        P("seq", "tp"),
        P("tp", None),
        P(),
        P(),
        P(),
    )
    return jax.shard_map(
        per_device, mesh=mesh, in_specs=placed, out_specs=P("seq", "tp"), check_vma=False
    )
```

```python
import jax
import jax.numpy as jnp
from jax import lax
from jax.experimental import pallas as pl
from jax.experimental.pallas import tpu as pltpu
from jax.sharding import PartitionSpec as P

HD = 64
NEW = 5
STEP = 1024
SPAN = 17
GROUP_MAX = 16
OWNERS = 2
CHUNKS = 8
PAD = 16
LANES = 128


fill_score = -1e30


def segment_starts(group_ids, prefix_len, suffix_len):
    groups = jnp.arange(prefix_len.shape[0], dtype=jnp.int32)
    prefix_excl = jnp.cumsum(prefix_len) - prefix_len
    suffix_excl = jnp.cumsum(suffix_len) - suffix_len
    earlier = group_ids[None, :] < groups[:, None]
    prompt_start = prefix_excl + jnp.sum(jnp.where(earlier, suffix_len[None, :], 0), axis=1)
    member = group_ids[:, None] == groups[None, :]
    req_prompt_start = jnp.sum(jnp.where(member, prompt_start[None, :], 0), axis=1)
    req_prompt_len = jnp.sum(jnp.where(member, prefix_len[None, :], 0), axis=1)
    prefix_incl = jnp.sum(jnp.where(member, (prefix_excl + prefix_len)[None, :], 0), axis=1)
    own_start = prefix_incl + suffix_excl
    return (req_prompt_start, req_prompt_len, own_start)


def attend_window(turn, low, span, masked, q_ref, bound_ref, k_ref, v_ref, o_ref, stat_ref):
    rows = span * PAD
    keys = k_ref[...]
    vals = v_ref[...]
    bound = bound_ref[pl.ds(low, span)].reshape(rows, LANES)
    if masked:
        places = turn * STEP + lax.broadcasted_iota(jnp.int32, (1, STEP), 1)
        mask = ((places >= bound[:, 0:1]) & (places < bound[:, 1:2])) | (
            (places >= bound[:, 2:3]) & (places < bound[:, 3:4])
        )
    else:
        first = turn * STEP
        keep = (bound[:, 0:1] <= first) & (bound[:, 1:2] >= first + STEP)
    stat = stat_ref[pl.ds(low, span)].reshape(rows, LANES)
    o_old = o_ref[pl.ds(low, span)].reshape(rows, LANES)
    lane = lax.broadcasted_iota(jnp.int32, (rows, LANES), 1)
    first_half = lane < HD
    o_new = None
    stat_new = jnp.zeros((rows, LANES), jnp.float32)
    for g in range(2):
        query = q_ref[g, pl.ds(low, span)].reshape(rows, LANES)
        score = lax.dot_general(
            query, keys, (((1,), (1,)), ((), ())), preferred_element_type=jnp.float32
        )
        if masked:
            score = jnp.where(mask, score, fill_score)
        m_old = stat[:, 2 * g : 2 * g + 1]
        l_old = stat[:, 2 * g + 1 : 2 * g + 2]
        m_new = jnp.maximum(m_old, jnp.max(score, axis=1, keepdims=True))
        expo = jnp.exp(score - m_new)
        alpha = jnp.exp(m_old - m_new)
        l_new = alpha * l_old + jnp.sum(expo, axis=1, keepdims=True)
        mixed = jnp.dot(expo.astype(jnp.bfloat16), vals, preferred_element_type=jnp.float32)
        if g == 0:
            o_new = jnp.where(first_half, o_old * alpha + mixed, 0.0)
        else:
            o_new = jnp.where(first_half, o_new, o_old * alpha + mixed)
        stat_new = jnp.where(lane == 2 * g, m_new, stat_new)
        stat_new = jnp.where(lane == 2 * g + 1, l_new, stat_new)
    if not masked:
        o_new = jnp.where(keep, o_new, o_old)
        stat_new = jnp.where(keep, stat_new, stat)
    o_ref[pl.ds(low, span)] = o_new.reshape(span, PAD, LANES)
    stat_ref[pl.ds(low, span)] = stat_new.reshape(span, PAD, LANES)


def attend_kernel(
    gid_ref, pre_ref, suf_ref, off_ref, q_ref, k_ref, v_ref, o_ref, stat_ref, edge_ref, bound_ref,
    chunk_ref, table_ref,
):
    turn = pl.program_id(0)
    requests = q_ref.shape[1]
    groups = pre_ref.shape[0]
    refs = (q_ref, bound_ref, k_ref, v_ref, o_ref, stat_ref)

    @pl.when(turn == 0)
    def _():
        o_ref[...] = jnp.zeros(o_ref.shape, jnp.float32)
        lane3 = lax.broadcasted_iota(jnp.int32, stat_ref.shape, 2)
        stat_ref[...] = jnp.where(lane3 % 2 == 0, fill_score, 0.0).astype(jnp.float32)
        offset = off_ref[0]
        for gg in range(groups):
            table_ref[3 * groups + gg] = 0
        for t in range(CHUNKS + 2):
            chunk_ref[3 * CHUNKS + t] = 0

        def sums(r, run):
            g = gid_ref[r]
            s = suf_ref[r]
            edge_ref[r] = run
            table_ref[3 * groups + g] = table_ref[3 * groups + g] + s
            return run + s

        lax.fori_loop(0, requests, sums, jnp.int32(0), unroll=8)
        prefix_excl = jnp.int32(0)
        earlier = jnp.int32(0)
        starts = []
        ends = []
        for gg in range(groups):
            start = prefix_excl + earlier - offset
            starts.append(start)
            ends.append(start + pre_ref[gg])
            table_ref[gg] = start
            table_ref[groups + gg] = start + pre_ref[gg]
            table_ref[2 * groups + gg] = prefix_excl + pre_ref[gg] - offset
            earlier = earlier + table_ref[3 * groups + gg]
            prefix_excl = prefix_excl + pre_ref[gg]
        for t in range(CHUNKS):
            begin = t * STEP
            inside = jnp.int32(0)
            touch = jnp.int32(0)
            for gg in range(groups):
                hold = (starts[gg] <= begin) & (ends[gg] >= begin + STEP)
                meet = (starts[gg] < begin + STEP) & (ends[gg] > begin)
                inside = jnp.maximum(inside, jnp.where(hold, 1, 0))
                touch = jnp.maximum(touch, jnp.where(meet, 1, 0))
            chunk_ref[CHUNKS + t] = inside
            chunk_ref[2 * CHUNKS + t] = touch
        lane = lax.broadcasted_iota(jnp.int32, (PAD, LANES), 1)

        def edges(r, c):
            g = gid_ref[r]
            ps = table_ref[g]
            pe = table_ref[groups + g]
            os_ = table_ref[2 * groups + g] + edge_ref[r]
            oe = os_ + suf_ref[r]
            bound_ref[r] = jnp.where(
                lane == 0, ps, jnp.where(lane == 1, pe, jnp.where(lane == 2, os_, oe))
            )
            bucket = jnp.clip(jnp.right_shift(oe + (STEP - 1), STEP.bit_length() - 1), 0, CHUNKS + 1)
            chunk_ref[3 * CHUNKS + bucket] = chunk_ref[3 * CHUNKS + bucket] + 1
            return c

        lax.fori_loop(0, requests, edges, 0, unroll=8)
        count = jnp.int32(0)
        for t in range(CHUNKS):
            count = count + chunk_ref[3 * CHUNKS + t]
            chunk_ref[t] = count

    first = chunk_ref[turn]
    inside = chunk_ref[CHUNKS + turn]
    touch = chunk_ref[2 * CHUNKS + turn]

    @pl.when((inside == 0) & (touch == 1))
    def _():
        span = min(SPAN, requests)
        attend_window(turn, jnp.minimum(first, requests - span), span, True, *refs)

    @pl.when(inside == 1)
    def _():
        span = min(GROUP_MAX, requests)
        attend_window(turn, jnp.minimum(first, requests - span), span, False, *refs)

    @pl.when((inside == 0) & (touch == 0))
    def _():
        span = min(OWNERS, requests)
        attend_window(turn, jnp.minimum(first, requests - span), span, True, *refs)


def per_device(
    queries,
    new_keys,
    new_values,
    key_cache,
    value_cache,
    out_weight,
    group_ids,
    prefix_len,
    suffix_len,
):
    rows = queries.shape[0]
    heads_local = queries.shape[1] // HD
    kv_local = key_cache.shape[1] // HD
    repeat = heads_local // kv_local
    requests = rows // NEW
    block = key_cache.shape[0]
    span = min(SPAN, requests)
    tj = NEW * repeat
    steps = block // STEP
    assert steps == CHUNKS
    offset = jnp.full((1,), lax.axis_index("seq") * block, jnp.int32)
    scaled = (queries * jnp.asarray(0.125, queries.dtype)).reshape(requests, NEW, kv_local, repeat, HD)
    scaled = scaled.transpose(2, 0, 1, 3, 4).reshape(kv_local, requests, tj, HD)
    query_pad = jnp.stack(
        [
            jnp.pad(scaled[g], ((0, 0), (0, PAD - tj), (g * HD, LANES - (g + 1) * HD)))
            for g in range(kv_local)
        ]
    )
    full = lambda shape: pl.BlockSpec(shape, lambda t, *_: (0,) * len(shape))
    o_out, stat_out = pl.pallas_call(
        attend_kernel,
        grid_spec=pltpu.PrefetchScalarGridSpec(
            num_scalar_prefetch=4,
            grid=(steps,),
            in_specs=[
                full((kv_local, requests, PAD, LANES)),
                pl.BlockSpec((STEP, LANES), lambda t, *_: (t, 0)),
                pl.BlockSpec((STEP, LANES), lambda t, *_: (t, 0)),
            ],
            out_specs=[full((requests, PAD, LANES)), full((requests, PAD, LANES))],
            scratch_shapes=[
                pltpu.SMEM((requests,), jnp.int32),
                pltpu.VMEM((requests, PAD, LANES), jnp.int32),
                pltpu.SMEM((4 * steps + 2,), jnp.int32),
                pltpu.SMEM((4 * prefix_len.shape[0],), jnp.int32),
            ],
        ),
        out_shape=[
            jax.ShapeDtypeStruct((requests, PAD, LANES), jnp.float32),
            jax.ShapeDtypeStruct((requests, PAD, LANES), jnp.float32),
        ],
        compiler_params=pltpu.CompilerParams(dimension_semantics=("arbitrary",)),
    )(group_ids, prefix_len, suffix_len, offset, query_pad, key_cache, value_cache)
    width = tj * LANES
    packed = jnp.concatenate(
        [
            o_out[:, :tj, :].reshape(requests, width),
            stat_out[:, :tj, : 2 * kv_local].reshape(requests, tj * 2 * kv_local),
        ],
        axis=1,
    )
    packed = lax.all_to_all(packed, "seq", split_axis=0, concat_axis=0, tiled=True)
    sums = packed[:, :width].reshape(requests, tj, kv_local, HD)
    stats = packed[:, width:].reshape(requests, tj, kv_local, 2)
    maxes = stats[..., 0]
    totals = stats[..., 1]
    own_max = jnp.max(maxes, axis=0)
    rescale = jnp.exp(maxes - own_max[None])
    own_total = jnp.sum(totals * rescale, axis=0)
    own_summed = jnp.sum(sums * rescale[..., None], axis=0)
    mine = lax.axis_index("seq")
    own_query = lax.dynamic_slice_in_dim(queries, mine * NEW, NEW, 0)
    own_query = own_query.reshape(NEW, kv_local, repeat, HD).transpose(0, 2, 1, 3)
    own_query = own_query.reshape(tj, kv_local, HD)
    keys_new = new_keys.reshape(NEW, kv_local, HD)
    values_new = new_values.reshape(NEW, kv_local, HD)
    token_of = jnp.arange(tj) // repeat
    causal = (token_of[:, None] >= jnp.arange(NEW)[None, :])[:, None, :]
    score_new = (
        jnp.einsum("qgd,ugd->qgu", own_query, keys_new, preferred_element_type=jnp.float32)
        * 0.125
    )
    joined = jnp.maximum(own_max, jnp.max(jnp.where(causal, score_new, fill_score), axis=-1))
    expo_new = jnp.where(causal, jnp.exp(score_new - joined[..., None]), 0.0)
    factor_own = jnp.exp(own_max - joined)
    denominator = own_total * factor_own + jnp.sum(expo_new, axis=-1)
    numerator = own_summed * factor_own[..., None] + jnp.einsum(
        "qgu,ugd->qgd",
        expo_new.astype(jnp.bfloat16),
        values_new,
        preferred_element_type=jnp.float32,
    )
    mixed = (numerator / denominator[..., None]).astype(jnp.bfloat16)
    mixed = mixed.reshape(NEW, repeat, kv_local, HD).transpose(0, 2, 1, 3)
    mixed = mixed.reshape(NEW, heads_local * HD)
    partial_out = jnp.dot(mixed, out_weight, preferred_element_type=jnp.float32)
    parts = lax.axis_size("tp")
    me = lax.axis_index("tp")
    result = partial_out
    half = parts // 2
    while half >= 1:
        width = result.shape[1] // 2
        mine_high = (me // half) % 2
        halves = result.reshape(NEW, 2, width)
        kept = lax.dynamic_index_in_dim(halves, mine_high, 1, keepdims=False)
        sent = lax.dynamic_index_in_dim(halves, 1 - mine_high, 1, keepdims=False)
        pairs = [(i, i ^ half) for i in range(parts)]
        result = kept + lax.ppermute(sent, "tp", pairs)
        half //= 2
    return result.astype(jnp.bfloat16)


def solution(mesh):
    placed = (
        P(None, "tp"),
        P("seq", "tp"),
        P("seq", "tp"),
        P("seq", "tp"),
        P("seq", "tp"),
        P("tp", None),
        P(),
        P(),
        P(),
    )
    return jax.shard_map(
        per_device, mesh=mesh, in_specs=placed, out_specs=P("seq", "tp"), check_vma=False
    )
```

```python
import jax
import jax.numpy as jnp
from jax import lax
from jax.experimental import pallas as pl
from jax.experimental.pallas import tpu as pltpu
from jax.sharding import PartitionSpec as P

HD = 64
NEW = 5
STEP = 1024
SPAN = 17
GROUP_MAX = 16
OWNERS = 2
CHUNKS = 8
PAD = 16
LANES = 128


fill_score = -1e30


def segment_starts(group_ids, prefix_len, suffix_len):
    groups = jnp.arange(prefix_len.shape[0], dtype=jnp.int32)
    prefix_excl = jnp.cumsum(prefix_len) - prefix_len
    suffix_excl = jnp.cumsum(suffix_len) - suffix_len
    earlier = group_ids[None, :] < groups[:, None]
    prompt_start = prefix_excl + jnp.sum(jnp.where(earlier, suffix_len[None, :], 0), axis=1)
    member = group_ids[:, None] == groups[None, :]
    req_prompt_start = jnp.sum(jnp.where(member, prompt_start[None, :], 0), axis=1)
    req_prompt_len = jnp.sum(jnp.where(member, prefix_len[None, :], 0), axis=1)
    prefix_incl = jnp.sum(jnp.where(member, (prefix_excl + prefix_len)[None, :], 0), axis=1)
    own_start = prefix_incl + suffix_excl
    return (req_prompt_start, req_prompt_len, own_start)


def attend_window(turn, low, span, masked, q_ref, bound_ref, k_ref, v_ref, o_ref, stat_ref):
    rows = span * PAD
    keys = k_ref[...]
    vals = v_ref[...]
    bound = bound_ref[pl.ds(low, span)].reshape(rows, LANES)
    if masked:
        begin = turn * STEP
        prompt_hit = (bound[:, 0:1] < begin + STEP) & (bound[:, 1:2] > begin)
        own_hit = (bound[:, 2:3] < begin + STEP) & (bound[:, 3:4] > begin)
        any_hit = prompt_hit | own_hit
        lo = jnp.where(any_hit, jnp.where(prompt_hit, bound[:, 0:1], bound[:, 2:3]), 0)
        hi = jnp.where(any_hit, jnp.where(own_hit, bound[:, 3:4], bound[:, 1:2]), 0)
        places = begin + lax.broadcasted_iota(jnp.int32, (1, STEP), 1)
        mask = (places >= lo) & (places < hi)
    else:
        first = turn * STEP
        keep = (bound[:, 0:1] <= first) & (bound[:, 1:2] >= first + STEP)
    stat = stat_ref[pl.ds(low, span)].reshape(rows, LANES)
    o_old = o_ref[pl.ds(low, span)].reshape(rows, LANES)
    lane = lax.broadcasted_iota(jnp.int32, (rows, LANES), 1)
    first_half = lane < HD
    o_new = None
    stat_new = jnp.zeros((rows, LANES), jnp.float32)
    for g in range(2):
        query = q_ref[g, pl.ds(low, span)].reshape(rows, LANES)
        score = lax.dot_general(
            query, keys, (((1,), (1,)), ((), ())), preferred_element_type=jnp.float32
        )
        if masked:
            score = jnp.where(mask, score, fill_score)
        m_old = stat[:, 2 * g : 2 * g + 1]
        l_old = stat[:, 2 * g + 1 : 2 * g + 2]
        m_new = jnp.maximum(m_old, jnp.max(score, axis=1, keepdims=True))
        expo = jnp.exp(score - m_new)
        alpha = jnp.exp(m_old - m_new)
        l_new = alpha * l_old + jnp.sum(expo, axis=1, keepdims=True)
        mixed = jnp.dot(expo.astype(jnp.bfloat16), vals, preferred_element_type=jnp.float32)
        if g == 0:
            o_new = jnp.where(first_half, o_old * alpha + mixed, 0.0)
        else:
            o_new = jnp.where(first_half, o_new, o_old * alpha + mixed)
        stat_new = jnp.where(lane == 2 * g, m_new, stat_new)
        stat_new = jnp.where(lane == 2 * g + 1, l_new, stat_new)
    if not masked:
        o_new = jnp.where(keep, o_new, o_old)
        stat_new = jnp.where(keep, stat_new, stat)
    o_ref[pl.ds(low, span)] = o_new.reshape(span, PAD, LANES)
    stat_ref[pl.ds(low, span)] = stat_new.reshape(span, PAD, LANES)


def attend_kernel(
    gid_ref, pre_ref, suf_ref, off_ref, q_ref, k_ref, v_ref, o_ref, stat_ref, edge_ref, bound_ref,
    chunk_ref, table_ref,
):
    turn = pl.program_id(0)
    requests = q_ref.shape[1]
    groups = pre_ref.shape[0]
    refs = (q_ref, bound_ref, k_ref, v_ref, o_ref, stat_ref)

    @pl.when(turn == 0)
    def _():
        o_ref[...] = jnp.zeros(o_ref.shape, jnp.float32)
        lane3 = lax.broadcasted_iota(jnp.int32, stat_ref.shape, 2)
        stat_ref[...] = jnp.where(lane3 % 2 == 0, fill_score, 0.0).astype(jnp.float32)
        offset = off_ref[0]
        for gg in range(groups):
            table_ref[3 * groups + gg] = 0
        for t in range(CHUNKS + 2):
            chunk_ref[3 * CHUNKS + t] = 0

        def sums(r, run):
            g = gid_ref[r]
            s = suf_ref[r]
            edge_ref[r] = run
            table_ref[3 * groups + g] = table_ref[3 * groups + g] + s
            return run + s

        lax.fori_loop(0, requests, sums, jnp.int32(0), unroll=8)
        prefix_excl = jnp.int32(0)
        earlier = jnp.int32(0)
        starts = []
        ends = []
        for gg in range(groups):
            start = prefix_excl + earlier - offset
            starts.append(start)
            ends.append(start + pre_ref[gg])
            table_ref[gg] = start
            table_ref[groups + gg] = start + pre_ref[gg]
            table_ref[2 * groups + gg] = prefix_excl + pre_ref[gg] - offset
            earlier = earlier + table_ref[3 * groups + gg]
            prefix_excl = prefix_excl + pre_ref[gg]
        for t in range(CHUNKS):
            begin = t * STEP
            inside = jnp.int32(0)
            touch = jnp.int32(0)
            for gg in range(groups):
                hold = (starts[gg] <= begin) & (ends[gg] >= begin + STEP)
                meet = (starts[gg] < begin + STEP) & (ends[gg] > begin)
                inside = jnp.maximum(inside, jnp.where(hold, 1, 0))
                touch = jnp.maximum(touch, jnp.where(meet, 1, 0))
            chunk_ref[CHUNKS + t] = inside
            chunk_ref[2 * CHUNKS + t] = touch
        lane = lax.broadcasted_iota(jnp.int32, (PAD, LANES), 1)

        def edges(r, c):
            g = gid_ref[r]
            ps = table_ref[g]
            pe = table_ref[groups + g]
            os_ = table_ref[2 * groups + g] + edge_ref[r]
            oe = os_ + suf_ref[r]
            bound_ref[r] = jnp.where(
                lane == 0, ps, jnp.where(lane == 1, pe, jnp.where(lane == 2, os_, oe))
            )
            bucket = jnp.clip(jnp.right_shift(oe + (STEP - 1), STEP.bit_length() - 1), 0, CHUNKS + 1)
            chunk_ref[3 * CHUNKS + bucket] = chunk_ref[3 * CHUNKS + bucket] + 1
            return c

        lax.fori_loop(0, requests, edges, 0, unroll=8)
        count = jnp.int32(0)
        for t in range(CHUNKS):
            count = count + chunk_ref[3 * CHUNKS + t]
            chunk_ref[t] = count

    first = chunk_ref[turn]
    inside = chunk_ref[CHUNKS + turn]
    touch = chunk_ref[2 * CHUNKS + turn]

    @pl.when((inside == 0) & (touch == 1))
    def _():
        span = min(SPAN, requests)
        attend_window(turn, jnp.minimum(first, requests - span), span, True, *refs)

    @pl.when(inside == 1)
    def _():
        span = min(GROUP_MAX, requests)
        attend_window(turn, jnp.minimum(first, requests - span), span, False, *refs)

    @pl.when((inside == 0) & (touch == 0))
    def _():
        span = min(OWNERS, requests)
        attend_window(turn, jnp.minimum(first, requests - span), span, True, *refs)


def per_device(
    queries,
    new_keys,
    new_values,
    key_cache,
    value_cache,
    out_weight,
    group_ids,
    prefix_len,
    suffix_len,
):
    rows = queries.shape[0]
    heads_local = queries.shape[1] // HD
    kv_local = key_cache.shape[1] // HD
    repeat = heads_local // kv_local
    requests = rows // NEW
    block = key_cache.shape[0]
    span = min(SPAN, requests)
    tj = NEW * repeat
    steps = block // STEP
    assert steps == CHUNKS
    offset = jnp.full((1,), lax.axis_index("seq") * block, jnp.int32)
    scaled = (queries * jnp.asarray(0.125, queries.dtype)).reshape(requests, NEW, kv_local, repeat, HD)
    scaled = scaled.transpose(2, 0, 1, 3, 4).reshape(kv_local, requests, tj, HD)
    query_pad = jnp.stack(
        [
            jnp.pad(scaled[g], ((0, 0), (0, PAD - tj), (g * HD, LANES - (g + 1) * HD)))
            for g in range(kv_local)
        ]
    )
    full = lambda shape: pl.BlockSpec(shape, lambda t, *_: (0,) * len(shape))
    o_out, stat_out = pl.pallas_call(
        attend_kernel,
        grid_spec=pltpu.PrefetchScalarGridSpec(
            num_scalar_prefetch=4,
            grid=(steps,),
            in_specs=[
                full((kv_local, requests, PAD, LANES)),
                pl.BlockSpec((STEP, LANES), lambda t, *_: (t, 0)),
                pl.BlockSpec((STEP, LANES), lambda t, *_: (t, 0)),
            ],
            out_specs=[full((requests, PAD, LANES)), full((requests, PAD, LANES))],
            scratch_shapes=[
                pltpu.SMEM((requests,), jnp.int32),
                pltpu.VMEM((requests, PAD, LANES), jnp.int32),
                pltpu.SMEM((4 * steps + 2,), jnp.int32),
                pltpu.SMEM((4 * prefix_len.shape[0],), jnp.int32),
            ],
        ),
        out_shape=[
            jax.ShapeDtypeStruct((requests, PAD, LANES), jnp.float32),
            jax.ShapeDtypeStruct((requests, PAD, LANES), jnp.float32),
        ],
        compiler_params=pltpu.CompilerParams(dimension_semantics=("arbitrary",)),
    )(group_ids, prefix_len, suffix_len, offset, query_pad, key_cache, value_cache)
    width = tj * LANES
    packed = jnp.concatenate(
        [
            o_out[:, :tj, :].reshape(requests, width),
            stat_out[:, :tj, : 2 * kv_local].reshape(requests, tj * 2 * kv_local),
        ],
        axis=1,
    )
    packed = lax.all_to_all(packed, "seq", split_axis=0, concat_axis=0, tiled=True)
    sums = packed[:, :width].reshape(requests, tj, kv_local, HD)
    stats = packed[:, width:].reshape(requests, tj, kv_local, 2)
    maxes = stats[..., 0]
    totals = stats[..., 1]
    own_max = jnp.max(maxes, axis=0)
    rescale = jnp.exp(maxes - own_max[None])
    own_total = jnp.sum(totals * rescale, axis=0)
    own_summed = jnp.sum(sums * rescale[..., None], axis=0)
    mine = lax.axis_index("seq")
    own_query = lax.dynamic_slice_in_dim(queries, mine * NEW, NEW, 0)
    own_query = own_query.reshape(NEW, kv_local, repeat, HD).transpose(0, 2, 1, 3)
    own_query = own_query.reshape(tj, kv_local, HD)
    keys_new = new_keys.reshape(NEW, kv_local, HD)
    values_new = new_values.reshape(NEW, kv_local, HD)
    token_of = jnp.arange(tj) // repeat
    causal = (token_of[:, None] >= jnp.arange(NEW)[None, :])[:, None, :]
    score_new = (
        jnp.einsum("qgd,ugd->qgu", own_query, keys_new, preferred_element_type=jnp.float32)
        * 0.125
    )
    joined = jnp.maximum(own_max, jnp.max(jnp.where(causal, score_new, fill_score), axis=-1))
    expo_new = jnp.where(causal, jnp.exp(score_new - joined[..., None]), 0.0)
    factor_own = jnp.exp(own_max - joined)
    denominator = own_total * factor_own + jnp.sum(expo_new, axis=-1)
    numerator = own_summed * factor_own[..., None] + jnp.einsum(
        "qgu,ugd->qgd",
        expo_new.astype(jnp.bfloat16),
        values_new,
        preferred_element_type=jnp.float32,
    )
    mixed = (numerator / denominator[..., None]).astype(jnp.bfloat16)
    mixed = mixed.reshape(NEW, repeat, kv_local, HD).transpose(0, 2, 1, 3)
    mixed = mixed.reshape(NEW, heads_local * HD)
    partial_out = jnp.dot(mixed, out_weight, preferred_element_type=jnp.float32)
    parts = lax.axis_size("tp")
    piece = partial_out.shape[1] // parts
    pieces = partial_out.reshape(NEW, parts, piece)
    me = lax.axis_index("tp")
    result = lax.dynamic_index_in_dim(pieces, me, 1, keepdims=False)
    for shift in range(1, parts):
        sent = lax.dynamic_index_in_dim(pieces, (me + shift) % parts, 1, keepdims=False)
        pairs = [(i, (i + shift) % parts) for i in range(parts)]
        result = result + lax.ppermute(sent, "tp", pairs)
    return result.astype(jnp.bfloat16)


def solution(mesh):
    placed = (
        P(None, "tp"),
        P("seq", "tp"),
        P("seq", "tp"),
        P("seq", "tp"),
        P("seq", "tp"),
        P("tp", None),
        P(),
        P(),
        P(),
    )
    return jax.shard_map(
        per_device, mesh=mesh, in_specs=placed, out_specs=P("seq", "tp"), check_vma=False
    )
```

```python
import jax
import jax.numpy as jnp
from jax import lax
from jax.experimental import pallas as pl
from jax.experimental.pallas import tpu as pltpu
from jax.sharding import PartitionSpec as P

HD = 64
NEW = 5
STEP = 1024
SPAN = 17
GROUP_SPANS = (8, 12, 16)
OWNERS = 2
CHUNKS = 8
PAD = 16
LANES = 128


fill_score = -1e30


def segment_starts(group_ids, prefix_len, suffix_len):
    groups = jnp.arange(prefix_len.shape[0], dtype=jnp.int32)
    prefix_excl = jnp.cumsum(prefix_len) - prefix_len
    suffix_excl = jnp.cumsum(suffix_len) - suffix_len
    earlier = group_ids[None, :] < groups[:, None]
    prompt_start = prefix_excl + jnp.sum(jnp.where(earlier, suffix_len[None, :], 0), axis=1)
    member = group_ids[:, None] == groups[None, :]
    req_prompt_start = jnp.sum(jnp.where(member, prompt_start[None, :], 0), axis=1)
    req_prompt_len = jnp.sum(jnp.where(member, prefix_len[None, :], 0), axis=1)
    prefix_incl = jnp.sum(jnp.where(member, (prefix_excl + prefix_len)[None, :], 0), axis=1)
    own_start = prefix_incl + suffix_excl
    return (req_prompt_start, req_prompt_len, own_start)


def attend_window(turn, low, span, masked, q_ref, bound_ref, k_ref, v_ref, o_ref, stat_ref):
    rows = span * PAD
    keys = k_ref[...]
    vals = v_ref[...]
    bound = bound_ref[pl.ds(low, span)].reshape(rows, LANES)
    if masked:
        begin = turn * STEP
        prompt_hit = (bound[:, 0:1] < begin + STEP) & (bound[:, 1:2] > begin)
        own_hit = (bound[:, 2:3] < begin + STEP) & (bound[:, 3:4] > begin)
        any_hit = prompt_hit | own_hit
        lo = jnp.where(any_hit, jnp.where(prompt_hit, bound[:, 0:1], bound[:, 2:3]), 0)
        hi = jnp.where(any_hit, jnp.where(own_hit, bound[:, 3:4], bound[:, 1:2]), 0)
        places = begin + lax.broadcasted_iota(jnp.int32, (1, STEP), 1)
        mask = (places >= lo) & (places < hi)
    else:
        first = turn * STEP
        keep = (bound[:, 0:1] <= first) & (bound[:, 1:2] >= first + STEP)
    stat = stat_ref[pl.ds(low, span)].reshape(rows, LANES)
    o_old = o_ref[pl.ds(low, span)].reshape(rows, LANES)
    lane = lax.broadcasted_iota(jnp.int32, (rows, LANES), 1)
    first_half = lane < HD
    o_new = None
    stat_new = jnp.zeros((rows, LANES), jnp.float32)
    for g in range(2):
        query = q_ref[g, pl.ds(low, span)].reshape(rows, LANES)
        score = lax.dot_general(
            query, keys, (((1,), (1,)), ((), ())), preferred_element_type=jnp.float32
        )
        if masked:
            score = jnp.where(mask, score, fill_score)
        m_old = stat[:, 2 * g : 2 * g + 1]
        l_old = stat[:, 2 * g + 1 : 2 * g + 2]
        m_new = jnp.maximum(m_old, jnp.max(score, axis=1, keepdims=True))
        expo = jnp.exp(score - m_new)
        alpha = jnp.exp(m_old - m_new)
        l_new = alpha * l_old + jnp.sum(expo, axis=1, keepdims=True)
        mixed = jnp.dot(expo.astype(jnp.bfloat16), vals, preferred_element_type=jnp.float32)
        if g == 0:
            o_new = jnp.where(first_half, o_old * alpha + mixed, 0.0)
        else:
            o_new = jnp.where(first_half, o_new, o_old * alpha + mixed)
        stat_new = jnp.where(lane == 2 * g, m_new, stat_new)
        stat_new = jnp.where(lane == 2 * g + 1, l_new, stat_new)
    if not masked:
        o_new = jnp.where(keep, o_new, o_old)
        stat_new = jnp.where(keep, stat_new, stat)
    o_ref[pl.ds(low, span)] = o_new.reshape(span, PAD, LANES)
    stat_ref[pl.ds(low, span)] = stat_new.reshape(span, PAD, LANES)


def attend_kernel(
    gid_ref, pre_ref, suf_ref, off_ref, q_ref, k_ref, v_ref, o_ref, stat_ref, edge_ref, bound_ref,
    chunk_ref, table_ref,
):
    turn = pl.program_id(0)
    requests = q_ref.shape[1]
    groups = pre_ref.shape[0]
    refs = (q_ref, bound_ref, k_ref, v_ref, o_ref, stat_ref)

    @pl.when(turn == 0)
    def _():
        o_ref[...] = jnp.zeros(o_ref.shape, jnp.float32)
        lane3 = lax.broadcasted_iota(jnp.int32, stat_ref.shape, 2)
        stat_ref[...] = jnp.where(lane3 % 2 == 0, fill_score, 0.0).astype(jnp.float32)
        offset = off_ref[0]
        for gg in range(groups):
            table_ref[3 * groups + gg] = 0
            table_ref[4 * groups + gg] = 0
        for t in range(CHUNKS + 2):
            chunk_ref[3 * CHUNKS + t] = 0

        def sums(r, run):
            g = gid_ref[r]
            s = suf_ref[r]
            edge_ref[r] = run
            table_ref[3 * groups + g] = table_ref[3 * groups + g] + s
            table_ref[4 * groups + g] = table_ref[4 * groups + g] + 1
            return run + s

        lax.fori_loop(0, requests, sums, jnp.int32(0), unroll=8)
        prefix_excl = jnp.int32(0)
        earlier = jnp.int32(0)
        starts = []
        ends = []
        for gg in range(groups):
            start = prefix_excl + earlier - offset
            starts.append(start)
            ends.append(start + pre_ref[gg])
            table_ref[gg] = start
            table_ref[groups + gg] = start + pre_ref[gg]
            table_ref[2 * groups + gg] = prefix_excl + pre_ref[gg] - offset
            earlier = earlier + table_ref[3 * groups + gg]
            prefix_excl = prefix_excl + pre_ref[gg]
        for t in range(CHUNKS):
            begin = t * STEP
            inside = jnp.int32(0)
            touch = jnp.int32(0)
            members = jnp.int32(0)
            for gg in range(groups):
                hold = (starts[gg] <= begin) & (ends[gg] >= begin + STEP)
                meet = (starts[gg] < begin + STEP) & (ends[gg] > begin)
                inside = jnp.maximum(inside, jnp.where(hold, 1, 0))
                touch = jnp.maximum(touch, jnp.where(meet, 1, 0))
                members = jnp.maximum(members, jnp.where(hold, table_ref[4 * groups + gg], 0))
            chunk_ref[CHUNKS + t] = inside
            chunk_ref[4 * CHUNKS + 2 + t] = members
            chunk_ref[2 * CHUNKS + t] = touch
        lane = lax.broadcasted_iota(jnp.int32, (PAD, LANES), 1)

        def edges(r, c):
            g = gid_ref[r]
            ps = table_ref[g]
            pe = table_ref[groups + g]
            os_ = table_ref[2 * groups + g] + edge_ref[r]
            oe = os_ + suf_ref[r]
            bound_ref[r] = jnp.where(
                lane == 0, ps, jnp.where(lane == 1, pe, jnp.where(lane == 2, os_, oe))
            )
            bucket = jnp.clip(jnp.right_shift(oe + (STEP - 1), STEP.bit_length() - 1), 0, CHUNKS + 1)
            chunk_ref[3 * CHUNKS + bucket] = chunk_ref[3 * CHUNKS + bucket] + 1
            return c

        lax.fori_loop(0, requests, edges, 0, unroll=8)
        count = jnp.int32(0)
        for t in range(CHUNKS):
            count = count + chunk_ref[3 * CHUNKS + t]
            chunk_ref[t] = count

    first = chunk_ref[turn]
    inside = chunk_ref[CHUNKS + turn]
    touch = chunk_ref[2 * CHUNKS + turn]

    @pl.when((inside == 0) & (touch == 1))
    def _():
        span = min(SPAN, requests)
        attend_window(turn, jnp.minimum(first, requests - span), span, True, *refs)

    members = chunk_ref[4 * CHUNKS + 2 + turn]
    lower = 0
    for size in GROUP_SPANS:
        span = min(size, requests)

        @pl.when((inside == 1) & (members > lower) & ((members <= size) | (size == GROUP_SPANS[-1])))
        def _():
            attend_window(turn, jnp.minimum(first, requests - span), span, False, *refs)

        lower = size

    @pl.when((inside == 0) & (touch == 0))
    def _():
        span = min(OWNERS, requests)
        attend_window(turn, jnp.minimum(first, requests - span), span, True, *refs)


def per_device(
    queries,
    new_keys,
    new_values,
    key_cache,
    value_cache,
    out_weight,
    group_ids,
    prefix_len,
    suffix_len,
):
    rows = queries.shape[0]
    heads_local = queries.shape[1] // HD
    kv_local = key_cache.shape[1] // HD
    repeat = heads_local // kv_local
    requests = rows // NEW
    block = key_cache.shape[0]
    span = min(SPAN, requests)
    tj = NEW * repeat
    steps = block // STEP
    assert steps == CHUNKS
    offset = jnp.full((1,), lax.axis_index("seq") * block, jnp.int32)
    scaled = (queries * jnp.asarray(0.125, queries.dtype)).reshape(requests, NEW, kv_local, repeat, HD)
    scaled = scaled.transpose(2, 0, 1, 3, 4).reshape(kv_local, requests, tj, HD)
    query_pad = jnp.stack(
        [
            jnp.pad(scaled[g], ((0, 0), (0, PAD - tj), (g * HD, LANES - (g + 1) * HD)))
            for g in range(kv_local)
        ]
    )
    full = lambda shape: pl.BlockSpec(shape, lambda t, *_: (0,) * len(shape))
    o_out, stat_out = pl.pallas_call(
        attend_kernel,
        grid_spec=pltpu.PrefetchScalarGridSpec(
            num_scalar_prefetch=4,
            grid=(steps,),
            in_specs=[
                full((kv_local, requests, PAD, LANES)),
                pl.BlockSpec((STEP, LANES), lambda t, *_: (t, 0)),
                pl.BlockSpec((STEP, LANES), lambda t, *_: (t, 0)),
            ],
            out_specs=[full((requests, PAD, LANES)), full((requests, PAD, LANES))],
            scratch_shapes=[
                pltpu.SMEM((requests,), jnp.int32),
                pltpu.VMEM((requests, PAD, LANES), jnp.int32),
                pltpu.SMEM((5 * steps + 2,), jnp.int32),
                pltpu.SMEM((5 * prefix_len.shape[0],), jnp.int32),
            ],
        ),
        out_shape=[
            jax.ShapeDtypeStruct((requests, PAD, LANES), jnp.float32),
            jax.ShapeDtypeStruct((requests, PAD, LANES), jnp.float32),
        ],
        compiler_params=pltpu.CompilerParams(dimension_semantics=("arbitrary",)),
    )(group_ids, prefix_len, suffix_len, offset, query_pad, key_cache, value_cache)
    width = tj * LANES
    packed = jnp.concatenate(
        [
            o_out[:, :tj, :].reshape(requests, width),
            stat_out[:, :tj, : 2 * kv_local].reshape(requests, tj * 2 * kv_local),
        ],
        axis=1,
    )
    packed = lax.all_to_all(packed, "seq", split_axis=0, concat_axis=0, tiled=True)
    sums = packed[:, :width].reshape(requests, tj, kv_local, HD)
    stats = packed[:, width:].reshape(requests, tj, kv_local, 2)
    maxes = stats[..., 0]
    totals = stats[..., 1]
    own_max = jnp.max(maxes, axis=0)
    rescale = jnp.exp(maxes - own_max[None])
    own_total = jnp.sum(totals * rescale, axis=0)
    own_summed = jnp.sum(sums * rescale[..., None], axis=0)
    mine = lax.axis_index("seq")
    own_query = lax.dynamic_slice_in_dim(queries, mine * NEW, NEW, 0)
    own_query = own_query.reshape(NEW, kv_local, repeat, HD).transpose(0, 2, 1, 3)
    own_query = own_query.reshape(tj, kv_local, HD)
    keys_new = new_keys.reshape(NEW, kv_local, HD)
    values_new = new_values.reshape(NEW, kv_local, HD)
    token_of = jnp.arange(tj) // repeat
    causal = (token_of[:, None] >= jnp.arange(NEW)[None, :])[:, None, :]
    score_new = (
        jnp.einsum("qgd,ugd->qgu", own_query, keys_new, preferred_element_type=jnp.float32)
        * 0.125
    )
    joined = jnp.maximum(own_max, jnp.max(jnp.where(causal, score_new, fill_score), axis=-1))
    expo_new = jnp.where(causal, jnp.exp(score_new - joined[..., None]), 0.0)
    factor_own = jnp.exp(own_max - joined)
    denominator = own_total * factor_own + jnp.sum(expo_new, axis=-1)
    numerator = own_summed * factor_own[..., None] + jnp.einsum(
        "qgu,ugd->qgd",
        expo_new.astype(jnp.bfloat16),
        values_new,
        preferred_element_type=jnp.float32,
    )
    mixed = (numerator / denominator[..., None]).astype(jnp.bfloat16)
    mixed = mixed.reshape(NEW, repeat, kv_local, HD).transpose(0, 2, 1, 3)
    mixed = mixed.reshape(NEW, heads_local * HD)
    partial_out = jnp.dot(mixed, out_weight, preferred_element_type=jnp.float32)
    parts = lax.axis_size("tp")
    piece = partial_out.shape[1] // parts
    pieces = partial_out.reshape(NEW, parts, piece)
    me = lax.axis_index("tp")
    result = lax.dynamic_index_in_dim(pieces, me, 1, keepdims=False)
    for shift in range(1, parts):
        sent = lax.dynamic_index_in_dim(pieces, (me + shift) % parts, 1, keepdims=False)
        pairs = [(i, (i + shift) % parts) for i in range(parts)]
        result = result + lax.ppermute(sent, "tp", pairs)
    return result.astype(jnp.bfloat16)


def solution(mesh):
    placed = (
        P(None, "tp"),
        P("seq", "tp"),
        P("seq", "tp"),
        P("seq", "tp"),
        P("seq", "tp"),
        P("tp", None),
        P(),
        P(),
        P(),
    )
    return jax.shard_map(
        per_device, mesh=mesh, in_specs=placed, out_specs=P("seq", "tp"), check_vma=False
    )
```

```python
import jax
import jax.numpy as jnp
from jax import lax
from jax.experimental import pallas as pl
from jax.experimental.pallas import tpu as pltpu
from jax.sharding import PartitionSpec as P

HD = 64
NEW = 5
STEP = 1024
SPAN = 17
GROUP_MAX = 16
OWNERS = 2
CHUNKS = 8
PAD = 16
LANES = 128


fill_score = -1e30


def segment_starts(group_ids, prefix_len, suffix_len):
    groups = jnp.arange(prefix_len.shape[0], dtype=jnp.int32)
    prefix_excl = jnp.cumsum(prefix_len) - prefix_len
    suffix_excl = jnp.cumsum(suffix_len) - suffix_len
    earlier = group_ids[None, :] < groups[:, None]
    prompt_start = prefix_excl + jnp.sum(jnp.where(earlier, suffix_len[None, :], 0), axis=1)
    member = group_ids[:, None] == groups[None, :]
    req_prompt_start = jnp.sum(jnp.where(member, prompt_start[None, :], 0), axis=1)
    req_prompt_len = jnp.sum(jnp.where(member, prefix_len[None, :], 0), axis=1)
    prefix_incl = jnp.sum(jnp.where(member, (prefix_excl + prefix_len)[None, :], 0), axis=1)
    own_start = prefix_incl + suffix_excl
    return (req_prompt_start, req_prompt_len, own_start)


def attend_window(
    turn, low, span, masked, q_ref, bound_ref, k_ref, v_ref, o_ref, stat_ref, s_scr, p_scr, red_scr, edge_scr
):
    rows = span * PAD
    keys = k_ref[...]
    vals = v_ref[...]
    bound = bound_ref[pl.ds(low, span)].reshape(rows, LANES)
    begin = turn * STEP
    lane = lax.broadcasted_iota(jnp.int32, (rows, LANES), 1)
    if masked:
        prompt_hit = (bound[:, 0:1] < begin + STEP) & (bound[:, 1:2] > begin)
        own_hit = (bound[:, 2:3] < begin + STEP) & (bound[:, 3:4] > begin)
        any_hit = prompt_hit | own_hit
        lo = jnp.where(any_hit, jnp.where(prompt_hit, bound[:, 0:1], bound[:, 2:3]), 0)
        hi = jnp.where(any_hit, jnp.where(own_hit, bound[:, 3:4], bound[:, 1:2]), 0)
        edge_scr[0:rows, :] = jnp.where(lane == 0, lo, hi)
    else:
        keep = (bound[:, 0:1] <= begin) & (bound[:, 1:2] >= begin + STEP)
    stat = stat_ref[pl.ds(low, span)].reshape(rows, LANES)
    o_old = o_ref[pl.ds(low, span)].reshape(rows, LANES)
    first_half = lane < HD
    for g in range(2):
        query = q_ref[g, pl.ds(low, span)].reshape(rows, LANES)
        s_scr[g * rows : (g + 1) * rows, :] = lax.dot_general(
            query, keys, (((1,), (1,)), ((), ())), preferred_element_type=jnp.float32
        )
    places = begin + lax.broadcasted_iota(jnp.int32, (1, STEP), 1)
    tile_lane = lax.broadcasted_iota(jnp.int32, (PAD, LANES), 1)

    def tile(t, carry):
        head = t // span
        at = pl.multiple_of(t * PAD, PAD)
        within = pl.multiple_of((t - head * span) * PAD, PAD)
        score = s_scr[pl.ds(at, PAD), :]
        if masked:
            edge = edge_scr[pl.ds(within, PAD), :]
            score = jnp.where((places >= edge[:, 0:1]) & (places < edge[:, 1:2]), score, fill_score)
        old = stat_ref[pl.ds(low + t - head * span, 1)].reshape(PAD, LANES)
        m_old = jnp.where(head == 0, old[:, 0:1], old[:, 2:3])
        m_new = jnp.maximum(m_old, jnp.max(score, axis=1, keepdims=True))
        expo = jnp.exp(score - m_new)
        p_scr[pl.ds(at, PAD), :] = expo.astype(jnp.bfloat16)
        part = jnp.sum(expo, axis=1, keepdims=True)
        red_scr[pl.ds(at, PAD), :] = jnp.where(tile_lane == 0, m_new, part)
        return carry

    lax.fori_loop(0, 2 * span, tile, 0)
    red = red_scr[0 : 2 * rows, :]
    m_new = red[:, 0:1]
    m_old = jnp.concatenate([stat[:, 0:1], stat[:, 2:3]], axis=0)
    l_old = jnp.concatenate([stat[:, 1:2], stat[:, 3:4]], axis=0)
    alpha = jnp.exp(m_old - m_new)
    l_new = alpha * l_old + red[:, 1:2]
    mixed = [
        jnp.dot(p_scr[g * rows : (g + 1) * rows, :], vals, preferred_element_type=jnp.float32)
        for g in range(2)
    ]
    o_new = jnp.where(
        first_half,
        o_old * alpha[:rows] + mixed[0],
        o_old * alpha[rows:] + mixed[1],
    )
    stat_new = jnp.where(lane == 0, m_new[:rows], 0.0)
    stat_new = jnp.where(lane == 1, l_new[:rows], stat_new)
    stat_new = jnp.where(lane == 2, m_new[rows:], stat_new)
    stat_new = jnp.where(lane == 3, l_new[rows:], stat_new)
    if not masked:
        o_new = jnp.where(keep, o_new, o_old)
        stat_new = jnp.where(keep, stat_new, stat)
    o_ref[pl.ds(low, span)] = o_new.reshape(span, PAD, LANES)
    stat_ref[pl.ds(low, span)] = stat_new.reshape(span, PAD, LANES)


def attend_kernel(
    gid_ref, pre_ref, suf_ref, off_ref, q_ref, k_ref, v_ref, o_ref, stat_ref, edge_ref, bound_ref,
    chunk_ref, table_ref, s_scr, p_scr, red_scr, edge_scr,
):
    turn = pl.program_id(0)
    requests = q_ref.shape[1]
    groups = pre_ref.shape[0]
    refs = (q_ref, bound_ref, k_ref, v_ref, o_ref, stat_ref, s_scr, p_scr, red_scr, edge_scr)

    @pl.when(turn == 0)
    def _():
        o_ref[...] = jnp.zeros(o_ref.shape, jnp.float32)
        lane3 = lax.broadcasted_iota(jnp.int32, stat_ref.shape, 2)
        stat_ref[...] = jnp.where(lane3 % 2 == 0, fill_score, 0.0).astype(jnp.float32)
        offset = off_ref[0]
        for gg in range(groups):
            table_ref[3 * groups + gg] = 0
        for t in range(CHUNKS + 2):
            chunk_ref[3 * CHUNKS + t] = 0

        def sums(r, run):
            g = gid_ref[r]
            s = suf_ref[r]
            edge_ref[r] = run
            table_ref[3 * groups + g] = table_ref[3 * groups + g] + s
            return run + s

        lax.fori_loop(0, requests, sums, jnp.int32(0), unroll=8)
        prefix_excl = jnp.int32(0)
        earlier = jnp.int32(0)
        starts = []
        ends = []
        for gg in range(groups):
            start = prefix_excl + earlier - offset
            starts.append(start)
            ends.append(start + pre_ref[gg])
            table_ref[gg] = start
            table_ref[groups + gg] = start + pre_ref[gg]
            table_ref[2 * groups + gg] = prefix_excl + pre_ref[gg] - offset
            earlier = earlier + table_ref[3 * groups + gg]
            prefix_excl = prefix_excl + pre_ref[gg]
        for t in range(CHUNKS):
            begin = t * STEP
            inside = jnp.int32(0)
            touch = jnp.int32(0)
            for gg in range(groups):
                hold = (starts[gg] <= begin) & (ends[gg] >= begin + STEP)
                meet = (starts[gg] < begin + STEP) & (ends[gg] > begin)
                inside = jnp.maximum(inside, jnp.where(hold, 1, 0))
                touch = jnp.maximum(touch, jnp.where(meet, 1, 0))
            chunk_ref[CHUNKS + t] = inside
            chunk_ref[2 * CHUNKS + t] = touch
        lane = lax.broadcasted_iota(jnp.int32, (PAD, LANES), 1)

        def edges(r, c):
            g = gid_ref[r]
            ps = table_ref[g]
            pe = table_ref[groups + g]
            os_ = table_ref[2 * groups + g] + edge_ref[r]
            oe = os_ + suf_ref[r]
            bound_ref[r] = jnp.where(
                lane == 0, ps, jnp.where(lane == 1, pe, jnp.where(lane == 2, os_, oe))
            )
            bucket = jnp.clip(jnp.right_shift(oe + (STEP - 1), STEP.bit_length() - 1), 0, CHUNKS + 1)
            chunk_ref[3 * CHUNKS + bucket] = chunk_ref[3 * CHUNKS + bucket] + 1
            return c

        lax.fori_loop(0, requests, edges, 0, unroll=8)
        count = jnp.int32(0)
        for t in range(CHUNKS):
            count = count + chunk_ref[3 * CHUNKS + t]
            chunk_ref[t] = count

    first = chunk_ref[turn]
    inside = chunk_ref[CHUNKS + turn]
    touch = chunk_ref[2 * CHUNKS + turn]

    @pl.when((inside == 0) & (touch == 1))
    def _():
        span = min(SPAN, requests)
        attend_window(turn, jnp.minimum(first, requests - span), span, True, *refs)

    @pl.when(inside == 1)
    def _():
        span = min(GROUP_MAX, requests)
        attend_window(turn, jnp.minimum(first, requests - span), span, False, *refs)

    @pl.when((inside == 0) & (touch == 0))
    def _():
        span = min(OWNERS, requests)
        attend_window(turn, jnp.minimum(first, requests - span), span, True, *refs)


def per_device(
    queries,
    new_keys,
    new_values,
    key_cache,
    value_cache,
    out_weight,
    group_ids,
    prefix_len,
    suffix_len,
):
    rows = queries.shape[0]
    heads_local = queries.shape[1] // HD
    kv_local = key_cache.shape[1] // HD
    repeat = heads_local // kv_local
    requests = rows // NEW
    block = key_cache.shape[0]
    span = min(SPAN, requests)
    tj = NEW * repeat
    steps = block // STEP
    assert steps == CHUNKS
    offset = jnp.full((1,), lax.axis_index("seq") * block, jnp.int32)
    scaled = (queries * jnp.asarray(0.125, queries.dtype)).reshape(requests, NEW, kv_local, repeat, HD)
    scaled = scaled.transpose(2, 0, 1, 3, 4).reshape(kv_local, requests, tj, HD)
    query_pad = jnp.stack(
        [
            jnp.pad(scaled[g], ((0, 0), (0, PAD - tj), (g * HD, LANES - (g + 1) * HD)))
            for g in range(kv_local)
        ]
    )
    full = lambda shape: pl.BlockSpec(shape, lambda t, *_: (0,) * len(shape))
    o_out, stat_out = pl.pallas_call(
        attend_kernel,
        grid_spec=pltpu.PrefetchScalarGridSpec(
            num_scalar_prefetch=4,
            grid=(steps,),
            in_specs=[
                full((kv_local, requests, PAD, LANES)),
                pl.BlockSpec((STEP, LANES), lambda t, *_: (t, 0)),
                pl.BlockSpec((STEP, LANES), lambda t, *_: (t, 0)),
            ],
            out_specs=[full((requests, PAD, LANES)), full((requests, PAD, LANES))],
            scratch_shapes=[
                pltpu.SMEM((requests,), jnp.int32),
                pltpu.VMEM((requests, PAD, LANES), jnp.int32),
                pltpu.SMEM((4 * steps + 2,), jnp.int32),
                pltpu.SMEM((4 * prefix_len.shape[0],), jnp.int32),
                pltpu.VMEM((2 * SPAN * PAD, STEP), jnp.float32),
                pltpu.VMEM((2 * SPAN * PAD, STEP), jnp.bfloat16),
                pltpu.VMEM((2 * SPAN * PAD, LANES), jnp.float32),
                pltpu.VMEM((SPAN * PAD, LANES), jnp.int32),
            ],
        ),
        out_shape=[
            jax.ShapeDtypeStruct((requests, PAD, LANES), jnp.float32),
            jax.ShapeDtypeStruct((requests, PAD, LANES), jnp.float32),
        ],
        compiler_params=pltpu.CompilerParams(dimension_semantics=("arbitrary",)),
    )(group_ids, prefix_len, suffix_len, offset, query_pad, key_cache, value_cache)
    width = tj * LANES
    packed = jnp.concatenate(
        [
            o_out[:, :tj, :].reshape(requests, width),
            stat_out[:, :tj, : 2 * kv_local].reshape(requests, tj * 2 * kv_local),
        ],
        axis=1,
    )
    packed = lax.all_to_all(packed, "seq", split_axis=0, concat_axis=0, tiled=True)
    sums = packed[:, :width].reshape(requests, tj, kv_local, HD)
    stats = packed[:, width:].reshape(requests, tj, kv_local, 2)
    maxes = stats[..., 0]
    totals = stats[..., 1]
    own_max = jnp.max(maxes, axis=0)
    rescale = jnp.exp(maxes - own_max[None])
    own_total = jnp.sum(totals * rescale, axis=0)
    own_summed = jnp.sum(sums * rescale[..., None], axis=0)
    mine = lax.axis_index("seq")
    own_query = lax.dynamic_slice_in_dim(queries, mine * NEW, NEW, 0)
    own_query = own_query.reshape(NEW, kv_local, repeat, HD).transpose(0, 2, 1, 3)
    own_query = own_query.reshape(tj, kv_local, HD)
    keys_new = new_keys.reshape(NEW, kv_local, HD)
    values_new = new_values.reshape(NEW, kv_local, HD)
    token_of = jnp.arange(tj) // repeat
    causal = (token_of[:, None] >= jnp.arange(NEW)[None, :])[:, None, :]
    score_new = (
        jnp.einsum("qgd,ugd->qgu", own_query, keys_new, preferred_element_type=jnp.float32)
        * 0.125
    )
    joined = jnp.maximum(own_max, jnp.max(jnp.where(causal, score_new, fill_score), axis=-1))
    expo_new = jnp.where(causal, jnp.exp(score_new - joined[..., None]), 0.0)
    factor_own = jnp.exp(own_max - joined)
    denominator = own_total * factor_own + jnp.sum(expo_new, axis=-1)
    numerator = own_summed * factor_own[..., None] + jnp.einsum(
        "qgu,ugd->qgd",
        expo_new.astype(jnp.bfloat16),
        values_new,
        preferred_element_type=jnp.float32,
    )
    mixed = (numerator / denominator[..., None]).astype(jnp.bfloat16)
    mixed = mixed.reshape(NEW, repeat, kv_local, HD).transpose(0, 2, 1, 3)
    mixed = mixed.reshape(NEW, heads_local * HD)
    partial_out = jnp.dot(mixed, out_weight, preferred_element_type=jnp.float32)
    parts = lax.axis_size("tp")
    piece = partial_out.shape[1] // parts
    pieces = partial_out.reshape(NEW, parts, piece)
    me = lax.axis_index("tp")
    result = lax.dynamic_index_in_dim(pieces, me, 1, keepdims=False)
    for shift in range(1, parts):
        sent = lax.dynamic_index_in_dim(pieces, (me + shift) % parts, 1, keepdims=False)
        pairs = [(i, (i + shift) % parts) for i in range(parts)]
        result = result + lax.ppermute(sent, "tp", pairs)
    return result.astype(jnp.bfloat16)


def solution(mesh):
    placed = (
        P(None, "tp"),
        P("seq", "tp"),
        P("seq", "tp"),
        P("seq", "tp"),
        P("seq", "tp"),
        P("tp", None),
        P(),
        P(),
        P(),
    )
    return jax.shard_map(
        per_device, mesh=mesh, in_specs=placed, out_specs=P("seq", "tp"), check_vma=False
    )
```

```python
import jax
import jax.numpy as jnp
from jax import lax
from jax.experimental import pallas as pl
from jax.experimental.pallas import tpu as pltpu
from jax.sharding import PartitionSpec as P

HD = 64
NEW = 5
STEP = 2048
SPAN = 18
GROUP_MAX = 16
OWNERS = 3
CHUNKS = 4
PAD = 16
LANES = 128


fill_score = -1e30


def segment_starts(group_ids, prefix_len, suffix_len):
    groups = jnp.arange(prefix_len.shape[0], dtype=jnp.int32)
    prefix_excl = jnp.cumsum(prefix_len) - prefix_len
    suffix_excl = jnp.cumsum(suffix_len) - suffix_len
    earlier = group_ids[None, :] < groups[:, None]
    prompt_start = prefix_excl + jnp.sum(jnp.where(earlier, suffix_len[None, :], 0), axis=1)
    member = group_ids[:, None] == groups[None, :]
    req_prompt_start = jnp.sum(jnp.where(member, prompt_start[None, :], 0), axis=1)
    req_prompt_len = jnp.sum(jnp.where(member, prefix_len[None, :], 0), axis=1)
    prefix_incl = jnp.sum(jnp.where(member, (prefix_excl + prefix_len)[None, :], 0), axis=1)
    own_start = prefix_incl + suffix_excl
    return (req_prompt_start, req_prompt_len, own_start)


def attend_window(turn, low, span, masked, q_ref, bound_ref, k_ref, v_ref, o_ref, stat_ref):
    rows = span * PAD
    keys = k_ref[...]
    vals = v_ref[...]
    bound = bound_ref[pl.ds(low, span)].reshape(rows, LANES)
    if masked:
        places = turn * STEP + lax.broadcasted_iota(jnp.int32, (1, STEP), 1)
        mask = ((places >= bound[:, 0:1]) & (places < bound[:, 1:2])) | (
            (places >= bound[:, 2:3]) & (places < bound[:, 3:4])
        )
    else:
        first = turn * STEP
        keep = (bound[:, 0:1] <= first) & (bound[:, 1:2] >= first + STEP)
    stat = stat_ref[pl.ds(low, span)].reshape(rows, LANES)
    o_old = o_ref[pl.ds(low, span)].reshape(rows, LANES)
    lane = lax.broadcasted_iota(jnp.int32, (rows, LANES), 1)
    first_half = lane < HD
    o_new = None
    stat_new = jnp.zeros((rows, LANES), jnp.float32)
    for g in range(2):
        query = q_ref[g, pl.ds(low, span)].reshape(rows, LANES)
        score = lax.dot_general(
            query, keys, (((1,), (1,)), ((), ())), preferred_element_type=jnp.float32
        )
        if masked:
            score = jnp.where(mask, score, fill_score)
        m_old = stat[:, 2 * g : 2 * g + 1]
        l_old = stat[:, 2 * g + 1 : 2 * g + 2]
        m_new = jnp.maximum(m_old, jnp.max(score, axis=1, keepdims=True))
        expo = jnp.exp(score - m_new)
        alpha = jnp.exp(m_old - m_new)
        l_new = alpha * l_old + jnp.sum(expo, axis=1, keepdims=True)
        mixed = jnp.dot(expo.astype(jnp.bfloat16), vals, preferred_element_type=jnp.float32)
        if g == 0:
            o_new = jnp.where(first_half, o_old * alpha + mixed, 0.0)
        else:
            o_new = jnp.where(first_half, o_new, o_old * alpha + mixed)
        stat_new = jnp.where(lane == 2 * g, m_new, stat_new)
        stat_new = jnp.where(lane == 2 * g + 1, l_new, stat_new)
    if not masked:
        o_new = jnp.where(keep, o_new, o_old)
        stat_new = jnp.where(keep, stat_new, stat)
    o_ref[pl.ds(low, span)] = o_new.reshape(span, PAD, LANES)
    stat_ref[pl.ds(low, span)] = stat_new.reshape(span, PAD, LANES)


def attend_kernel(
    gid_ref, pre_ref, suf_ref, off_ref, q_ref, k_ref, v_ref, o_ref, stat_ref, edge_ref, bound_ref,
    chunk_ref, table_ref,
):
    turn = pl.program_id(0)
    requests = q_ref.shape[1]
    groups = pre_ref.shape[0]
    refs = (q_ref, bound_ref, k_ref, v_ref, o_ref, stat_ref)

    @pl.when(turn == 0)
    def _():
        o_ref[...] = jnp.zeros(o_ref.shape, jnp.float32)
        lane3 = lax.broadcasted_iota(jnp.int32, stat_ref.shape, 2)
        stat_ref[...] = jnp.where(lane3 % 2 == 0, fill_score, 0.0).astype(jnp.float32)
        offset = off_ref[0]
        for gg in range(groups):
            table_ref[3 * groups + gg] = 0
        for t in range(CHUNKS + 2):
            chunk_ref[3 * CHUNKS + t] = 0

        def sums(r, run):
            g = gid_ref[r]
            s = suf_ref[r]
            edge_ref[r] = run
            table_ref[3 * groups + g] = table_ref[3 * groups + g] + s
            return run + s

        lax.fori_loop(0, requests, sums, jnp.int32(0), unroll=8)
        prefix_excl = jnp.int32(0)
        earlier = jnp.int32(0)
        starts = []
        ends = []
        for gg in range(groups):
            start = prefix_excl + earlier - offset
            starts.append(start)
            ends.append(start + pre_ref[gg])
            table_ref[gg] = start
            table_ref[groups + gg] = start + pre_ref[gg]
            table_ref[2 * groups + gg] = prefix_excl + pre_ref[gg] - offset
            earlier = earlier + table_ref[3 * groups + gg]
            prefix_excl = prefix_excl + pre_ref[gg]
        for t in range(CHUNKS):
            begin = t * STEP
            inside = jnp.int32(0)
            touch = jnp.int32(0)
            for gg in range(groups):
                hold = (starts[gg] <= begin) & (ends[gg] >= begin + STEP)
                meet = (starts[gg] < begin + STEP) & (ends[gg] > begin)
                inside = jnp.maximum(inside, jnp.where(hold, 1, 0))
                touch = jnp.maximum(touch, jnp.where(meet, 1, 0))
            chunk_ref[CHUNKS + t] = inside
            chunk_ref[2 * CHUNKS + t] = touch
        lane = lax.broadcasted_iota(jnp.int32, (PAD, LANES), 1)

        def edges(r, c):
            g = gid_ref[r]
            ps = table_ref[g]
            pe = table_ref[groups + g]
            os_ = table_ref[2 * groups + g] + edge_ref[r]
            oe = os_ + suf_ref[r]
            bound_ref[r] = jnp.where(
                lane == 0, ps, jnp.where(lane == 1, pe, jnp.where(lane == 2, os_, oe))
            )
            bucket = jnp.clip(jnp.right_shift(oe + (STEP - 1), STEP.bit_length() - 1), 0, CHUNKS + 1)
            chunk_ref[3 * CHUNKS + bucket] = chunk_ref[3 * CHUNKS + bucket] + 1
            return c

        lax.fori_loop(0, requests, edges, 0, unroll=8)
        count = jnp.int32(0)
        for t in range(CHUNKS):
            count = count + chunk_ref[3 * CHUNKS + t]
            chunk_ref[t] = count

    first = chunk_ref[turn]
    inside = chunk_ref[CHUNKS + turn]
    touch = chunk_ref[2 * CHUNKS + turn]

    @pl.when((inside == 0) & (touch == 1))
    def _():
        span = min(SPAN, requests)
        attend_window(turn, jnp.minimum(first, requests - span), span, True, *refs)

    @pl.when(inside == 1)
    def _():
        span = min(GROUP_MAX, requests)
        attend_window(turn, jnp.minimum(first, requests - span), span, False, *refs)

    @pl.when((inside == 0) & (touch == 0))
    def _():
        span = min(OWNERS, requests)
        attend_window(turn, jnp.minimum(first, requests - span), span, True, *refs)


def per_device(
    queries,
    new_keys,
    new_values,
    key_cache,
    value_cache,
    out_weight,
    group_ids,
    prefix_len,
    suffix_len,
):
    rows = queries.shape[0]
    heads_local = queries.shape[1] // HD
    kv_local = key_cache.shape[1] // HD
    repeat = heads_local // kv_local
    requests = rows // NEW
    block = key_cache.shape[0]
    span = min(SPAN, requests)
    tj = NEW * repeat
    steps = block // STEP
    assert steps == CHUNKS
    offset = jnp.full((1,), lax.axis_index("seq") * block, jnp.int32)
    scaled = (queries * jnp.asarray(0.125, queries.dtype)).reshape(requests, NEW, kv_local, repeat, HD)
    scaled = scaled.transpose(2, 0, 1, 3, 4).reshape(kv_local, requests, tj, HD)
    query_pad = jnp.stack(
        [
            jnp.pad(scaled[g], ((0, 0), (0, PAD - tj), (g * HD, LANES - (g + 1) * HD)))
            for g in range(kv_local)
        ]
    )
    full = lambda shape: pl.BlockSpec(shape, lambda t, *_: (0,) * len(shape))
    o_out, stat_out = pl.pallas_call(
        attend_kernel,
        grid_spec=pltpu.PrefetchScalarGridSpec(
            num_scalar_prefetch=4,
            grid=(steps,),
            in_specs=[
                full((kv_local, requests, PAD, LANES)),
                pl.BlockSpec((STEP, LANES), lambda t, *_: (t, 0)),
                pl.BlockSpec((STEP, LANES), lambda t, *_: (t, 0)),
            ],
            out_specs=[full((requests, PAD, LANES)), full((requests, PAD, LANES))],
            scratch_shapes=[
                pltpu.SMEM((requests,), jnp.int32),
                pltpu.VMEM((requests, PAD, LANES), jnp.int32),
                pltpu.SMEM((4 * steps + 2,), jnp.int32),
                pltpu.SMEM((4 * prefix_len.shape[0],), jnp.int32),
            ],
        ),
        out_shape=[
            jax.ShapeDtypeStruct((requests, PAD, LANES), jnp.float32),
            jax.ShapeDtypeStruct((requests, PAD, LANES), jnp.float32),
        ],
        compiler_params=pltpu.CompilerParams(dimension_semantics=("arbitrary",)),
    )(group_ids, prefix_len, suffix_len, offset, query_pad, key_cache, value_cache)
    width = tj * LANES
    packed = jnp.concatenate(
        [
            o_out[:, :tj, :].reshape(requests, width),
            stat_out[:, :tj, : 2 * kv_local].reshape(requests, tj * 2 * kv_local),
        ],
        axis=1,
    )
    packed = lax.all_to_all(packed, "seq", split_axis=0, concat_axis=0, tiled=True)
    sums = packed[:, :width].reshape(requests, tj, kv_local, HD)
    stats = packed[:, width:].reshape(requests, tj, kv_local, 2)
    maxes = stats[..., 0]
    totals = stats[..., 1]
    own_max = jnp.max(maxes, axis=0)
    rescale = jnp.exp(maxes - own_max[None])
    own_total = jnp.sum(totals * rescale, axis=0)
    own_summed = jnp.sum(sums * rescale[..., None], axis=0)
    mine = lax.axis_index("seq")
    own_query = lax.dynamic_slice_in_dim(queries, mine * NEW, NEW, 0)
    own_query = own_query.reshape(NEW, kv_local, repeat, HD).transpose(0, 2, 1, 3)
    own_query = own_query.reshape(tj, kv_local, HD)
    keys_new = new_keys.reshape(NEW, kv_local, HD)
    values_new = new_values.reshape(NEW, kv_local, HD)
    token_of = jnp.arange(tj) // repeat
    causal = (token_of[:, None] >= jnp.arange(NEW)[None, :])[:, None, :]
    score_new = (
        jnp.einsum("qgd,ugd->qgu", own_query, keys_new, preferred_element_type=jnp.float32)
        * 0.125
    )
    joined = jnp.maximum(own_max, jnp.max(jnp.where(causal, score_new, fill_score), axis=-1))
    expo_new = jnp.where(causal, jnp.exp(score_new - joined[..., None]), 0.0)
    factor_own = jnp.exp(own_max - joined)
    denominator = own_total * factor_own + jnp.sum(expo_new, axis=-1)
    numerator = own_summed * factor_own[..., None] + jnp.einsum(
        "qgu,ugd->qgd",
        expo_new.astype(jnp.bfloat16),
        values_new,
        preferred_element_type=jnp.float32,
    )
    mixed = (numerator / denominator[..., None]).astype(jnp.bfloat16)
    mixed = mixed.reshape(NEW, repeat, kv_local, HD).transpose(0, 2, 1, 3)
    mixed = mixed.reshape(NEW, heads_local * HD)
    partial_out = jnp.dot(mixed, out_weight, preferred_element_type=jnp.float32)
    parts = lax.axis_size("tp")
    piece = partial_out.shape[1] // parts
    pieces = partial_out.reshape(NEW, parts, piece)
    me = lax.axis_index("tp")
    result = lax.dynamic_index_in_dim(pieces, me, 1, keepdims=False)
    for shift in range(1, parts):
        sent = lax.dynamic_index_in_dim(pieces, (me + shift) % parts, 1, keepdims=False)
        pairs = [(i, (i + shift) % parts) for i in range(parts)]
        result = result + lax.ppermute(sent, "tp", pairs)
    return result.astype(jnp.bfloat16)


def solution(mesh):
    placed = (
        P(None, "tp"),
        P("seq", "tp"),
        P("seq", "tp"),
        P("seq", "tp"),
        P("seq", "tp"),
        P("tp", None),
        P(),
        P(),
        P(),
    )
    return jax.shard_map(
        per_device, mesh=mesh, in_specs=placed, out_specs=P("seq", "tp"), check_vma=False
    )
```

```python
import jax
import jax.numpy as jnp
from jax import lax
from jax.experimental import pallas as pl
from jax.experimental.pallas import tpu as pltpu
from jax.sharding import PartitionSpec as P

HD = 64
NEW = 5
STEP = 4096
SPAN = 19
GROUP_MAX = 16
OWNERS = 4
CHUNKS = 2
PAD = 16
LANES = 128


fill_score = -1e30


def segment_starts(group_ids, prefix_len, suffix_len):
    groups = jnp.arange(prefix_len.shape[0], dtype=jnp.int32)
    prefix_excl = jnp.cumsum(prefix_len) - prefix_len
    suffix_excl = jnp.cumsum(suffix_len) - suffix_len
    earlier = group_ids[None, :] < groups[:, None]
    prompt_start = prefix_excl + jnp.sum(jnp.where(earlier, suffix_len[None, :], 0), axis=1)
    member = group_ids[:, None] == groups[None, :]
    req_prompt_start = jnp.sum(jnp.where(member, prompt_start[None, :], 0), axis=1)
    req_prompt_len = jnp.sum(jnp.where(member, prefix_len[None, :], 0), axis=1)
    prefix_incl = jnp.sum(jnp.where(member, (prefix_excl + prefix_len)[None, :], 0), axis=1)
    own_start = prefix_incl + suffix_excl
    return (req_prompt_start, req_prompt_len, own_start)


def attend_window(turn, low, span, masked, q_ref, bound_ref, k_ref, v_ref, o_ref, stat_ref):
    rows = span * PAD
    keys = k_ref[...]
    vals = v_ref[...]
    bound = bound_ref[pl.ds(low, span)].reshape(rows, LANES)
    if masked:
        places = turn * STEP + lax.broadcasted_iota(jnp.int32, (1, STEP), 1)
        mask = ((places >= bound[:, 0:1]) & (places < bound[:, 1:2])) | (
            (places >= bound[:, 2:3]) & (places < bound[:, 3:4])
        )
    else:
        first = turn * STEP
        keep = (bound[:, 0:1] <= first) & (bound[:, 1:2] >= first + STEP)
    stat = stat_ref[pl.ds(low, span)].reshape(rows, LANES)
    o_old = o_ref[pl.ds(low, span)].reshape(rows, LANES)
    lane = lax.broadcasted_iota(jnp.int32, (rows, LANES), 1)
    first_half = lane < HD
    o_new = None
    stat_new = jnp.zeros((rows, LANES), jnp.float32)
    for g in range(2):
        query = q_ref[g, pl.ds(low, span)].reshape(rows, LANES)
        score = lax.dot_general(
            query, keys, (((1,), (1,)), ((), ())), preferred_element_type=jnp.float32
        )
        if masked:
            score = jnp.where(mask, score, fill_score)
        m_old = stat[:, 2 * g : 2 * g + 1]
        l_old = stat[:, 2 * g + 1 : 2 * g + 2]
        m_new = jnp.maximum(m_old, jnp.max(score, axis=1, keepdims=True))
        expo = jnp.exp(score - m_new)
        alpha = jnp.exp(m_old - m_new)
        l_new = alpha * l_old + jnp.sum(expo, axis=1, keepdims=True)
        mixed = jnp.dot(expo.astype(jnp.bfloat16), vals, preferred_element_type=jnp.float32)
        if g == 0:
            o_new = jnp.where(first_half, o_old * alpha + mixed, 0.0)
        else:
            o_new = jnp.where(first_half, o_new, o_old * alpha + mixed)
        stat_new = jnp.where(lane == 2 * g, m_new, stat_new)
        stat_new = jnp.where(lane == 2 * g + 1, l_new, stat_new)
    if not masked:
        o_new = jnp.where(keep, o_new, o_old)
        stat_new = jnp.where(keep, stat_new, stat)
    o_ref[pl.ds(low, span)] = o_new.reshape(span, PAD, LANES)
    stat_ref[pl.ds(low, span)] = stat_new.reshape(span, PAD, LANES)


def attend_kernel(
    gid_ref, pre_ref, suf_ref, off_ref, q_ref, k_ref, v_ref, o_ref, stat_ref, edge_ref, bound_ref,
    chunk_ref, table_ref,
):
    turn = pl.program_id(0)
    requests = q_ref.shape[1]
    groups = pre_ref.shape[0]
    refs = (q_ref, bound_ref, k_ref, v_ref, o_ref, stat_ref)

    @pl.when(turn == 0)
    def _():
        o_ref[...] = jnp.zeros(o_ref.shape, jnp.float32)
        lane3 = lax.broadcasted_iota(jnp.int32, stat_ref.shape, 2)
        stat_ref[...] = jnp.where(lane3 % 2 == 0, fill_score, 0.0).astype(jnp.float32)
        offset = off_ref[0]
        for gg in range(groups):
            table_ref[3 * groups + gg] = 0
        for t in range(CHUNKS + 2):
            chunk_ref[3 * CHUNKS + t] = 0

        def sums(r, run):
            g = gid_ref[r]
            s = suf_ref[r]
            edge_ref[r] = run
            table_ref[3 * groups + g] = table_ref[3 * groups + g] + s
            return run + s

        lax.fori_loop(0, requests, sums, jnp.int32(0), unroll=8)
        prefix_excl = jnp.int32(0)
        earlier = jnp.int32(0)
        starts = []
        ends = []
        for gg in range(groups):
            start = prefix_excl + earlier - offset
            starts.append(start)
            ends.append(start + pre_ref[gg])
            table_ref[gg] = start
            table_ref[groups + gg] = start + pre_ref[gg]
            table_ref[2 * groups + gg] = prefix_excl + pre_ref[gg] - offset
            earlier = earlier + table_ref[3 * groups + gg]
            prefix_excl = prefix_excl + pre_ref[gg]
        for t in range(CHUNKS):
            begin = t * STEP
            inside = jnp.int32(0)
            touch = jnp.int32(0)
            for gg in range(groups):
                hold = (starts[gg] <= begin) & (ends[gg] >= begin + STEP)
                meet = (starts[gg] < begin + STEP) & (ends[gg] > begin)
                inside = jnp.maximum(inside, jnp.where(hold, 1, 0))
                touch = jnp.maximum(touch, jnp.where(meet, 1, 0))
            chunk_ref[CHUNKS + t] = inside
            chunk_ref[2 * CHUNKS + t] = touch
        lane = lax.broadcasted_iota(jnp.int32, (PAD, LANES), 1)

        def edges(r, c):
            g = gid_ref[r]
            ps = table_ref[g]
            pe = table_ref[groups + g]
            os_ = table_ref[2 * groups + g] + edge_ref[r]
            oe = os_ + suf_ref[r]
            bound_ref[r] = jnp.where(
                lane == 0, ps, jnp.where(lane == 1, pe, jnp.where(lane == 2, os_, oe))
            )
            bucket = jnp.clip(jnp.right_shift(oe + (STEP - 1), STEP.bit_length() - 1), 0, CHUNKS + 1)
            chunk_ref[3 * CHUNKS + bucket] = chunk_ref[3 * CHUNKS + bucket] + 1
            return c

        lax.fori_loop(0, requests, edges, 0, unroll=8)
        count = jnp.int32(0)
        for t in range(CHUNKS):
            count = count + chunk_ref[3 * CHUNKS + t]
            chunk_ref[t] = count

    first = chunk_ref[turn]
    inside = chunk_ref[CHUNKS + turn]
    touch = chunk_ref[2 * CHUNKS + turn]

    @pl.when((inside == 0) & (touch == 1))
    def _():
        span = min(SPAN, requests)
        attend_window(turn, jnp.minimum(first, requests - span), span, True, *refs)

    @pl.when(inside == 1)
    def _():
        span = min(GROUP_MAX, requests)
        attend_window(turn, jnp.minimum(first, requests - span), span, False, *refs)

    @pl.when((inside == 0) & (touch == 0))
    def _():
        span = min(OWNERS, requests)
        attend_window(turn, jnp.minimum(first, requests - span), span, True, *refs)


def per_device(
    queries,
    new_keys,
    new_values,
    key_cache,
    value_cache,
    out_weight,
    group_ids,
    prefix_len,
    suffix_len,
):
    rows = queries.shape[0]
    heads_local = queries.shape[1] // HD
    kv_local = key_cache.shape[1] // HD
    repeat = heads_local // kv_local
    requests = rows // NEW
    block = key_cache.shape[0]
    span = min(SPAN, requests)
    tj = NEW * repeat
    steps = block // STEP
    assert steps == CHUNKS
    offset = jnp.full((1,), lax.axis_index("seq") * block, jnp.int32)
    scaled = (queries * jnp.asarray(0.125, queries.dtype)).reshape(requests, NEW, kv_local, repeat, HD)
    scaled = scaled.transpose(2, 0, 1, 3, 4).reshape(kv_local, requests, tj, HD)
    query_pad = jnp.stack(
        [
            jnp.pad(scaled[g], ((0, 0), (0, PAD - tj), (g * HD, LANES - (g + 1) * HD)))
            for g in range(kv_local)
        ]
    )
    full = lambda shape: pl.BlockSpec(shape, lambda t, *_: (0,) * len(shape))
    o_out, stat_out = pl.pallas_call(
        attend_kernel,
        grid_spec=pltpu.PrefetchScalarGridSpec(
            num_scalar_prefetch=4,
            grid=(steps,),
            in_specs=[
                full((kv_local, requests, PAD, LANES)),
                pl.BlockSpec((STEP, LANES), lambda t, *_: (t, 0)),
                pl.BlockSpec((STEP, LANES), lambda t, *_: (t, 0)),
            ],
            out_specs=[full((requests, PAD, LANES)), full((requests, PAD, LANES))],
            scratch_shapes=[
                pltpu.SMEM((requests,), jnp.int32),
                pltpu.VMEM((requests, PAD, LANES), jnp.int32),
                pltpu.SMEM((4 * steps + 2,), jnp.int32),
                pltpu.SMEM((4 * prefix_len.shape[0],), jnp.int32),
            ],
        ),
        out_shape=[
            jax.ShapeDtypeStruct((requests, PAD, LANES), jnp.float32),
            jax.ShapeDtypeStruct((requests, PAD, LANES), jnp.float32),
        ],
        compiler_params=pltpu.CompilerParams(dimension_semantics=("arbitrary",)),
    )(group_ids, prefix_len, suffix_len, offset, query_pad, key_cache, value_cache)
    width = tj * LANES
    packed = jnp.concatenate(
        [
            o_out[:, :tj, :].reshape(requests, width),
            stat_out[:, :tj, : 2 * kv_local].reshape(requests, tj * 2 * kv_local),
        ],
        axis=1,
    )
    packed = lax.all_to_all(packed, "seq", split_axis=0, concat_axis=0, tiled=True)
    sums = packed[:, :width].reshape(requests, tj, kv_local, HD)
    stats = packed[:, width:].reshape(requests, tj, kv_local, 2)
    maxes = stats[..., 0]
    totals = stats[..., 1]
    own_max = jnp.max(maxes, axis=0)
    rescale = jnp.exp(maxes - own_max[None])
    own_total = jnp.sum(totals * rescale, axis=0)
    own_summed = jnp.sum(sums * rescale[..., None], axis=0)
    mine = lax.axis_index("seq")
    own_query = lax.dynamic_slice_in_dim(queries, mine * NEW, NEW, 0)
    own_query = own_query.reshape(NEW, kv_local, repeat, HD).transpose(0, 2, 1, 3)
    own_query = own_query.reshape(tj, kv_local, HD)
    keys_new = new_keys.reshape(NEW, kv_local, HD)
    values_new = new_values.reshape(NEW, kv_local, HD)
    token_of = jnp.arange(tj) // repeat
    causal = (token_of[:, None] >= jnp.arange(NEW)[None, :])[:, None, :]
    score_new = (
        jnp.einsum("qgd,ugd->qgu", own_query, keys_new, preferred_element_type=jnp.float32)
        * 0.125
    )
    joined = jnp.maximum(own_max, jnp.max(jnp.where(causal, score_new, fill_score), axis=-1))
    expo_new = jnp.where(causal, jnp.exp(score_new - joined[..., None]), 0.0)
    factor_own = jnp.exp(own_max - joined)
    denominator = own_total * factor_own + jnp.sum(expo_new, axis=-1)
    numerator = own_summed * factor_own[..., None] + jnp.einsum(
        "qgu,ugd->qgd",
        expo_new.astype(jnp.bfloat16),
        values_new,
        preferred_element_type=jnp.float32,
    )
    mixed = (numerator / denominator[..., None]).astype(jnp.bfloat16)
    mixed = mixed.reshape(NEW, repeat, kv_local, HD).transpose(0, 2, 1, 3)
    mixed = mixed.reshape(NEW, heads_local * HD)
    partial_out = jnp.dot(mixed, out_weight, preferred_element_type=jnp.float32)
    parts = lax.axis_size("tp")
    piece = partial_out.shape[1] // parts
    pieces = partial_out.reshape(NEW, parts, piece)
    me = lax.axis_index("tp")
    result = lax.dynamic_index_in_dim(pieces, me, 1, keepdims=False)
    for shift in range(1, parts):
        sent = lax.dynamic_index_in_dim(pieces, (me + shift) % parts, 1, keepdims=False)
        pairs = [(i, (i + shift) % parts) for i in range(parts)]
        result = result + lax.ppermute(sent, "tp", pairs)
    return result.astype(jnp.bfloat16)


def solution(mesh):
    placed = (
        P(None, "tp"),
        P("seq", "tp"),
        P("seq", "tp"),
        P("seq", "tp"),
        P("seq", "tp"),
        P("tp", None),
        P(),
        P(),
        P(),
    )
    return jax.shard_map(
        per_device, mesh=mesh, in_specs=placed, out_specs=P("seq", "tp"), check_vma=False
    )
```

```python
import jax
import jax.numpy as jnp
from jax import lax
from jax.experimental import pallas as pl
from jax.experimental.pallas import tpu as pltpu
from jax.sharding import PartitionSpec as P

HD = 64
NEW = 5
STEP = 2048
SPAN = 18
GROUP_MAX = 16
OWNERS = 3
CHUNKS = 4
PAD = 16
LANES = 128


fill_score = -1e30


def segment_starts(group_ids, prefix_len, suffix_len):
    groups = jnp.arange(prefix_len.shape[0], dtype=jnp.int32)
    prefix_excl = jnp.cumsum(prefix_len) - prefix_len
    suffix_excl = jnp.cumsum(suffix_len) - suffix_len
    earlier = group_ids[None, :] < groups[:, None]
    prompt_start = prefix_excl + jnp.sum(jnp.where(earlier, suffix_len[None, :], 0), axis=1)
    member = group_ids[:, None] == groups[None, :]
    req_prompt_start = jnp.sum(jnp.where(member, prompt_start[None, :], 0), axis=1)
    req_prompt_len = jnp.sum(jnp.where(member, prefix_len[None, :], 0), axis=1)
    prefix_incl = jnp.sum(jnp.where(member, (prefix_excl + prefix_len)[None, :], 0), axis=1)
    own_start = prefix_incl + suffix_excl
    return (req_prompt_start, req_prompt_len, own_start)


def attend_window(turn, low, span, masked, q_ref, bound_ref, k_ref, v_ref, o_ref, stat_ref):
    rows = span * PAD
    keys = k_ref[...]
    vals = v_ref[...]
    bound = bound_ref[pl.ds(low, span)].reshape(rows, LANES)
    if masked:
        places = turn * STEP + lax.broadcasted_iota(jnp.int32, (1, STEP), 1)
        mask = ((places >= bound[:, 0:1]) & (places < bound[:, 1:2])) | (
            (places >= bound[:, 2:3]) & (places < bound[:, 3:4])
        )
    else:
        first = turn * STEP
        keep = (bound[:, 0:1] <= first) & (bound[:, 1:2] >= first + STEP)
    stat = stat_ref[pl.ds(low, span)].reshape(rows, LANES)
    o_old = o_ref[pl.ds(low, span)].reshape(rows, LANES)
    lane = lax.broadcasted_iota(jnp.int32, (rows, LANES), 1)
    first_half = lane < HD
    o_new = None
    stat_new = jnp.zeros((rows, LANES), jnp.float32)
    for g in range(2):
        query = q_ref[g, pl.ds(low, span)].reshape(rows, LANES)
        score = lax.dot_general(
            query, keys, (((1,), (1,)), ((), ())), preferred_element_type=jnp.float32
        )
        if masked:
            score = jnp.where(mask, score, fill_score)
        m_old = stat[:, 2 * g : 2 * g + 1]
        l_old = stat[:, 2 * g + 1 : 2 * g + 2]
        m_new = jnp.maximum(m_old, jnp.max(score, axis=1, keepdims=True))
        expo = jnp.exp(score - m_new)
        alpha = jnp.exp(m_old - m_new)
        l_new = alpha * l_old + jnp.sum(expo, axis=1, keepdims=True)
        mixed = jnp.dot(expo.astype(jnp.bfloat16), vals, preferred_element_type=jnp.float32)
        if g == 0:
            o_new = jnp.where(first_half, o_old * alpha + mixed, 0.0)
        else:
            o_new = jnp.where(first_half, o_new, o_old * alpha + mixed)
        stat_new = jnp.where(lane == 2 * g, m_new, stat_new)
        stat_new = jnp.where(lane == 2 * g + 1, l_new, stat_new)
    if not masked:
        o_new = jnp.where(keep, o_new, o_old)
        stat_new = jnp.where(keep, stat_new, stat)
    o_ref[pl.ds(low, span)] = o_new.reshape(span, PAD, LANES)
    stat_ref[pl.ds(low, span)] = stat_new.reshape(span, PAD, LANES)


def attend_kernel(
    gid_ref, pre_ref, suf_ref, off_ref, q_ref, k_ref, v_ref, o_ref, stat_ref, edge_ref, bound_ref,
    chunk_ref, table_ref,
):
    turn = pl.program_id(0)
    requests = q_ref.shape[1]
    groups = pre_ref.shape[0]
    refs = (q_ref, bound_ref, k_ref, v_ref, o_ref, stat_ref)

    @pl.when(turn == 0)
    def _():
        o_ref[...] = jnp.zeros(o_ref.shape, jnp.float32)
        lane3 = lax.broadcasted_iota(jnp.int32, stat_ref.shape, 2)
        stat_ref[...] = jnp.where(lane3 % 2 == 0, fill_score, 0.0).astype(jnp.float32)
        offset = off_ref[0]
        def sums(r, carry):
            run = carry[0]
            g = gid_ref[r]
            s = suf_ref[r]
            edge_ref[r] = run
            acc = tuple(a + jnp.where(g == gg, s, 0) for gg, a in enumerate(carry[1:]))
            return (run + s,) + acc

        carry = lax.fori_loop(0, requests, sums, (jnp.int32(0),) * (1 + groups), unroll=8)
        for gg in range(groups):
            table_ref[3 * groups + gg] = carry[1 + gg]
        prefix_excl = jnp.int32(0)
        earlier = jnp.int32(0)
        starts = []
        ends = []
        for gg in range(groups):
            start = prefix_excl + earlier - offset
            starts.append(start)
            ends.append(start + pre_ref[gg])
            table_ref[gg] = start
            table_ref[groups + gg] = start + pre_ref[gg]
            table_ref[2 * groups + gg] = prefix_excl + pre_ref[gg] - offset
            earlier = earlier + table_ref[3 * groups + gg]
            prefix_excl = prefix_excl + pre_ref[gg]
        for t in range(CHUNKS):
            begin = t * STEP
            inside = jnp.int32(0)
            touch = jnp.int32(0)
            for gg in range(groups):
                hold = (starts[gg] <= begin) & (ends[gg] >= begin + STEP)
                meet = (starts[gg] < begin + STEP) & (ends[gg] > begin)
                inside = jnp.maximum(inside, jnp.where(hold, 1, 0))
                touch = jnp.maximum(touch, jnp.where(meet, 1, 0))
            chunk_ref[CHUNKS + t] = inside
            chunk_ref[2 * CHUNKS + t] = touch
        lane = lax.broadcasted_iota(jnp.int32, (PAD, LANES), 1)

        def edges(r, c):
            g = gid_ref[r]
            ps = table_ref[g]
            pe = table_ref[groups + g]
            os_ = table_ref[2 * groups + g] + edge_ref[r]
            oe = os_ + suf_ref[r]
            bound_ref[r] = jnp.where(
                lane == 0, ps, jnp.where(lane == 1, pe, jnp.where(lane == 2, os_, oe))
            )
            return tuple(f + jnp.where(oe <= t * STEP, 1, 0) for t, f in enumerate(c))

        firsts = lax.fori_loop(0, requests, edges, (jnp.int32(0),) * CHUNKS, unroll=8)
        for t in range(CHUNKS):
            chunk_ref[t] = firsts[t]

    first = chunk_ref[turn]
    inside = chunk_ref[CHUNKS + turn]
    touch = chunk_ref[2 * CHUNKS + turn]

    @pl.when((inside == 0) & (touch == 1))
    def _():
        span = min(SPAN, requests)
        attend_window(turn, jnp.minimum(first, requests - span), span, True, *refs)

    @pl.when(inside == 1)
    def _():
        span = min(GROUP_MAX, requests)
        attend_window(turn, jnp.minimum(first, requests - span), span, False, *refs)

    @pl.when((inside == 0) & (touch == 0))
    def _():
        span = min(OWNERS, requests)
        attend_window(turn, jnp.minimum(first, requests - span), span, True, *refs)


def per_device(
    queries,
    new_keys,
    new_values,
    key_cache,
    value_cache,
    out_weight,
    group_ids,
    prefix_len,
    suffix_len,
):
    rows = queries.shape[0]
    heads_local = queries.shape[1] // HD
    kv_local = key_cache.shape[1] // HD
    repeat = heads_local // kv_local
    requests = rows // NEW
    block = key_cache.shape[0]
    span = min(SPAN, requests)
    tj = NEW * repeat
    steps = block // STEP
    assert steps == CHUNKS
    offset = jnp.full((1,), lax.axis_index("seq") * block, jnp.int32)
    scaled = (queries * jnp.asarray(0.125, queries.dtype)).reshape(requests, NEW, kv_local, repeat, HD)
    scaled = scaled.transpose(2, 0, 1, 3, 4).reshape(kv_local, requests, tj, HD)
    query_pad = jnp.stack(
        [
            jnp.pad(scaled[g], ((0, 0), (0, PAD - tj), (g * HD, LANES - (g + 1) * HD)))
            for g in range(kv_local)
        ]
    )
    full = lambda shape: pl.BlockSpec(shape, lambda t, *_: (0,) * len(shape))
    o_out, stat_out = pl.pallas_call(
        attend_kernel,
        grid_spec=pltpu.PrefetchScalarGridSpec(
            num_scalar_prefetch=4,
            grid=(steps,),
            in_specs=[
                full((kv_local, requests, PAD, LANES)),
                pl.BlockSpec((STEP, LANES), lambda t, *_: (t, 0)),
                pl.BlockSpec((STEP, LANES), lambda t, *_: (t, 0)),
            ],
            out_specs=[full((requests, PAD, LANES)), full((requests, PAD, LANES))],
            scratch_shapes=[
                pltpu.SMEM((requests,), jnp.int32),
                pltpu.VMEM((requests, PAD, LANES), jnp.int32),
                pltpu.SMEM((4 * steps + 2,), jnp.int32),
                pltpu.SMEM((4 * prefix_len.shape[0],), jnp.int32),
            ],
        ),
        out_shape=[
            jax.ShapeDtypeStruct((requests, PAD, LANES), jnp.float32),
            jax.ShapeDtypeStruct((requests, PAD, LANES), jnp.float32),
        ],
        compiler_params=pltpu.CompilerParams(dimension_semantics=("arbitrary",)),
    )(group_ids, prefix_len, suffix_len, offset, query_pad, key_cache, value_cache)
    width = tj * LANES
    packed = jnp.concatenate(
        [
            o_out[:, :tj, :].reshape(requests, width),
            stat_out[:, :tj, : 2 * kv_local].reshape(requests, tj * 2 * kv_local),
        ],
        axis=1,
    )
    packed = lax.all_to_all(packed, "seq", split_axis=0, concat_axis=0, tiled=True)
    sums = packed[:, :width].reshape(requests, tj, kv_local, HD)
    stats = packed[:, width:].reshape(requests, tj, kv_local, 2)
    maxes = stats[..., 0]
    totals = stats[..., 1]
    own_max = jnp.max(maxes, axis=0)
    rescale = jnp.exp(maxes - own_max[None])
    own_total = jnp.sum(totals * rescale, axis=0)
    own_summed = jnp.sum(sums * rescale[..., None], axis=0)
    mine = lax.axis_index("seq")
    own_query = lax.dynamic_slice_in_dim(queries, mine * NEW, NEW, 0)
    own_query = own_query.reshape(NEW, kv_local, repeat, HD).transpose(0, 2, 1, 3)
    own_query = own_query.reshape(tj, kv_local, HD)
    keys_new = new_keys.reshape(NEW, kv_local, HD)
    values_new = new_values.reshape(NEW, kv_local, HD)
    token_of = jnp.arange(tj) // repeat
    causal = (token_of[:, None] >= jnp.arange(NEW)[None, :])[:, None, :]
    score_new = (
        jnp.einsum("qgd,ugd->qgu", own_query, keys_new, preferred_element_type=jnp.float32)
        * 0.125
    )
    joined = jnp.maximum(own_max, jnp.max(jnp.where(causal, score_new, fill_score), axis=-1))
    expo_new = jnp.where(causal, jnp.exp(score_new - joined[..., None]), 0.0)
    factor_own = jnp.exp(own_max - joined)
    denominator = own_total * factor_own + jnp.sum(expo_new, axis=-1)
    numerator = own_summed * factor_own[..., None] + jnp.einsum(
        "qgu,ugd->qgd",
        expo_new.astype(jnp.bfloat16),
        values_new,
        preferred_element_type=jnp.float32,
    )
    mixed = (numerator / denominator[..., None]).astype(jnp.bfloat16)
    mixed = mixed.reshape(NEW, repeat, kv_local, HD).transpose(0, 2, 1, 3)
    mixed = mixed.reshape(NEW, heads_local * HD)
    partial_out = jnp.dot(mixed, out_weight, preferred_element_type=jnp.float32)
    parts = lax.axis_size("tp")
    piece = partial_out.shape[1] // parts
    pieces = partial_out.reshape(NEW, parts, piece)
    me = lax.axis_index("tp")
    result = lax.dynamic_index_in_dim(pieces, me, 1, keepdims=False)
    for shift in range(1, parts):
        sent = lax.dynamic_index_in_dim(pieces, (me + shift) % parts, 1, keepdims=False)
        pairs = [(i, (i + shift) % parts) for i in range(parts)]
        result = result + lax.ppermute(sent, "tp", pairs)
    return result.astype(jnp.bfloat16)


def solution(mesh):
    placed = (
        P(None, "tp"),
        P("seq", "tp"),
        P("seq", "tp"),
        P("seq", "tp"),
        P("seq", "tp"),
        P("tp", None),
        P(),
        P(),
        P(),
    )
    return jax.shard_map(
        per_device, mesh=mesh, in_specs=placed, out_specs=P("seq", "tp"), check_vma=False
    )
```

```python
import jax
import jax.numpy as jnp
from jax import lax
from jax.experimental import pallas as pl
from jax.experimental.pallas import tpu as pltpu
from jax.sharding import PartitionSpec as P

HD = 64
NEW = 5
STEP = 2048
SPAN = 18
GROUP_MAX = 16
OWNERS = 3
CHUNKS = 4
PAD = 16
LANES = 128


fill_score = -1e30


def segment_starts(group_ids, prefix_len, suffix_len):
    groups = jnp.arange(prefix_len.shape[0], dtype=jnp.int32)
    prefix_excl = jnp.cumsum(prefix_len) - prefix_len
    suffix_excl = jnp.cumsum(suffix_len) - suffix_len
    earlier = group_ids[None, :] < groups[:, None]
    prompt_start = prefix_excl + jnp.sum(jnp.where(earlier, suffix_len[None, :], 0), axis=1)
    member = group_ids[:, None] == groups[None, :]
    req_prompt_start = jnp.sum(jnp.where(member, prompt_start[None, :], 0), axis=1)
    req_prompt_len = jnp.sum(jnp.where(member, prefix_len[None, :], 0), axis=1)
    prefix_incl = jnp.sum(jnp.where(member, (prefix_excl + prefix_len)[None, :], 0), axis=1)
    own_start = prefix_incl + suffix_excl
    return (req_prompt_start, req_prompt_len, own_start)


def attend_window(turn, low, span, masked, q_ref, bound_ref, k_ref, v_ref, o_ref, stat_ref):
    rows = span * PAD
    keys = k_ref[...]
    vals = v_ref[...]
    bound = bound_ref[pl.ds(low, span)].reshape(rows, LANES)
    if masked:
        places = turn * STEP + lax.broadcasted_iota(jnp.int32, (1, STEP), 1)
        mask = ((places >= bound[:, 0:1]) & (places < bound[:, 1:2])) | (
            (places >= bound[:, 2:3]) & (places < bound[:, 3:4])
        )
    else:
        first = turn * STEP
        keep = (bound[:, 0:1] <= first) & (bound[:, 1:2] >= first + STEP)
    stat = stat_ref[pl.ds(low, span)].reshape(rows, LANES)
    o_old = o_ref[pl.ds(low, span)].reshape(rows, LANES)
    lane = lax.broadcasted_iota(jnp.int32, (rows, LANES), 1)
    first_half = lane < HD
    o_new = None
    stat_new = jnp.zeros((rows, LANES), jnp.float32)
    for g in range(2):
        query = q_ref[g, pl.ds(low, span)].reshape(rows, LANES)
        score = lax.dot_general(
            query, keys, (((1,), (1,)), ((), ())), preferred_element_type=jnp.float32
        )
        if masked:
            score = jnp.where(mask, score, fill_score)
        m_old = stat[:, 2 * g : 2 * g + 1]
        l_old = stat[:, 2 * g + 1 : 2 * g + 2]
        m_new = jnp.maximum(m_old, jnp.max(score, axis=1, keepdims=True))
        expo = jnp.exp(score - m_new)
        alpha = jnp.exp(m_old - m_new)
        l_new = alpha * l_old + jnp.sum(expo, axis=1, keepdims=True)
        mixed = jnp.dot(expo.astype(jnp.bfloat16), vals, preferred_element_type=jnp.float32)
        if g == 0:
            o_new = jnp.where(first_half, o_old * alpha + mixed, 0.0)
        else:
            o_new = jnp.where(first_half, o_new, o_old * alpha + mixed)
        stat_new = jnp.where(lane == 2 * g, m_new, stat_new)
        stat_new = jnp.where(lane == 2 * g + 1, l_new, stat_new)
    if not masked:
        o_new = jnp.where(keep, o_new, o_old)
        stat_new = jnp.where(keep, stat_new, stat)
    o_ref[pl.ds(low, span)] = o_new.reshape(span, PAD, LANES)
    stat_ref[pl.ds(low, span)] = stat_new.reshape(span, PAD, LANES)


def attend_kernel(
    gid_ref, pre_ref, suf_ref, off_ref, q_ref, k_ref, v_ref, o_ref, stat_ref, edge_ref, bound_ref,
    chunk_ref, table_ref,
):
    turn = pl.program_id(0)
    requests = q_ref.shape[1]
    groups = pre_ref.shape[0]
    refs = (q_ref, bound_ref, k_ref, v_ref, o_ref, stat_ref)

    @pl.when(turn == 0)
    def _():
        o_ref[...] = jnp.zeros(o_ref.shape, jnp.float32)
        lane3 = lax.broadcasted_iota(jnp.int32, stat_ref.shape, 2)
        stat_ref[...] = jnp.where(lane3 % 2 == 0, fill_score, 0.0).astype(jnp.float32)
        offset = off_ref[0]
        for t in range(CHUNKS + 2):
            chunk_ref[3 * CHUNKS + t] = 0
        prefix_excl = jnp.int32(0)
        for gg in range(groups):
            table_ref[2 * groups + gg] = prefix_excl
            table_ref[gg] = prefix_excl - offset
            table_ref[groups + gg] = prefix_excl - offset
            prefix_excl = prefix_excl + pre_ref[gg]
        lane = lax.broadcasted_iota(jnp.int32, (PAD, LANES), 1)

        def edges(r, carry):
            run, within, last = carry
            g = gid_ref[r]
            s = suf_ref[r]
            within = jnp.where(g == last, within, 0)
            base = table_ref[2 * groups + g]
            ps = base + run - within - offset
            pe = ps + pre_ref[g]
            os_ = base + pre_ref[g] + run - offset
            oe = os_ + s
            table_ref[g] = ps
            table_ref[groups + g] = pe
            bound_ref[r] = jnp.where(
                lane == 0, ps, jnp.where(lane == 1, pe, jnp.where(lane == 2, os_, oe))
            )
            bucket = jnp.clip(jnp.right_shift(oe + (STEP - 1), STEP.bit_length() - 1), 0, CHUNKS + 1)
            chunk_ref[3 * CHUNKS + bucket] = chunk_ref[3 * CHUNKS + bucket] + 1
            return (run + s, within + s, g)

        zero = jnp.int32(0)
        lax.fori_loop(0, requests, edges, (zero, zero, jnp.int32(-1)), unroll=8)
        for t in range(CHUNKS):
            begin = t * STEP
            inside = jnp.int32(0)
            touch = jnp.int32(0)
            for gg in range(groups):
                start = table_ref[gg]
                end = table_ref[groups + gg]
                hold = (start <= begin) & (end >= begin + STEP)
                meet = (start < begin + STEP) & (end > begin)
                inside = jnp.maximum(inside, jnp.where(hold, 1, 0))
                touch = jnp.maximum(touch, jnp.where(meet, 1, 0))
            chunk_ref[CHUNKS + t] = inside
            chunk_ref[2 * CHUNKS + t] = touch
        count = jnp.int32(0)
        for t in range(CHUNKS):
            count = count + chunk_ref[3 * CHUNKS + t]
            chunk_ref[t] = count

    first = chunk_ref[turn]
    inside = chunk_ref[CHUNKS + turn]
    touch = chunk_ref[2 * CHUNKS + turn]

    @pl.when((inside == 0) & (touch == 1))
    def _():
        span = min(SPAN, requests)
        attend_window(turn, jnp.minimum(first, requests - span), span, True, *refs)

    @pl.when(inside == 1)
    def _():
        span = min(GROUP_MAX, requests)
        attend_window(turn, jnp.minimum(first, requests - span), span, False, *refs)

    @pl.when((inside == 0) & (touch == 0))
    def _():
        span = min(OWNERS, requests)
        attend_window(turn, jnp.minimum(first, requests - span), span, True, *refs)


def per_device(
    queries,
    new_keys,
    new_values,
    key_cache,
    value_cache,
    out_weight,
    group_ids,
    prefix_len,
    suffix_len,
):
    rows = queries.shape[0]
    heads_local = queries.shape[1] // HD
    kv_local = key_cache.shape[1] // HD
    repeat = heads_local // kv_local
    requests = rows // NEW
    block = key_cache.shape[0]
    span = min(SPAN, requests)
    tj = NEW * repeat
    steps = block // STEP
    assert steps == CHUNKS
    offset = jnp.full((1,), lax.axis_index("seq") * block, jnp.int32)
    scaled = (queries * jnp.asarray(0.125, queries.dtype)).reshape(requests, NEW, kv_local, repeat, HD)
    scaled = scaled.transpose(2, 0, 1, 3, 4).reshape(kv_local, requests, tj, HD)
    query_pad = jnp.stack(
        [
            jnp.pad(scaled[g], ((0, 0), (0, PAD - tj), (g * HD, LANES - (g + 1) * HD)))
            for g in range(kv_local)
        ]
    )
    full = lambda shape: pl.BlockSpec(shape, lambda t, *_: (0,) * len(shape))
    o_out, stat_out = pl.pallas_call(
        attend_kernel,
        grid_spec=pltpu.PrefetchScalarGridSpec(
            num_scalar_prefetch=4,
            grid=(steps,),
            in_specs=[
                full((kv_local, requests, PAD, LANES)),
                pl.BlockSpec((STEP, LANES), lambda t, *_: (t, 0)),
                pl.BlockSpec((STEP, LANES), lambda t, *_: (t, 0)),
            ],
            out_specs=[full((requests, PAD, LANES)), full((requests, PAD, LANES))],
            scratch_shapes=[
                pltpu.SMEM((requests,), jnp.int32),
                pltpu.VMEM((requests, PAD, LANES), jnp.int32),
                pltpu.SMEM((4 * steps + 2,), jnp.int32),
                pltpu.SMEM((4 * prefix_len.shape[0],), jnp.int32),
            ],
        ),
        out_shape=[
            jax.ShapeDtypeStruct((requests, PAD, LANES), jnp.float32),
            jax.ShapeDtypeStruct((requests, PAD, LANES), jnp.float32),
        ],
        compiler_params=pltpu.CompilerParams(dimension_semantics=("arbitrary",)),
    )(group_ids, prefix_len, suffix_len, offset, query_pad, key_cache, value_cache)
    width = tj * LANES
    packed = jnp.concatenate(
        [
            o_out[:, :tj, :].reshape(requests, width),
            stat_out[:, :tj, : 2 * kv_local].reshape(requests, tj * 2 * kv_local),
        ],
        axis=1,
    )
    packed = lax.all_to_all(packed, "seq", split_axis=0, concat_axis=0, tiled=True)
    sums = packed[:, :width].reshape(requests, tj, kv_local, HD)
    stats = packed[:, width:].reshape(requests, tj, kv_local, 2)
    maxes = stats[..., 0]
    totals = stats[..., 1]
    own_max = jnp.max(maxes, axis=0)
    rescale = jnp.exp(maxes - own_max[None])
    own_total = jnp.sum(totals * rescale, axis=0)
    own_summed = jnp.sum(sums * rescale[..., None], axis=0)
    mine = lax.axis_index("seq")
    own_query = lax.dynamic_slice_in_dim(queries, mine * NEW, NEW, 0)
    own_query = own_query.reshape(NEW, kv_local, repeat, HD).transpose(0, 2, 1, 3)
    own_query = own_query.reshape(tj, kv_local, HD)
    keys_new = new_keys.reshape(NEW, kv_local, HD)
    values_new = new_values.reshape(NEW, kv_local, HD)
    token_of = jnp.arange(tj) // repeat
    causal = (token_of[:, None] >= jnp.arange(NEW)[None, :])[:, None, :]
    score_new = (
        jnp.einsum("qgd,ugd->qgu", own_query, keys_new, preferred_element_type=jnp.float32)
        * 0.125
    )
    joined = jnp.maximum(own_max, jnp.max(jnp.where(causal, score_new, fill_score), axis=-1))
    expo_new = jnp.where(causal, jnp.exp(score_new - joined[..., None]), 0.0)
    factor_own = jnp.exp(own_max - joined)
    denominator = own_total * factor_own + jnp.sum(expo_new, axis=-1)
    numerator = own_summed * factor_own[..., None] + jnp.einsum(
        "qgu,ugd->qgd",
        expo_new.astype(jnp.bfloat16),
        values_new,
        preferred_element_type=jnp.float32,
    )
    mixed = (numerator / denominator[..., None]).astype(jnp.bfloat16)
    mixed = mixed.reshape(NEW, repeat, kv_local, HD).transpose(0, 2, 1, 3)
    mixed = mixed.reshape(NEW, heads_local * HD)
    partial_out = jnp.dot(mixed, out_weight, preferred_element_type=jnp.float32)
    parts = lax.axis_size("tp")
    piece = partial_out.shape[1] // parts
    pieces = partial_out.reshape(NEW, parts, piece)
    me = lax.axis_index("tp")
    result = lax.dynamic_index_in_dim(pieces, me, 1, keepdims=False)
    for shift in range(1, parts):
        sent = lax.dynamic_index_in_dim(pieces, (me + shift) % parts, 1, keepdims=False)
        pairs = [(i, (i + shift) % parts) for i in range(parts)]
        result = result + lax.ppermute(sent, "tp", pairs)
    return result.astype(jnp.bfloat16)


def solution(mesh):
    placed = (
        P(None, "tp"),
        P("seq", "tp"),
        P("seq", "tp"),
        P("seq", "tp"),
        P("seq", "tp"),
        P("tp", None),
        P(),
        P(),
        P(),
    )
    return jax.shard_map(
        per_device, mesh=mesh, in_specs=placed, out_specs=P("seq", "tp"), check_vma=False
    )
```

```python
import jax
import jax.numpy as jnp
from jax import lax
from jax.experimental import pallas as pl
from jax.experimental.pallas import tpu as pltpu
from jax.sharding import PartitionSpec as P

HD = 64
NEW = 5
STEP = 2048
SPAN = 18
GROUP_MAX = 16
OWNERS = 3
CHUNKS = 4
PAD = 16
LANES = 128


fill_score = -1e30


def segment_starts(group_ids, prefix_len, suffix_len):
    groups = jnp.arange(prefix_len.shape[0], dtype=jnp.int32)
    prefix_excl = jnp.cumsum(prefix_len) - prefix_len
    suffix_excl = jnp.cumsum(suffix_len) - suffix_len
    earlier = group_ids[None, :] < groups[:, None]
    prompt_start = prefix_excl + jnp.sum(jnp.where(earlier, suffix_len[None, :], 0), axis=1)
    member = group_ids[:, None] == groups[None, :]
    req_prompt_start = jnp.sum(jnp.where(member, prompt_start[None, :], 0), axis=1)
    req_prompt_len = jnp.sum(jnp.where(member, prefix_len[None, :], 0), axis=1)
    prefix_incl = jnp.sum(jnp.where(member, (prefix_excl + prefix_len)[None, :], 0), axis=1)
    own_start = prefix_incl + suffix_excl
    return (req_prompt_start, req_prompt_len, own_start)


def attend_window(turn, low, span, masked, q_ref, bound_ref, k_ref, v_ref, o_ref, stat_ref):
    rows = span * PAD
    keys = k_ref[...]
    vals = v_ref[...]
    bound = bound_ref[pl.ds(low, span)].reshape(rows, LANES)
    if masked:
        places = turn * STEP + lax.broadcasted_iota(jnp.int32, (1, STEP), 1)
        mask = ((places >= bound[:, 0:1]) & (places < bound[:, 1:2])) | (
            (places >= bound[:, 2:3]) & (places < bound[:, 3:4])
        )
    else:
        first = turn * STEP
        keep = (bound[:, 0:1] <= first) & (bound[:, 1:2] >= first + STEP)
    stat = stat_ref[pl.ds(low, span)].reshape(rows, LANES)
    o_old = o_ref[pl.ds(low, span)].reshape(rows, LANES)
    lane = lax.broadcasted_iota(jnp.int32, (rows, LANES), 1)
    first_half = lane < HD
    o_new = None
    stat_new = jnp.zeros((rows, LANES), jnp.float32)
    for g in range(2):
        query = q_ref[g, pl.ds(low, span)].reshape(rows, LANES)
        score = lax.dot_general(
            query, keys, (((1,), (1,)), ((), ())), preferred_element_type=jnp.float32
        )
        if masked:
            score = jnp.where(mask, score, fill_score)
        m_old = stat[:, 2 * g : 2 * g + 1]
        l_old = stat[:, 2 * g + 1 : 2 * g + 2]
        m_new = jnp.maximum(m_old, jnp.max(score, axis=1, keepdims=True))
        expo = jnp.exp(score - m_new)
        alpha = jnp.exp(m_old - m_new)
        l_new = alpha * l_old + jnp.sum(expo, axis=1, keepdims=True)
        mixed = jnp.dot(expo.astype(jnp.bfloat16), vals, preferred_element_type=jnp.float32)
        if g == 0:
            o_new = jnp.where(first_half, o_old * alpha + mixed, 0.0)
        else:
            o_new = jnp.where(first_half, o_new, o_old * alpha + mixed)
        stat_new = jnp.where(lane == 2 * g, m_new, stat_new)
        stat_new = jnp.where(lane == 2 * g + 1, l_new, stat_new)
    if not masked:
        o_new = jnp.where(keep, o_new, o_old)
        stat_new = jnp.where(keep, stat_new, stat)
    o_ref[pl.ds(low, span)] = o_new.reshape(span, PAD, LANES)
    stat_ref[pl.ds(low, span)] = stat_new.reshape(span, PAD, LANES)


def attend_kernel(
    gid_ref, pre_ref, suf_ref, off_ref, q_ref, k_ref, v_ref, acc_ref, edge_ref, bound_ref,
    chunk_ref, table_ref,
):
    o_ref = acc_ref.at[:, 0:PAD, :]
    stat_ref = acc_ref.at[:, PAD : 2 * PAD, :]
    turn = pl.program_id(0)
    requests = q_ref.shape[1]
    groups = pre_ref.shape[0]
    refs = (q_ref, bound_ref, k_ref, v_ref, o_ref, stat_ref)

    @pl.when(turn == 0)
    def _():
        o_ref[...] = jnp.zeros(o_ref.shape, jnp.float32)
        lane3 = lax.broadcasted_iota(jnp.int32, stat_ref.shape, 2)
        stat_ref[...] = jnp.where(lane3 % 2 == 0, fill_score, 0.0).astype(jnp.float32)
        offset = off_ref[0]
        for gg in range(groups):
            table_ref[3 * groups + gg] = 0
        for t in range(CHUNKS + 2):
            chunk_ref[3 * CHUNKS + t] = 0

        def sums(r, run):
            g = gid_ref[r]
            s = suf_ref[r]
            edge_ref[r] = run
            table_ref[3 * groups + g] = table_ref[3 * groups + g] + s
            return run + s

        lax.fori_loop(0, requests, sums, jnp.int32(0), unroll=8)
        prefix_excl = jnp.int32(0)
        earlier = jnp.int32(0)
        starts = []
        ends = []
        for gg in range(groups):
            start = prefix_excl + earlier - offset
            starts.append(start)
            ends.append(start + pre_ref[gg])
            table_ref[gg] = start
            table_ref[groups + gg] = start + pre_ref[gg]
            table_ref[2 * groups + gg] = prefix_excl + pre_ref[gg] - offset
            earlier = earlier + table_ref[3 * groups + gg]
            prefix_excl = prefix_excl + pre_ref[gg]
        for t in range(CHUNKS):
            begin = t * STEP
            inside = jnp.int32(0)
            touch = jnp.int32(0)
            for gg in range(groups):
                hold = (starts[gg] <= begin) & (ends[gg] >= begin + STEP)
                meet = (starts[gg] < begin + STEP) & (ends[gg] > begin)
                inside = jnp.maximum(inside, jnp.where(hold, 1, 0))
                touch = jnp.maximum(touch, jnp.where(meet, 1, 0))
            chunk_ref[CHUNKS + t] = inside
            chunk_ref[2 * CHUNKS + t] = touch
        lane = lax.broadcasted_iota(jnp.int32, (PAD, LANES), 1)

        def edges(r, c):
            g = gid_ref[r]
            ps = table_ref[g]
            pe = table_ref[groups + g]
            os_ = table_ref[2 * groups + g] + edge_ref[r]
            oe = os_ + suf_ref[r]
            bound_ref[r] = jnp.where(
                lane == 0, ps, jnp.where(lane == 1, pe, jnp.where(lane == 2, os_, oe))
            )
            bucket = jnp.clip(jnp.right_shift(oe + (STEP - 1), STEP.bit_length() - 1), 0, CHUNKS + 1)
            chunk_ref[3 * CHUNKS + bucket] = chunk_ref[3 * CHUNKS + bucket] + 1
            return c

        lax.fori_loop(0, requests, edges, 0, unroll=8)
        count = jnp.int32(0)
        for t in range(CHUNKS):
            count = count + chunk_ref[3 * CHUNKS + t]
            chunk_ref[t] = count

    first = chunk_ref[turn]
    inside = chunk_ref[CHUNKS + turn]
    touch = chunk_ref[2 * CHUNKS + turn]

    @pl.when((inside == 0) & (touch == 1))
    def _():
        span = min(SPAN, requests)
        attend_window(turn, jnp.minimum(first, requests - span), span, True, *refs)

    @pl.when(inside == 1)
    def _():
        span = min(GROUP_MAX, requests)
        attend_window(turn, jnp.minimum(first, requests - span), span, False, *refs)

    @pl.when((inside == 0) & (touch == 0))
    def _():
        span = min(OWNERS, requests)
        attend_window(turn, jnp.minimum(first, requests - span), span, True, *refs)


def per_device(
    queries,
    new_keys,
    new_values,
    key_cache,
    value_cache,
    out_weight,
    group_ids,
    prefix_len,
    suffix_len,
):
    rows = queries.shape[0]
    heads_local = queries.shape[1] // HD
    kv_local = key_cache.shape[1] // HD
    repeat = heads_local // kv_local
    requests = rows // NEW
    block = key_cache.shape[0]
    span = min(SPAN, requests)
    tj = NEW * repeat
    steps = block // STEP
    assert steps == CHUNKS
    offset = jnp.full((1,), lax.axis_index("seq") * block, jnp.int32)
    scaled = (queries * jnp.asarray(0.125, queries.dtype)).reshape(requests, NEW, kv_local, repeat, HD)
    scaled = scaled.transpose(2, 0, 1, 3, 4).reshape(kv_local, requests, tj, HD)
    query_pad = jnp.stack(
        [
            jnp.pad(scaled[g], ((0, 0), (0, PAD - tj), (g * HD, LANES - (g + 1) * HD)))
            for g in range(kv_local)
        ]
    )
    full = lambda shape: pl.BlockSpec(shape, lambda t, *_: (0,) * len(shape))
    packed = pl.pallas_call(
        attend_kernel,
        grid_spec=pltpu.PrefetchScalarGridSpec(
            num_scalar_prefetch=4,
            grid=(steps,),
            in_specs=[
                full((kv_local, requests, PAD, LANES)),
                pl.BlockSpec((STEP, LANES), lambda t, *_: (t, 0)),
                pl.BlockSpec((STEP, LANES), lambda t, *_: (t, 0)),
            ],
            out_specs=full((requests, 2 * PAD, LANES)),
            scratch_shapes=[
                pltpu.SMEM((requests,), jnp.int32),
                pltpu.VMEM((requests, PAD, LANES), jnp.int32),
                pltpu.SMEM((4 * steps + 2,), jnp.int32),
                pltpu.SMEM((4 * prefix_len.shape[0],), jnp.int32),
            ],
        ),
        out_shape=jax.ShapeDtypeStruct((requests, 2 * PAD, LANES), jnp.float32),
        compiler_params=pltpu.CompilerParams(dimension_semantics=("arbitrary",)),
    )(group_ids, prefix_len, suffix_len, offset, query_pad, key_cache, value_cache)
    packed = lax.all_to_all(packed, "seq", split_axis=0, concat_axis=0, tiled=True)
    sums = packed[:, :tj, :].reshape(requests, tj, kv_local, HD)
    stats = packed[:, PAD : PAD + tj, : 2 * kv_local].reshape(requests, tj, kv_local, 2)
    maxes = stats[..., 0]
    totals = stats[..., 1]
    own_max = jnp.max(maxes, axis=0)
    rescale = jnp.exp(maxes - own_max[None])
    own_total = jnp.sum(totals * rescale, axis=0)
    own_summed = jnp.sum(sums * rescale[..., None], axis=0)
    mine = lax.axis_index("seq")
    own_query = lax.dynamic_slice_in_dim(queries, mine * NEW, NEW, 0)
    own_query = own_query.reshape(NEW, kv_local, repeat, HD).transpose(0, 2, 1, 3)
    own_query = own_query.reshape(tj, kv_local, HD)
    keys_new = new_keys.reshape(NEW, kv_local, HD)
    values_new = new_values.reshape(NEW, kv_local, HD)
    token_of = jnp.arange(tj) // repeat
    causal = (token_of[:, None] >= jnp.arange(NEW)[None, :])[:, None, :]
    score_new = (
        jnp.einsum("qgd,ugd->qgu", own_query, keys_new, preferred_element_type=jnp.float32)
        * 0.125
    )
    joined = jnp.maximum(own_max, jnp.max(jnp.where(causal, score_new, fill_score), axis=-1))
    expo_new = jnp.where(causal, jnp.exp(score_new - joined[..., None]), 0.0)
    factor_own = jnp.exp(own_max - joined)
    denominator = own_total * factor_own + jnp.sum(expo_new, axis=-1)
    numerator = own_summed * factor_own[..., None] + jnp.einsum(
        "qgu,ugd->qgd",
        expo_new.astype(jnp.bfloat16),
        values_new,
        preferred_element_type=jnp.float32,
    )
    mixed = (numerator / denominator[..., None]).astype(jnp.bfloat16)
    mixed = mixed.reshape(NEW, repeat, kv_local, HD).transpose(0, 2, 1, 3)
    mixed = mixed.reshape(NEW, heads_local * HD)
    partial_out = jnp.dot(mixed, out_weight, preferred_element_type=jnp.float32)
    parts = lax.axis_size("tp")
    piece = partial_out.shape[1] // parts
    pieces = partial_out.reshape(NEW, parts, piece)
    me = lax.axis_index("tp")
    result = lax.dynamic_index_in_dim(pieces, me, 1, keepdims=False)
    for shift in range(1, parts):
        sent = lax.dynamic_index_in_dim(pieces, (me + shift) % parts, 1, keepdims=False)
        pairs = [(i, (i + shift) % parts) for i in range(parts)]
        result = result + lax.ppermute(sent, "tp", pairs)
    return result.astype(jnp.bfloat16)


def solution(mesh):
    placed = (
        P(None, "tp"),
        P("seq", "tp"),
        P("seq", "tp"),
        P("seq", "tp"),
        P("seq", "tp"),
        P("tp", None),
        P(),
        P(),
        P(),
    )
    return jax.shard_map(
        per_device, mesh=mesh, in_specs=placed, out_specs=P("seq", "tp"), check_vma=False
    )
```

```python
import jax
import jax.numpy as jnp
from jax import lax
from jax.experimental import pallas as pl
from jax.experimental.pallas import tpu as pltpu
from jax.sharding import PartitionSpec as P

HD = 64
NEW = 5
STEP = 2048
SPAN = 18
GROUP_MAX = 16
OWNERS = 3
CHUNKS = 4
PAD = 16
LANES = 128


fill_score = -1e30


def segment_starts(group_ids, prefix_len, suffix_len):
    groups = jnp.arange(prefix_len.shape[0], dtype=jnp.int32)
    prefix_excl = jnp.cumsum(prefix_len) - prefix_len
    suffix_excl = jnp.cumsum(suffix_len) - suffix_len
    earlier = group_ids[None, :] < groups[:, None]
    prompt_start = prefix_excl + jnp.sum(jnp.where(earlier, suffix_len[None, :], 0), axis=1)
    member = group_ids[:, None] == groups[None, :]
    req_prompt_start = jnp.sum(jnp.where(member, prompt_start[None, :], 0), axis=1)
    req_prompt_len = jnp.sum(jnp.where(member, prefix_len[None, :], 0), axis=1)
    prefix_incl = jnp.sum(jnp.where(member, (prefix_excl + prefix_len)[None, :], 0), axis=1)
    own_start = prefix_incl + suffix_excl
    return (req_prompt_start, req_prompt_len, own_start)


def attend_window(turn, low, span, masked, q_ref, bound_ref, k_ref, v_ref, o_ref, stat_ref):
    rows = span * PAD
    keys = k_ref[...]
    vals = v_ref[...]
    bound = bound_ref[pl.ds(low, span)].reshape(rows, LANES)
    if masked:
        places = turn * STEP + lax.broadcasted_iota(jnp.int32, (1, STEP), 1)
        mask = ((places >= bound[:, 0:1]) & (places < bound[:, 1:2])) | (
            (places >= bound[:, 2:3]) & (places < bound[:, 3:4])
        )
    else:
        first = turn * STEP
        keep = (bound[:, 0:1] <= first) & (bound[:, 1:2] >= first + STEP)
    stat = stat_ref[pl.ds(low, span)].reshape(rows, LANES)
    o_old = o_ref[pl.ds(low, span)].reshape(rows, LANES)
    lane = lax.broadcasted_iota(jnp.int32, (rows, LANES), 1)
    first_half = lane < HD
    o_new = None
    stat_new = jnp.zeros((rows, LANES), jnp.float32)
    for g in range(2):
        query = q_ref[g, pl.ds(low, span)].reshape(rows, LANES)
        score = lax.dot_general(
            query, keys, (((1,), (1,)), ((), ())), preferred_element_type=jnp.float32
        )
        if masked:
            score = jnp.where(mask, score, fill_score)
        m_old = stat[:, 2 * g : 2 * g + 1]
        l_old = stat[:, 2 * g + 1 : 2 * g + 2]
        m_new = jnp.maximum(m_old, jnp.max(score, axis=1, keepdims=True))
        expo = jnp.exp(score - m_new)
        alpha = jnp.exp(m_old - m_new)
        l_new = alpha * l_old + jnp.sum(expo, axis=1, keepdims=True)
        mixed = jnp.dot(expo.astype(jnp.bfloat16), vals, preferred_element_type=jnp.float32)
        if g == 0:
            o_new = jnp.where(first_half, o_old * alpha + mixed, 0.0)
        else:
            o_new = jnp.where(first_half, o_new, o_old * alpha + mixed)
        stat_new = jnp.where(lane == 2 * g, m_new, stat_new)
        stat_new = jnp.where(lane == 2 * g + 1, l_new, stat_new)
    if not masked:
        o_new = jnp.where(keep, o_new, o_old)
        stat_new = jnp.where(keep, stat_new, stat)
    o_ref[pl.ds(low, span)] = o_new.reshape(span, PAD, LANES)
    stat_ref[pl.ds(low, span)] = stat_new.reshape(span, PAD, LANES)


def attend_kernel(
    gid_ref, pre_ref, suf_ref, off_ref, q_ref, k_ref, v_ref, o_ref, stat_ref, edge_ref, bound_ref,
    chunk_ref, table_ref,
):
    turn = pl.program_id(0)
    requests = q_ref.shape[1]
    groups = pre_ref.shape[0]
    refs = (q_ref, bound_ref, k_ref, v_ref, o_ref, stat_ref)

    @pl.when(turn == 0)
    def _():
        o_ref[...] = jnp.zeros(o_ref.shape, jnp.float32)
        lane3 = lax.broadcasted_iota(jnp.int32, stat_ref.shape, 2)
        stat_ref[...] = jnp.where(lane3 % 2 == 0, fill_score, 0.0).astype(jnp.float32)
        offset = off_ref[0]
        for gg in range(groups):
            table_ref[3 * groups + gg] = 0
        for t in range(CHUNKS + 2):
            chunk_ref[3 * CHUNKS + t] = 0

        def sums(r, run):
            g = gid_ref[r]
            s = suf_ref[r]
            edge_ref[r] = run
            table_ref[3 * groups + g] = table_ref[3 * groups + g] + s
            return run + s

        lax.fori_loop(0, requests, sums, jnp.int32(0), unroll=8)
        prefix_excl = jnp.int32(0)
        earlier = jnp.int32(0)
        starts = []
        ends = []
        for gg in range(groups):
            start = prefix_excl + earlier - offset
            starts.append(start)
            ends.append(start + pre_ref[gg])
            table_ref[gg] = start
            table_ref[groups + gg] = start + pre_ref[gg]
            table_ref[2 * groups + gg] = prefix_excl + pre_ref[gg] - offset
            earlier = earlier + table_ref[3 * groups + gg]
            prefix_excl = prefix_excl + pre_ref[gg]
        for t in range(CHUNKS):
            begin = t * STEP
            inside = jnp.int32(0)
            touch = jnp.int32(0)
            for gg in range(groups):
                hold = (starts[gg] <= begin) & (ends[gg] >= begin + STEP)
                meet = (starts[gg] < begin + STEP) & (ends[gg] > begin)
                opens = (starts[gg] > begin) & (starts[gg] < begin + STEP)
                inside = jnp.maximum(inside, jnp.where(hold, 1, 0))
                touch = jnp.maximum(touch, jnp.where(meet & opens, 2, jnp.where(meet, 1, 0)))
            chunk_ref[CHUNKS + t] = inside
            chunk_ref[2 * CHUNKS + t] = touch
        lane = lax.broadcasted_iota(jnp.int32, (PAD, LANES), 1)

        def edges(r, c):
            g = gid_ref[r]
            ps = table_ref[g]
            pe = table_ref[groups + g]
            os_ = table_ref[2 * groups + g] + edge_ref[r]
            oe = os_ + suf_ref[r]
            bound_ref[r] = jnp.where(
                lane == 0, ps, jnp.where(lane == 1, pe, jnp.where(lane == 2, os_, oe))
            )
            bucket = jnp.clip(jnp.right_shift(oe + (STEP - 1), STEP.bit_length() - 1), 0, CHUNKS + 1)
            chunk_ref[3 * CHUNKS + bucket] = chunk_ref[3 * CHUNKS + bucket] + 1
            return c

        lax.fori_loop(0, requests, edges, 0, unroll=8)
        count = jnp.int32(0)
        for t in range(CHUNKS):
            count = count + chunk_ref[3 * CHUNKS + t]
            chunk_ref[t] = count

    first = chunk_ref[turn]
    inside = chunk_ref[CHUNKS + turn]
    touch = chunk_ref[2 * CHUNKS + turn]

    @pl.when((inside == 0) & (touch == 2))
    def _():
        span = min(SPAN, requests)
        attend_window(turn, jnp.minimum(first, requests - span), span, True, *refs)

    @pl.when((inside == 0) & (touch == 1))
    def _():
        span = min(GROUP_MAX, requests)
        attend_window(turn, jnp.minimum(first, requests - span), span, True, *refs)

    @pl.when(inside == 1)
    def _():
        span = min(GROUP_MAX, requests)
        attend_window(turn, jnp.minimum(first, requests - span), span, False, *refs)

    @pl.when((inside == 0) & (touch == 0))
    def _():
        span = min(OWNERS, requests)
        attend_window(turn, jnp.minimum(first, requests - span), span, True, *refs)


def per_device(
    queries,
    new_keys,
    new_values,
    key_cache,
    value_cache,
    out_weight,
    group_ids,
    prefix_len,
    suffix_len,
):
    rows = queries.shape[0]
    heads_local = queries.shape[1] // HD
    kv_local = key_cache.shape[1] // HD
    repeat = heads_local // kv_local
    requests = rows // NEW
    block = key_cache.shape[0]
    span = min(SPAN, requests)
    tj = NEW * repeat
    steps = block // STEP
    assert steps == CHUNKS
    offset = jnp.full((1,), lax.axis_index("seq") * block, jnp.int32)
    scaled = (queries * jnp.asarray(0.125, queries.dtype)).reshape(requests, NEW, kv_local, repeat, HD)
    scaled = scaled.transpose(2, 0, 1, 3, 4).reshape(kv_local, requests, tj, HD)
    query_pad = jnp.stack(
        [
            jnp.pad(scaled[g], ((0, 0), (0, PAD - tj), (g * HD, LANES - (g + 1) * HD)))
            for g in range(kv_local)
        ]
    )
    full = lambda shape: pl.BlockSpec(shape, lambda t, *_: (0,) * len(shape))
    o_out, stat_out = pl.pallas_call(
        attend_kernel,
        grid_spec=pltpu.PrefetchScalarGridSpec(
            num_scalar_prefetch=4,
            grid=(steps,),
            in_specs=[
                full((kv_local, requests, PAD, LANES)),
                pl.BlockSpec((STEP, LANES), lambda t, *_: (t, 0)),
                pl.BlockSpec((STEP, LANES), lambda t, *_: (t, 0)),
            ],
            out_specs=[full((requests, PAD, LANES)), full((requests, PAD, LANES))],
            scratch_shapes=[
                pltpu.SMEM((requests,), jnp.int32),
                pltpu.VMEM((requests, PAD, LANES), jnp.int32),
                pltpu.SMEM((4 * steps + 2,), jnp.int32),
                pltpu.SMEM((4 * prefix_len.shape[0],), jnp.int32),
            ],
        ),
        out_shape=[
            jax.ShapeDtypeStruct((requests, PAD, LANES), jnp.float32),
            jax.ShapeDtypeStruct((requests, PAD, LANES), jnp.float32),
        ],
        compiler_params=pltpu.CompilerParams(dimension_semantics=("arbitrary",)),
    )(group_ids, prefix_len, suffix_len, offset, query_pad, key_cache, value_cache)
    width = tj * LANES
    packed = jnp.concatenate(
        [
            o_out[:, :tj, :].reshape(requests, width),
            stat_out[:, :tj, : 2 * kv_local].reshape(requests, tj * 2 * kv_local),
        ],
        axis=1,
    )
    packed = lax.all_to_all(packed, "seq", split_axis=0, concat_axis=0, tiled=True)
    sums = packed[:, :width].reshape(requests, tj, kv_local, HD)
    stats = packed[:, width:].reshape(requests, tj, kv_local, 2)
    maxes = stats[..., 0]
    totals = stats[..., 1]
    own_max = jnp.max(maxes, axis=0)
    rescale = jnp.exp(maxes - own_max[None])
    own_total = jnp.sum(totals * rescale, axis=0)
    own_summed = jnp.sum(sums * rescale[..., None], axis=0)
    mine = lax.axis_index("seq")
    own_query = lax.dynamic_slice_in_dim(queries, mine * NEW, NEW, 0)
    own_query = own_query.reshape(NEW, kv_local, repeat, HD).transpose(0, 2, 1, 3)
    own_query = own_query.reshape(tj, kv_local, HD)
    keys_new = new_keys.reshape(NEW, kv_local, HD)
    values_new = new_values.reshape(NEW, kv_local, HD)
    token_of = jnp.arange(tj) // repeat
    causal = (token_of[:, None] >= jnp.arange(NEW)[None, :])[:, None, :]
    score_new = (
        jnp.einsum("qgd,ugd->qgu", own_query, keys_new, preferred_element_type=jnp.float32)
        * 0.125
    )
    joined = jnp.maximum(own_max, jnp.max(jnp.where(causal, score_new, fill_score), axis=-1))
    expo_new = jnp.where(causal, jnp.exp(score_new - joined[..., None]), 0.0)
    factor_own = jnp.exp(own_max - joined)
    denominator = own_total * factor_own + jnp.sum(expo_new, axis=-1)
    numerator = own_summed * factor_own[..., None] + jnp.einsum(
        "qgu,ugd->qgd",
        expo_new.astype(jnp.bfloat16),
        values_new,
        preferred_element_type=jnp.float32,
    )
    mixed = (numerator / denominator[..., None]).astype(jnp.bfloat16)
    mixed = mixed.reshape(NEW, repeat, kv_local, HD).transpose(0, 2, 1, 3)
    mixed = mixed.reshape(NEW, heads_local * HD)
    partial_out = jnp.dot(mixed, out_weight, preferred_element_type=jnp.float32)
    parts = lax.axis_size("tp")
    piece = partial_out.shape[1] // parts
    pieces = partial_out.reshape(NEW, parts, piece)
    me = lax.axis_index("tp")
    result = lax.dynamic_index_in_dim(pieces, me, 1, keepdims=False)
    for shift in range(1, parts):
        sent = lax.dynamic_index_in_dim(pieces, (me + shift) % parts, 1, keepdims=False)
        pairs = [(i, (i + shift) % parts) for i in range(parts)]
        result = result + lax.ppermute(sent, "tp", pairs)
    return result.astype(jnp.bfloat16)


def solution(mesh):
    placed = (
        P(None, "tp"),
        P("seq", "tp"),
        P("seq", "tp"),
        P("seq", "tp"),
        P("seq", "tp"),
        P("tp", None),
        P(),
        P(),
        P(),
    )
    return jax.shard_map(
        per_device, mesh=mesh, in_specs=placed, out_specs=P("seq", "tp"), check_vma=False
    )
```

```python
import jax
import jax.numpy as jnp
from jax import lax
from jax.experimental import pallas as pl
from jax.experimental.pallas import tpu as pltpu
from jax.sharding import PartitionSpec as P

HD = 64
NEW = 5
STEP = 2048
SPAN = 18
GROUP_MAX = 16
OWNERS = 3
CHUNKS = 4
PAD = 16
LANES = 128


fill_score = -1e30


def segment_starts(group_ids, prefix_len, suffix_len):
    groups = jnp.arange(prefix_len.shape[0], dtype=jnp.int32)
    prefix_excl = jnp.cumsum(prefix_len) - prefix_len
    suffix_excl = jnp.cumsum(suffix_len) - suffix_len
    earlier = group_ids[None, :] < groups[:, None]
    prompt_start = prefix_excl + jnp.sum(jnp.where(earlier, suffix_len[None, :], 0), axis=1)
    member = group_ids[:, None] == groups[None, :]
    req_prompt_start = jnp.sum(jnp.where(member, prompt_start[None, :], 0), axis=1)
    req_prompt_len = jnp.sum(jnp.where(member, prefix_len[None, :], 0), axis=1)
    prefix_incl = jnp.sum(jnp.where(member, (prefix_excl + prefix_len)[None, :], 0), axis=1)
    own_start = prefix_incl + suffix_excl
    return (req_prompt_start, req_prompt_len, own_start)


def attend_window(turn, low, span, masked, q_ref, bound_ref, k_ref, v_ref, o_ref, stat_ref):
    rows = span * PAD
    keys = k_ref[...]
    vals = v_ref[...]
    bound = bound_ref[pl.ds(low, span)].reshape(rows, LANES)
    if masked:
        places = turn * STEP + lax.broadcasted_iota(jnp.int32, (1, STEP), 1)
        mask = ((places >= bound[:, 0:1]) & (places < bound[:, 1:2])) | (
            (places >= bound[:, 2:3]) & (places < bound[:, 3:4])
        )
    else:
        first = turn * STEP
        keep = (bound[:, 0:1] <= first) & (bound[:, 1:2] >= first + STEP)
    stat = stat_ref[pl.ds(low, span)].reshape(rows, LANES)
    o_old = o_ref[pl.ds(low, span)].reshape(rows, LANES)
    lane = lax.broadcasted_iota(jnp.int32, (rows, LANES), 1)
    first_half = lane < HD
    o_new = None
    stat_new = jnp.zeros((rows, LANES), jnp.float32)
    for g in range(2):
        query = q_ref[g, pl.ds(low, span)].reshape(rows, LANES)
        score = lax.dot_general(
            query, keys, (((1,), (1,)), ((), ())), preferred_element_type=jnp.float32
        )
        if masked:
            score = jnp.where(mask, score, fill_score)
        m_old = stat[:, 2 * g : 2 * g + 1]
        l_old = stat[:, 2 * g + 1 : 2 * g + 2]
        m_new = jnp.maximum(m_old, jnp.max(score, axis=1, keepdims=True))
        expo = jnp.exp(score - m_new)
        alpha = jnp.exp(m_old - m_new)
        l_new = alpha * l_old + jnp.sum(expo, axis=1, keepdims=True)
        mixed = jnp.dot(expo.astype(jnp.bfloat16), vals, preferred_element_type=jnp.float32)
        if g == 0:
            o_new = jnp.where(first_half, o_old * alpha + mixed, 0.0)
        else:
            o_new = jnp.where(first_half, o_new, o_old * alpha + mixed)
        stat_new = jnp.where(lane == 2 * g, m_new, stat_new)
        stat_new = jnp.where(lane == 2 * g + 1, l_new, stat_new)
    if not masked:
        o_new = jnp.where(keep, o_new, o_old)
        stat_new = jnp.where(keep, stat_new, stat)
    o_ref[pl.ds(low, span)] = o_new.reshape(span, PAD, LANES)
    stat_ref[pl.ds(low, span)] = stat_new.reshape(span, PAD, LANES)


def attend_kernel(
    gid_ref, pre_ref, suf_ref, off_ref, q_ref, k_ref, v_ref, o_ref, stat_ref, edge_ref, bound_ref,
    chunk_ref, table_ref,
):
    turn = pl.program_id(0)
    requests = q_ref.shape[1]
    groups = pre_ref.shape[0]
    refs = (q_ref, bound_ref, k_ref, v_ref, o_ref, stat_ref)

    @pl.when(turn == 0)
    def _():
        o_ref[...] = jnp.zeros(o_ref.shape, jnp.float32)
        lane3 = lax.broadcasted_iota(jnp.int32, stat_ref.shape, 2)
        stat_ref[...] = jnp.where(lane3 % 2 == 0, fill_score, 0.0).astype(jnp.float32)
        offset = off_ref[0]
        for gg in range(groups):
            table_ref[3 * groups + gg] = 0
        for t in range(CHUNKS + 2):
            chunk_ref[3 * CHUNKS + t] = 0

        def sums(r, run):
            g = gid_ref[r]
            s = suf_ref[r]
            edge_ref[r] = run
            table_ref[3 * groups + g] = table_ref[3 * groups + g] + s
            return run + s

        lax.fori_loop(0, requests, sums, jnp.int32(0), unroll=8)
        prefix_excl = jnp.int32(0)
        earlier = jnp.int32(0)
        starts = []
        ends = []
        for gg in range(groups):
            start = prefix_excl + earlier - offset
            starts.append(start)
            ends.append(start + pre_ref[gg])
            table_ref[gg] = start
            table_ref[groups + gg] = start + pre_ref[gg]
            table_ref[2 * groups + gg] = prefix_excl + pre_ref[gg] - offset
            earlier = earlier + table_ref[3 * groups + gg]
            prefix_excl = prefix_excl + pre_ref[gg]
        for t in range(CHUNKS):
            begin = t * STEP
            inside = jnp.int32(0)
            touch = jnp.int32(0)
            for gg in range(groups):
                hold = (starts[gg] <= begin) & (ends[gg] >= begin + STEP)
                meet = (starts[gg] < begin + STEP) & (ends[gg] > begin)
                inside = jnp.maximum(inside, jnp.where(hold, 1, 0))
                touch = jnp.maximum(touch, jnp.where(meet, 1, 0))
            chunk_ref[CHUNKS + t] = inside
            chunk_ref[2 * CHUNKS + t] = touch
        lane = lax.broadcasted_iota(jnp.int32, (PAD, LANES), 1)

        def edges(r, c):
            g = gid_ref[r]
            ps = table_ref[g]
            pe = table_ref[groups + g]
            os_ = table_ref[2 * groups + g] + edge_ref[r]
            oe = os_ + suf_ref[r]
            bound_ref[r] = jnp.where(
                lane == 0, ps, jnp.where(lane == 1, pe, jnp.where(lane == 2, os_, oe))
            )
            bucket = jnp.clip(jnp.right_shift(oe + (STEP - 1), STEP.bit_length() - 1), 0, CHUNKS + 1)
            chunk_ref[3 * CHUNKS + bucket] = chunk_ref[3 * CHUNKS + bucket] + 1
            return c

        lax.fori_loop(0, requests, edges, 0, unroll=8)
        count = jnp.int32(0)
        for t in range(CHUNKS):
            count = count + chunk_ref[3 * CHUNKS + t]
            chunk_ref[t] = count

    first = chunk_ref[turn]
    inside = chunk_ref[CHUNKS + turn]
    touch = chunk_ref[2 * CHUNKS + turn]

    @pl.when((inside == 0) & (touch == 1))
    def _():
        span = min(SPAN, requests)
        attend_window(turn, jnp.minimum(first, requests - span), span, True, *refs)

    @pl.when(inside == 1)
    def _():
        span = min(GROUP_MAX, requests)
        attend_window(turn, jnp.minimum(first, requests - span), span, False, *refs)

    @pl.when((inside == 0) & (touch == 0))
    def _():
        span = min(OWNERS, requests)
        attend_window(turn, jnp.minimum(first, requests - span), span, True, *refs)


def per_device(
    queries,
    new_keys,
    new_values,
    key_cache,
    value_cache,
    out_weight,
    group_ids,
    prefix_len,
    suffix_len,
):
    rows = queries.shape[0]
    heads_local = queries.shape[1] // HD
    kv_local = key_cache.shape[1] // HD
    repeat = heads_local // kv_local
    requests = rows // NEW
    block = key_cache.shape[0]
    span = min(SPAN, requests)
    tj = NEW * repeat
    steps = block // STEP
    assert steps == CHUNKS
    offset = jnp.full((1,), lax.axis_index("seq") * block, jnp.int32)
    scaled = (queries * jnp.asarray(0.125, queries.dtype)).reshape(requests, NEW, kv_local, repeat, HD)
    scaled = scaled.transpose(2, 0, 1, 3, 4).reshape(kv_local, requests, tj, HD)
    query_pad = jnp.stack(
        [
            jnp.pad(scaled[g], ((0, 0), (0, PAD - tj), (g * HD, LANES - (g + 1) * HD)))
            for g in range(kv_local)
        ]
    )
    full = lambda shape: pl.BlockSpec(shape, lambda t, *_: (0,) * len(shape))
    o_out, stat_out = pl.pallas_call(
        attend_kernel,
        grid_spec=pltpu.PrefetchScalarGridSpec(
            num_scalar_prefetch=4,
            grid=(steps,),
            in_specs=[
                full((kv_local, requests, PAD, LANES)),
                pl.BlockSpec((STEP, LANES), lambda t, *_: (t, 0)),
                pl.BlockSpec((STEP, LANES), lambda t, *_: (t, 0)),
            ],
            out_specs=[full((requests, PAD, LANES)), full((requests, PAD, LANES))],
            scratch_shapes=[
                pltpu.SMEM((requests,), jnp.int32),
                pltpu.VMEM((requests, PAD, LANES), jnp.int32),
                pltpu.SMEM((4 * steps + 2,), jnp.int32),
                pltpu.SMEM((4 * prefix_len.shape[0],), jnp.int32),
            ],
        ),
        out_shape=[
            jax.ShapeDtypeStruct((requests, PAD, LANES), jnp.float32),
            jax.ShapeDtypeStruct((requests, PAD, LANES), jnp.float32),
        ],
        compiler_params=pltpu.CompilerParams(dimension_semantics=("arbitrary",)),
    )(group_ids, prefix_len, suffix_len, offset, query_pad, key_cache, value_cache)
    width = tj * LANES
    packed = jnp.concatenate(
        [
            o_out[:, :tj, :].reshape(requests, width),
            stat_out[:, :tj, : 2 * kv_local].reshape(requests, tj * 2 * kv_local),
        ],
        axis=1,
    )
    packed = lax.all_to_all(packed, "seq", split_axis=0, concat_axis=0, tiled=True)
    sums = packed[:, :width].reshape(requests, tj, kv_local, HD)
    stats = packed[:, width:].reshape(requests, tj, kv_local, 2)
    maxes = stats[..., 0]
    totals = stats[..., 1]
    own_max = jnp.max(maxes, axis=0)
    rescale = jnp.exp(maxes - own_max[None])
    own_total = jnp.sum(totals * rescale, axis=0)
    own_summed = jnp.sum(sums * rescale[..., None], axis=0)
    mine = lax.axis_index("seq")
    own_query = lax.dynamic_slice_in_dim(queries, mine * NEW, NEW, 0)
    own_query = own_query.reshape(NEW, kv_local, repeat, HD).transpose(0, 2, 1, 3)
    own_query = own_query.reshape(tj, kv_local, HD)
    keys_new = new_keys.reshape(NEW, kv_local, HD)
    values_new = new_values.reshape(NEW, kv_local, HD)
    token_of = jnp.arange(tj) // repeat
    causal = (token_of[:, None] >= jnp.arange(NEW)[None, :])[:, None, :]
    score_new = (
        jnp.einsum("qgd,ugd->qgu", own_query, keys_new, preferred_element_type=jnp.float32)
        * 0.125
    )
    joined = jnp.maximum(own_max, jnp.max(jnp.where(causal, score_new, fill_score), axis=-1))
    expo_new = jnp.where(causal, jnp.exp(score_new - joined[..., None]), 0.0)
    factor_own = jnp.exp(own_max - joined)
    denominator = own_total * factor_own + jnp.sum(expo_new, axis=-1)
    numerator = own_summed * factor_own[..., None] + jnp.einsum(
        "qgu,ugd->qgd",
        expo_new.astype(jnp.bfloat16),
        values_new,
        preferred_element_type=jnp.float32,
    )
    mixed = (numerator / denominator[..., None]).astype(jnp.bfloat16)
    mixed = mixed.reshape(NEW, repeat, kv_local, HD).transpose(0, 2, 1, 3)
    mixed = mixed.reshape(NEW, heads_local * HD)
    partial_out = jnp.dot(mixed, out_weight, preferred_element_type=jnp.float32)
    parts = lax.axis_size("tp")
    piece = partial_out.shape[1] // parts
    pieces = partial_out.reshape(NEW, parts, piece)
    me = lax.axis_index("tp")
    result = lax.dynamic_index_in_dim(pieces, me, 1, keepdims=False)
    for shift in sorted(range(1, parts), key=lambda k: -min(k, parts - k)):
        sent = lax.dynamic_index_in_dim(pieces, (me + shift) % parts, 1, keepdims=False)
        pairs = [(i, (i + shift) % parts) for i in range(parts)]
        result = result + lax.ppermute(sent, "tp", pairs)
    return result.astype(jnp.bfloat16)


def solution(mesh):
    placed = (
        P(None, "tp"),
        P("seq", "tp"),
        P("seq", "tp"),
        P("seq", "tp"),
        P("seq", "tp"),
        P("tp", None),
        P(),
        P(),
        P(),
    )
    return jax.shard_map(
        per_device, mesh=mesh, in_specs=placed, out_specs=P("seq", "tp"), check_vma=False
    )
```
